32 devices in a mesh: tile: 4 (over z), seq: 8 (over y, x, core).
Axes of the slice: x: 2, y: 2, z: 4, core: 2. Of those that a mesh axis runs over, the one named last changes fastest.
Arguments:
- embeddings: bfloat16 [32768, 1536], P(('tile', 'seq')), may hold values from -6 to 6
- slot: int32 [32768], P(('tile', 'seq')), may hold values from 0 to 32767, as said below
- lengths: int32 [4], P('tile'), may hold values from 1 to 8192, 20480 in all
- in_weight: bfloat16 [1536, 768], replicated, may hold values from -0.15625 to 0.15625
- norm_gain: float32 [768], replicated, may hold values from 0.1 to 1.9
- qkv_weight: bfloat16 [768, 2304], replicated, may hold values from -1 to 1
- out_weight: bfloat16 [768, 768], replicated, may hold values from -0.21875 to 0.21875
Outputs:
- encoded: bfloat16 [4, 8192, 768], P('tile', 'seq')
The draws below stay inside these ranges and needn't reach their ends.
Inputs may be any that keep to these rules, and one draw needn't show every extreme that they name: `slot`: every value appears exactly once. With P = 32 and B = 1024 // P, the rows q * 1024 + k * B to q * 1024 + (k + 1) * B - 1 have slots between k * 1024 and (k + 1) * 1024 - 1, for every q and k.
All inputs are finite; a program needn't handle non-finite values. No bound on the sum of `lengths` on one device may be relied on, other than what follows from the above.
Results may differ from the reference program's by a relative error of at most 0.017.
The reference program's roundings to bfloat16 on the way count: a program that leaves them out, or rounds other values in their place, can miss the bound.
Values may be sent and summed in bfloat16 or wider, within the bound.
No kernel may reach another device: no remote copies, remote signals or barrier semaphores. Data moves between devices by JAX's collectives and lax.ppermute only.
A program may use at most 256 MiB of HBM per device.

```python
import math
import jax
import jax.numpy as jnp
import numpy as np
from jax import lax

E = 1536
D = 768
HEAD_COUNT = 16
HEAD_SIZE = 48
DILATION_RATE = 8
SEGMENT_LENGTH = 1024
SLIDE_LEN = 8192
SLIDES = 4
TOKENS = 32768
N_TILE = 4
N_SEQ = 8


def draw_slot(key, part):
    devices = TOKENS // SEGMENT_LENGTH
    per_block = SEGMENT_LENGTH // devices
    subkeys = jax.random.split(key, devices)

    def shuffle(single_key):
        return jax.random.permutation(single_key, SEGMENT_LENGTH).astype(jnp.int32)
    orders = jax.vmap(shuffle)(subkeys)
    orders = orders + (jnp.arange(devices, dtype=jnp.int32) * SEGMENT_LENGTH)[:, None]
    orders = orders.reshape(devices, devices, per_block).transpose(1, 0, 2)
    return orders.reshape(TOKENS).astype(jnp.int32)


def draw_qkv_weight(key, part):
    result = jax.random.normal(key, (D, 3 * D), jnp.float32) * D ** (-0.5)
    result = jnp.clip(result, -1.0, 1.0)
    return result.astype(jnp.bfloat16)


def shard_levels(stream_key, shape, pieces, smallest, largest):
    level = 1.0
    for dim, parts in pieces:
        steps = jax.random.uniform(jax.random.fold_in(jax.random.fold_in(stream_key, 6), dim), (parts,), jnp.float32, smallest / len(pieces), largest / len(pieces))
        level = level * jnp.repeat(jnp.exp(steps), shape[dim] // parts).reshape((-1,) + (1,) * (len(shape) - 1 - dim))
    return level


def split_up(amount, total, most, skew):
    weights = [(1 << 20) // math.isqrt(rank ** skew) + 1 for rank in range(2, amount + 1)]
    surplus, counts = total - most - (amount - 1), [1] * (amount - 1)
    while surplus > 0:
        movable = [i for i in range(amount - 1) if counts[i] < most]
        whole, remaining = sum([weights[i] for i in movable]), surplus
        for i in movable:
            extra = min(most - counts[i], max(1, remaining * weights[i] // whole), surplus)
            counts[i] = counts[i] + extra
            surplus = surplus - extra
    return np.array([most] + counts)


def ragged_sizes(key, number_of, total, bound, skew):
    if number_of == 2:
        one = jax.random.randint(key, (), max(1, total - bound), min(bound, total - 1) + 1)
        return jnp.stack([one, total - one])
    sizes = jnp.asarray(split_up(number_of, total, bound, skew), jnp.int32)
    pairs = (number_of - 1) // 2
    donor, receiver = sizes[1:1 + 2 * pairs:2], sizes[2:2 + 2 * pairs:2]
    slack = jnp.minimum(donor - 1, bound - receiver)
    shifted = jax.random.randint(jax.random.fold_in(key, 1), (pairs,), 0, 1 << 20) % (slack + 1)
    sizes = sizes.at[1:1 + 2 * pairs:2].set(donor - shifted).at[2:2 + 2 * pairs:2].set(receiver + shifted)
    return sizes[jax.random.permutation(jax.random.fold_in(key, 2), number_of)]


def gaussian(own_key, dims, width, most, cuts=(), kind=jnp.bfloat16):
    values = width * jax.random.normal(own_key, dims, jnp.float32)
    if cuts:
        values = values * shard_levels(own_key, dims, cuts, -0.22, 0.18)
    return jnp.clip(values, -most, most).astype(kind)


def setup_inputs(seed: int = 0) -> dict:
    key_list = jax.random.split(jax.random.key(seed), 8)
    embeddings = gaussian(key_list[0], (TOKENS, E), 1.0, 6.0, ((0, 32),))
    slot = draw_slot(jax.random.fold_in(key_list[7], 71), 0)
    lengths = ragged_sizes(key_list[2], SLIDES, 5 * SLIDE_LEN * SLIDES // 8, SLIDE_LEN, 2).astype(jnp.int32)
    in_weight = gaussian(key_list[3], (E, D), E ** -0.5, 0.15625)
    norm_gain = jnp.clip(1.0 + 0.18 * jax.random.normal(key_list[4], (D,), jnp.float32), 0.1, 1.9)
    qkv_weight = draw_qkv_weight(jax.random.fold_in(key_list[7], 71), 0)
    out_weight = gaussian(key_list[6], (D, D), D ** -0.5, 0.21875)
    return dict(embeddings=embeddings, slot=slot, lengths=lengths, in_weight=in_weight, norm_gain=norm_gain, qkv_weight=qkv_weight, out_weight=out_weight)


big_negative = -1e+30
norm_epsilon = 1e-05

def normalize(features, gain):
    wide = features.astype(jnp.float32)
    average = lax.optimization_barrier(jnp.mean(wide, axis=-1, keepdims=True))
    centered = wide - average
    spread = lax.optimization_barrier(jnp.mean(centered * centered, axis=-1, keepdims=True))
    return (centered * lax.rsqrt(spread + norm_epsilon) * gain).astype(jnp.bfloat16)

def rounded_attention_weights(weights):
    narrow = weights.astype(jnp.bfloat16)
    narrow = lax.optimization_barrier(narrow)
    return narrow.astype(jnp.float32)

def encode_slide(features, slide_length, norm_gain, qkv_weight, out_weight):
    slide_token_length = features.shape[0]
    normed = normalize(features, norm_gain)
    projections = jnp.dot(normed, qkv_weight, preferred_element_type=jnp.float32).astype(jnp.bfloat16)
    query_matrix = projections[:, :D].reshape(slide_token_length, HEAD_COUNT, HEAD_SIZE)
    key_matrix = projections[:, D:2 * D].reshape(slide_token_length, HEAD_COUNT, HEAD_SIZE)
    value_matrix = projections[:, 2 * D:].reshape(slide_token_length, HEAD_COUNT, HEAD_SIZE)
    start_offsets = jnp.arange(HEAD_COUNT, dtype=jnp.int32) % DILATION_RATE
    head_index_list = jnp.arange(HEAD_COUNT, dtype=jnp.int32)
    dilated_count = slide_token_length // DILATION_RATE
    dilated_key_rows = key_matrix.reshape(dilated_count, DILATION_RATE, HEAD_COUNT, HEAD_SIZE)[:, start_offsets, head_index_list, :].astype(jnp.float32)
    dilated_value_rows = value_matrix.reshape(dilated_count, DILATION_RATE, HEAD_COUNT, HEAD_SIZE)[:, start_offsets, head_index_list, :].astype(jnp.float32)
    dilated_positions = jnp.arange(dilated_count, dtype=jnp.int32)[:, None] * DILATION_RATE + start_offsets[None, :]
    sparse_valid = dilated_positions < slide_length
    dilated_mask = jnp.arange(DILATION_RATE, dtype=jnp.int32)[None, :] == start_offsets[:, None]
    query_block_rows = SEGMENT_LENGTH // DILATION_RATE
    logit_scale = HEAD_SIZE ** (-0.5)

    def one_block(block_index):
        first_row = (block_index * SEGMENT_LENGTH).astype(jnp.int32)
        block_query_rows = lax.dynamic_slice_in_dim(query_matrix, first_row, SEGMENT_LENGTH, 0).astype(jnp.float32)
        block_k = lax.dynamic_slice_in_dim(key_matrix, first_row, SEGMENT_LENGTH, 0).astype(jnp.float32)
        block_v = lax.dynamic_slice_in_dim(value_matrix, first_row, SEGMENT_LENGTH, 0).astype(jnp.float32)
        block_x = lax.dynamic_slice_in_dim(features, first_row, SEGMENT_LENGTH, 0).astype(jnp.float32)
        positions = first_row + jnp.arange(SEGMENT_LENGTH, dtype=jnp.int32)
        key_valid = positions < slide_length
        nearby_scores = jnp.einsum('qhd,khd->hqk', block_query_rows, block_k) * logit_scale
        nearby_scores = jnp.where(key_valid[None, None, :], nearby_scores, big_negative)
        dilated_query_block = block_query_rows.reshape(query_block_rows, DILATION_RATE, HEAD_COUNT, HEAD_SIZE)[:, start_offsets, head_index_list, :]
        distant_scores = jnp.einsum('sbz,ebz->bse', dilated_query_block, dilated_key_rows) * logit_scale
        distant_scores = jnp.where(sparse_valid.T[:, None, :], distant_scores, big_negative)
        nearby_maximum = lax.optimization_barrier(jnp.max(nearby_scores, axis=-1)).reshape(HEAD_COUNT, query_block_rows, DILATION_RATE)
        local_sparse_max = lax.optimization_barrier(jnp.max(jnp.where(dilated_mask[:, None, :], nearby_maximum, big_negative), axis=-1))
        joint = jnp.maximum(local_sparse_max, lax.optimization_barrier(jnp.max(distant_scores, axis=-1)))
        row_max = jnp.where(dilated_mask[:, None, :], joint[:, :, None], nearby_maximum).reshape(HEAD_COUNT, SEGMENT_LENGTH)
        local_weights = jnp.exp(nearby_scores - row_max[:, :, None])
        distant_weights = jnp.exp(distant_scores - joint[:, :, None])
        nearby_total = lax.optimization_barrier(jnp.sum(local_weights, axis=-1))
        distant_total = lax.optimization_barrier(jnp.sum(distant_weights, axis=-1))
        nearby_accumulator = jnp.einsum('hqk,khd->qhd', rounded_attention_weights(local_weights), block_v)
        distant_accumulator = jnp.einsum('aup,pae->uae', rounded_attention_weights(distant_weights), dilated_value_rows)
        softmax_totals = nearby_total.reshape(HEAD_COUNT, query_block_rows, DILATION_RATE) + jnp.where(dilated_mask[:, None, :], distant_total[:, :, None], 0.0)
        softmax_totals = softmax_totals.transpose(1, 2, 0).reshape(SEGMENT_LENGTH, HEAD_COUNT)
        summed_output = nearby_accumulator.reshape(query_block_rows, DILATION_RATE, HEAD_COUNT, HEAD_SIZE) + jnp.where(dilated_mask.T[None, :, :, None], distant_accumulator[:, None, :, :], 0.0)
        summed_output = summed_output.reshape(SEGMENT_LENGTH, HEAD_COUNT, HEAD_SIZE) / softmax_totals[:, :, None]
        attended = summed_output.reshape(SEGMENT_LENGTH, D).astype(jnp.bfloat16)
        output = jnp.dot(attended, out_weight, preferred_element_type=jnp.float32) + block_x
        return jnp.where(key_valid[:, None], output, 0.0).astype(jnp.bfloat16)
    blocks = lax.map(one_block, jnp.arange(slide_token_length // SEGMENT_LENGTH, dtype=jnp.int32))
    return blocks.reshape(slide_token_length, D)

def reference(embeddings, slot, lengths, in_weight, norm_gain, qkv_weight, out_weight):
    projected = jnp.dot(embeddings, in_weight, preferred_element_type=jnp.float32).astype(jnp.bfloat16)
    placed = jnp.zeros((TOKENS, D), jnp.bfloat16).at[slot].set(projected)
    slides = placed.reshape(N_TILE, SEGMENT_LENGTH * N_SEQ, D)
    outputs = [encode_slide(slides[index], lengths[index], norm_gain, qkv_weight, out_weight) for index in range(N_TILE)]
    return jnp.stack(outputs)
```

```python
import jax
import jax.numpy as jnp
from jax import lax
from jax.sharding import PartitionSpec as P

HEAD_COUNT = 16
DILATION_RATE = 8


big_negative = -1e30
norm_epsilon = 1e-05


def normalize(features, gain):
    wide = features.astype(jnp.float32)
    average = jnp.mean(wide, axis=-1, keepdims=True)
    centered = wide - average
    spread = jnp.mean(centered * centered, axis=-1, keepdims=True)
    return (centered * lax.rsqrt(spread + norm_epsilon) * gain).astype(jnp.bfloat16)


def body(embeddings, slot, lengths, in_weight, norm_gain, qkv_weight, out_weight):
    seq_count = lax.axis_size("seq")
    device_count = lax.axis_size("tile") * seq_count
    sequence_rows = embeddings.shape[0]
    block_rows = sequence_rows // device_count
    model_width = in_weight.shape[1]
    my_index = lax.axis_index("tile") * seq_count + lax.axis_index("seq")
    parted_slot = slot.reshape(device_count, block_rows)
    projected = jnp.dot(embeddings, in_weight, preferred_element_type=jnp.float32).astype(
        jnp.bfloat16
    )
    arrived_raw, arrived_slot = (
        lax.all_to_all(
            projected.reshape(device_count, block_rows, model_width),
            ("tile", "seq"),
            split_axis=0,
            concat_axis=0,
            tiled=True,
        ),
        lax.all_to_all(parted_slot, ("tile", "seq"), split_axis=0, concat_axis=0, tiled=True),
    )
    arrived = arrived_raw.reshape(sequence_rows, model_width)
    local_slot = arrived_slot.reshape(sequence_rows) - my_index * sequence_rows
    features = jnp.zeros((sequence_rows, model_width), jnp.bfloat16).at[local_slot].set(arrived)
    slide_length = lengths[0]
    first_pos = lax.axis_index("seq") * sequence_rows
    positions = first_pos + jnp.arange(sequence_rows, dtype=jnp.int32)
    key_ok = positions < slide_length
    head_feature_size = model_width // HEAD_COUNT
    logit_scale = head_feature_size ** (-0.5)
    start_offsets = jnp.arange(HEAD_COUNT, dtype=jnp.int32) % DILATION_RATE
    head_index_list = jnp.arange(HEAD_COUNT, dtype=jnp.int32)
    dilated_mask = jnp.arange(DILATION_RATE, dtype=jnp.int32)[None, :] == start_offsets[:, None]
    dilated_row_index = sequence_rows // DILATION_RATE
    normed = normalize(features, norm_gain)
    projections = jnp.dot(normed, qkv_weight, preferred_element_type=jnp.float32).astype(
        jnp.bfloat16
    )
    query_matrix = projections[:, :model_width].reshape(
        sequence_rows, HEAD_COUNT, head_feature_size
    )
    key_matrix = projections[:, model_width : 2 * model_width].reshape(
        sequence_rows, HEAD_COUNT, head_feature_size
    )
    value_matrix = projections[:, 2 * model_width :].reshape(
        sequence_rows, HEAD_COUNT, head_feature_size
    )
    dilated_query_rows = query_matrix.reshape(
        dilated_row_index, DILATION_RATE, HEAD_COUNT, head_feature_size
    )[:, start_offsets, head_index_list, :]
    dilated_key_rows = key_matrix.reshape(
        dilated_row_index, DILATION_RATE, HEAD_COUNT, head_feature_size
    )[:, start_offsets, head_index_list, :]
    dilated_value_rows = value_matrix.reshape(
        dilated_row_index, DILATION_RATE, HEAD_COUNT, head_feature_size
    )[:, start_offsets, head_index_list, :]
    packed = jnp.stack(
        [
            dilated_key_rows.reshape(dilated_row_index, model_width),
            dilated_value_rows.reshape(dilated_row_index, model_width),
        ]
    )
    gathered = lax.all_gather(packed, "seq", axis=1, tiled=True)
    distant_count = gathered.shape[1]
    far_keys = gathered[0].reshape(distant_count, HEAD_COUNT, head_feature_size)
    far_values = gathered[1].reshape(distant_count, HEAD_COUNT, head_feature_size)
    distant_valid_mask = (
        jnp.arange(distant_count, dtype=jnp.int32)[:, None] * DILATION_RATE + start_offsets[None, :]
        < slide_length
    )
    grouped_heads = 4
    pieces = []
    for first_head in range(0, HEAD_COUNT, grouped_heads):
        chosen = slice(first_head, first_head + grouped_heads)
        group_mask = dilated_mask[chosen]
        nearby_scores = (
            jnp.einsum(
                "qhd,khd->hqk",
                query_matrix[:, chosen],
                key_matrix[:, chosen],
                preferred_element_type=jnp.float32,
            )
            * logit_scale
        )
        nearby_scores = jnp.where(key_ok[None, None, :], nearby_scores, big_negative)
        nearby_maximum = jnp.max(nearby_scores, axis=-1).reshape(
            grouped_heads, dilated_row_index, DILATION_RATE
        )
        local_sparse_max = jnp.max(
            jnp.where(group_mask[:, None, :], nearby_maximum, big_negative), axis=-1
        )
        distant_scores = (
            jnp.einsum(
                "sbz,ebz->bse",
                dilated_query_rows[:, chosen],
                far_keys[:, chosen],
                preferred_element_type=jnp.float32,
            )
            * logit_scale
        )
        distant_scores = jnp.where(
            distant_valid_mask[:, chosen].T[:, None, :], distant_scores, big_negative
        )
        joint = jnp.maximum(local_sparse_max, jnp.max(distant_scores, axis=-1))
        distant_weights = jnp.exp(distant_scores - joint[:, :, None])
        distant_total = jnp.sum(distant_weights, axis=-1)
        distant_accumulator = jnp.einsum(
            "aup,pae->uae",
            distant_weights.astype(jnp.bfloat16),
            far_values[:, chosen],
            preferred_element_type=jnp.float32,
        )
        row_max = jnp.where(group_mask[:, None, :], joint[:, :, None], nearby_maximum).reshape(
            grouped_heads, sequence_rows
        )
        local_weights = jnp.exp(nearby_scores - row_max[:, :, None])
        nearby_total = jnp.sum(local_weights, axis=-1)
        nearby_accumulator = jnp.einsum(
            "hqk,khd->qhd",
            local_weights.astype(jnp.bfloat16),
            value_matrix[:, chosen],
            preferred_element_type=jnp.float32,
        )
        softmax_totals = nearby_total.reshape(
            grouped_heads, dilated_row_index, DILATION_RATE
        ) + jnp.where(group_mask[:, None, :], distant_total[:, :, None], 0.0)
        softmax_totals = softmax_totals.transpose(1, 2, 0).reshape(sequence_rows, grouped_heads)
        summed_output = nearby_accumulator.reshape(
            dilated_row_index, DILATION_RATE, grouped_heads, head_feature_size
        ) + jnp.where(group_mask.T[None, :, :, None], distant_accumulator[:, None, :, :], 0.0)
        pieces.append(
            summed_output.reshape(sequence_rows, grouped_heads, head_feature_size)
            / softmax_totals[:, :, None]
        )
    attended = (
        jnp.concatenate(pieces, axis=1).reshape(sequence_rows, model_width).astype(jnp.bfloat16)
    )
    output = jnp.dot(attended, out_weight, preferred_element_type=jnp.float32) + features.astype(
        jnp.float32
    )
    output = jnp.where(key_ok[:, None], output, 0.0).astype(jnp.bfloat16)
    return output.reshape(1, sequence_rows, model_width)


def solution(mesh):
    return jax.shard_map(
        body,
        mesh=mesh,
        in_specs=(P(("tile", "seq"), None), P(("tile", "seq")), P("tile"), P(), P(), P(), P()),
        out_specs=P("tile", "seq", None),
        check_vma=False,
    )
```

```python
import functools

import jax
import jax.numpy as jnp
from jax import lax
from jax.experimental import pallas as pl
from jax.sharding import PartitionSpec as P

HEAD_COUNT = 16
DILATION_RATE = 8


big_negative = -1e30
norm_epsilon = 1e-05


def normalize(features, gain):
    wide = features.astype(jnp.float32)
    average = jnp.mean(wide, axis=-1, keepdims=True)
    centered = wide - average
    spread = jnp.mean(centered * centered, axis=-1, keepdims=True)
    return (centered * lax.rsqrt(spread + norm_epsilon) * gain).astype(jnp.bfloat16)


def nearby_kernel(q_ref, kt_ref, v_ref, bias_ref, o_ref, *, groups, group_rows, scale):
    offset = pl.program_id(0) % DILATION_RATE
    keys = kt_ref[0]
    values = v_ref[0]
    bias = bias_ref[...]
    for group in range(groups):

        @pl.when(group != offset)
        def _():
            rows = pl.ds(group * group_rows, group_rows)
            scores = jnp.dot(q_ref[0, rows, :], keys, preferred_element_type=jnp.float32)
            scores = scores * scale + bias
            top = jnp.max(scores, axis=1, keepdims=True)
            weights = jnp.exp(scores - top)
            total = jnp.sum(weights, axis=1, keepdims=True)
            summed = jnp.dot(
                weights.astype(jnp.bfloat16), values, preferred_element_type=jnp.float32
            )
            o_ref[0, rows, :] = (summed / total).astype(o_ref.dtype)


def dilated_kernel(
    q_ref, kt_ref, v_ref, bias_ref, fk_ref, fv_ref, fbias_ref, prev_ref, o_ref, *, scale
):
    del prev_ref
    queries = q_ref[0]
    near = jnp.dot(queries, kt_ref[0], preferred_element_type=jnp.float32)
    near = near * scale + bias_ref[...]
    far = jnp.dot(queries, fk_ref[0, 0], preferred_element_type=jnp.float32)
    far = far * scale + fbias_ref[0]
    top = jnp.maximum(
        jnp.max(near, axis=1, keepdims=True), jnp.max(far, axis=1, keepdims=True)
    )
    near_w = jnp.exp(near - top)
    far_w = jnp.exp(far - top)
    total = jnp.sum(near_w, axis=1, keepdims=True) + jnp.sum(far_w, axis=1, keepdims=True)
    summed = jnp.dot(near_w.astype(jnp.bfloat16), v_ref[0], preferred_element_type=jnp.float32)
    summed = summed + lax.dot_general(
        far_w.astype(jnp.bfloat16),
        fv_ref[0, 0],
        (((1,), (1,)), ((), ())),
        preferred_element_type=jnp.float32,
    )
    o_ref[0] = (summed / total).astype(o_ref.dtype)


def body(embeddings, slot, lengths, in_weight, norm_gain, qkv_weight, out_weight):
    seq_count = lax.axis_size("seq")
    device_count = lax.axis_size("tile") * seq_count
    rows = embeddings.shape[0]
    block_rows = rows // device_count
    width = in_weight.shape[1]
    head_size = width // HEAD_COUNT
    group_rows = rows // DILATION_RATE
    far_count = group_rows * seq_count
    scale = head_size ** (-0.5)
    my_index = lax.axis_index("tile") * seq_count + lax.axis_index("seq")

    projected = jnp.dot(embeddings, in_weight, preferred_element_type=jnp.float32).astype(
        jnp.bfloat16
    )
    arrived = lax.all_to_all(
        projected.reshape(device_count, block_rows, width),
        ("tile", "seq"),
        split_axis=0,
        concat_axis=0,
        tiled=True,
    ).reshape(rows, width)
    arrived_slot = lax.all_to_all(
        slot.reshape(device_count, block_rows), ("tile", "seq"), split_axis=0, concat_axis=0, tiled=True
    ).reshape(rows)
    local_slot = arrived_slot - my_index * rows
    stored_slot = (local_slot % DILATION_RATE) * group_rows + local_slot // DILATION_RATE
    placement = (
        stored_slot[None, :] == jnp.arange(rows, dtype=jnp.int32)[:, None]
    ).astype(jnp.bfloat16)
    features = jnp.dot(placement, arrived, preferred_element_type=jnp.float32).astype(
        jnp.bfloat16
    )

    slide_length = lengths[0]
    stored = jnp.arange(rows, dtype=jnp.int32)
    local_position = (stored % group_rows) * DILATION_RATE + stored // group_rows
    position_ok = lax.axis_index("seq") * rows + local_position < slide_length
    near_bias = jnp.where(position_ok, 0.0, big_negative).astype(jnp.float32).reshape(1, rows)

    normed = normalize(features, norm_gain)
    projections = jnp.dot(normed, qkv_weight, preferred_element_type=jnp.float32).astype(
        jnp.bfloat16
    )
    split = projections.reshape(rows, 3, HEAD_COUNT, head_size)
    queries = split[:, 0].transpose(1, 0, 2)
    keys_t = split[:, 1].transpose(1, 2, 0)
    values = split[:, 2].transpose(1, 0, 2)

    offsets = [head % DILATION_RATE for head in range(HEAD_COUNT)]
    own_far = jnp.stack(
        [
            jnp.stack(
                [keys_t[h, :, o * group_rows : (o + 1) * group_rows] for h, o in enumerate(offsets)]
            ),
            jnp.stack(
                [
                    values[h, o * group_rows : (o + 1) * group_rows, :].T
                    for h, o in enumerate(offsets)
                ]
            ),
        ]
    )
    far = lax.all_gather(own_far, "seq", axis=3, tiled=True)
    far_position = (
        jnp.arange(far_count, dtype=jnp.int32)[None, :] * DILATION_RATE
        + jnp.asarray(offsets, jnp.int32)[:, None]
    )
    far_bias = (
        jnp.where(far_position < slide_length, 0.0, big_negative)
        .astype(jnp.float32)
        .reshape(HEAD_COUNT, 1, far_count)
    )

    head_block = pl.BlockSpec((1, rows, head_size), lambda h: (h, 0, 0))
    keys_block = pl.BlockSpec((1, head_size, rows), lambda h: (h, 0, 0))
    bias_block = pl.BlockSpec((1, rows), lambda h: (0, 0))
    nearby = pl.pallas_call(
        functools.partial(
            nearby_kernel, groups=DILATION_RATE, group_rows=group_rows, scale=scale
        ),
        grid=(HEAD_COUNT,),
        in_specs=[head_block, keys_block, head_block, bias_block],
        out_specs=head_block,
        out_shape=jax.ShapeDtypeStruct((HEAD_COUNT, rows, head_size), jnp.bfloat16),
    )(queries, keys_t, values, near_bias)

    group_block = pl.BlockSpec((1, group_rows, head_size), lambda h: (h, h % DILATION_RATE, 0))
    attended = pl.pallas_call(
        functools.partial(dilated_kernel, scale=scale),
        grid=(HEAD_COUNT,),
        in_specs=[
            group_block,
            keys_block,
            head_block,
            bias_block,
            pl.BlockSpec((1, 1, head_size, far_count), lambda h: (0, h, 0, 0)),
            pl.BlockSpec((1, 1, head_size, far_count), lambda h: (1, h, 0, 0)),
            pl.BlockSpec((1, 1, far_count), lambda h: (h, 0, 0)),
            pl.BlockSpec(memory_space=pl.ANY),
        ],
        out_specs=group_block,
        out_shape=jax.ShapeDtypeStruct((HEAD_COUNT, rows, head_size), jnp.bfloat16),
        input_output_aliases={7: 0},
    )(queries, keys_t, values, near_bias, far, far, far_bias, nearby)

    output = jnp.einsum(
        "hnd,hde->ne",
        attended,
        out_weight.reshape(HEAD_COUNT, head_size, width),
        preferred_element_type=jnp.float32,
    ) + features.astype(jnp.float32)
    output = jnp.where(position_ok[:, None], output, 0.0).astype(jnp.bfloat16)
    output = output.reshape(DILATION_RATE, group_rows, width).transpose(1, 0, 2)
    return output.reshape(1, rows, width)


def solution(mesh):
    return jax.shard_map(
        body,
        mesh=mesh,
        in_specs=(P(("tile", "seq"), None), P(("tile", "seq")), P("tile"), P(), P(), P(), P()),
        out_specs=P("tile", "seq", None),
        check_vma=False,
    )
```

```python
import functools

import jax
import jax.numpy as jnp
from jax import lax
from jax.experimental import pallas as pl
from jax.sharding import PartitionSpec as P

HEAD_COUNT = 16
DILATION_RATE = 8


big_negative = -1e30
norm_epsilon = 1e-05


def normalize(features, gain):
    wide = features.astype(jnp.float32)
    average = jnp.mean(wide, axis=-1, keepdims=True)
    centered = wide - average
    spread = jnp.mean(centered * centered, axis=-1, keepdims=True)
    return (centered * lax.rsqrt(spread + norm_epsilon) * gain).astype(jnp.bfloat16)


def nearby_kernel(qt_ref, kt_ref, vt_ref, bias_ref, o_ref, *, groups, group_rows, factor):
    offset = pl.program_id(0) % DILATION_RATE
    keys = kt_ref[...]
    values = vt_ref[...].T
    bias = bias_ref[...]
    for group in range(groups):

        @pl.when(group != offset)
        def _():
            rows = pl.ds(group * group_rows, group_rows)
            queries = qt_ref[:, rows].T
            scores = jnp.dot(queries, keys, preferred_element_type=jnp.float32) + bias
            top = jnp.max(scores, axis=1, keepdims=True)
            weights = jnp.exp2((scores - top) * factor)
            total = jnp.sum(weights, axis=1, keepdims=True)
            summed = jnp.dot(
                weights.astype(jnp.bfloat16), values, preferred_element_type=jnp.float32
            )
            o_ref[0, rows, :] = (summed / total).astype(o_ref.dtype)


def dilated_kernel(
    qt_ref, kt_ref, vt_ref, bias_ref, fk_ref, fv_ref, fbias_ref, prev_ref, o_ref, *, factor
):
    del prev_ref
    queries = qt_ref[...].T
    near = jnp.dot(queries, kt_ref[...], preferred_element_type=jnp.float32) + bias_ref[...]
    far = jnp.dot(queries, fk_ref[0, 0], preferred_element_type=jnp.float32) + fbias_ref[0]
    top = jnp.maximum(
        jnp.max(near, axis=1, keepdims=True), jnp.max(far, axis=1, keepdims=True)
    )
    near_w = jnp.exp2((near - top) * factor)
    far_w = jnp.exp2((far - top) * factor)
    total = jnp.sum(near_w, axis=1, keepdims=True) + jnp.sum(far_w, axis=1, keepdims=True)
    summed = jnp.dot(
        near_w.astype(jnp.bfloat16), vt_ref[...].T, preferred_element_type=jnp.float32
    )
    summed = summed + jnp.dot(
        far_w.astype(jnp.bfloat16), fv_ref[0, 0].T, preferred_element_type=jnp.float32
    )
    o_ref[0] = (summed / total).astype(o_ref.dtype)


def body(embeddings, slot, lengths, in_weight, norm_gain, qkv_weight, out_weight):
    seq_count = lax.axis_size("seq")
    device_count = lax.axis_size("tile") * seq_count
    rows = embeddings.shape[0]
    block_rows = rows // device_count
    width = in_weight.shape[1]
    head_size = width // HEAD_COUNT
    group_rows = rows // DILATION_RATE
    far_count = group_rows * seq_count
    scale = head_size ** (-0.5)
    my_index = lax.axis_index("tile") * seq_count + lax.axis_index("seq")

    projected = jnp.dot(embeddings, in_weight, preferred_element_type=jnp.float32).astype(
        jnp.bfloat16
    )
    arrived = lax.all_to_all(
        projected.reshape(device_count, block_rows, width),
        ("tile", "seq"),
        split_axis=0,
        concat_axis=0,
        tiled=True,
    ).reshape(rows, width)
    arrived_slot = lax.all_to_all(
        slot.reshape(device_count, block_rows), ("tile", "seq"), split_axis=0, concat_axis=0, tiled=True
    ).reshape(rows)
    local_slot = arrived_slot - my_index * rows
    stored_slot = (local_slot % DILATION_RATE) * group_rows + local_slot // DILATION_RATE
    placement = (
        stored_slot[None, :] == jnp.arange(rows, dtype=jnp.int32)[:, None]
    ).astype(jnp.bfloat16)
    features = jnp.dot(placement, arrived, preferred_element_type=jnp.float32).astype(
        jnp.bfloat16
    )

    slide_length = lengths[0]
    stored = jnp.arange(rows, dtype=jnp.int32)
    local_position = (stored % group_rows) * DILATION_RATE + stored // group_rows
    position_ok = lax.axis_index("seq") * rows + local_position < slide_length
    near_bias = jnp.where(position_ok, 0.0, big_negative).astype(jnp.float32).reshape(1, rows)

    normed = normalize(features, norm_gain)
    projected_t = lax.dot_general(
        qkv_weight, normed, (((0,), (1,)), ((), ())), preferred_element_type=jnp.float32
    ).astype(jnp.bfloat16)

    offsets = [head % DILATION_RATE for head in range(HEAD_COUNT)]
    own_far = jnp.stack(
        [
            jnp.stack(
                [
                    projected_t[
                        (part * HEAD_COUNT + h) * head_size : (part * HEAD_COUNT + h + 1) * head_size,
                        o * group_rows : (o + 1) * group_rows,
                    ]
                    for h, o in enumerate(offsets)
                ]
            )
            for part in (1, 2)
        ]
    )
    far = lax.all_gather(own_far, "seq", axis=3, tiled=True)
    far_position = (
        jnp.arange(far_count, dtype=jnp.int32)[None, :] * DILATION_RATE
        + jnp.asarray(offsets, jnp.int32)[:, None]
    )
    far_bias = (
        jnp.where(far_position < slide_length, 0.0, big_negative)
        .astype(jnp.float32)
        .reshape(HEAD_COUNT, 1, far_count)
    )

    head_block = pl.BlockSpec((1, rows, head_size), lambda h: (h, 0, 0))
    query_block = pl.BlockSpec((head_size, rows), lambda h: (h, 0))
    keys_block = pl.BlockSpec((head_size, rows), lambda h: (HEAD_COUNT + h, 0))
    values_block = pl.BlockSpec((head_size, rows), lambda h: (2 * HEAD_COUNT + h, 0))
    bias_block = pl.BlockSpec((1, rows), lambda h: (0, 0))
    factor = scale * 1.4426950408889634
    nearby = pl.pallas_call(
        functools.partial(
            nearby_kernel, groups=DILATION_RATE, group_rows=group_rows, factor=factor
        ),
        grid=(HEAD_COUNT,),
        in_specs=[query_block, keys_block, values_block, bias_block],
        out_specs=head_block,
        out_shape=jax.ShapeDtypeStruct((HEAD_COUNT, rows, head_size), jnp.bfloat16),
    )(projected_t, projected_t, projected_t, near_bias)

    group_block = pl.BlockSpec((1, group_rows, head_size), lambda h: (h, h % DILATION_RATE, 0))
    attended = pl.pallas_call(
        functools.partial(dilated_kernel, factor=factor),
        grid=(HEAD_COUNT,),
        in_specs=[
            pl.BlockSpec((head_size, group_rows), lambda h: (h, h % DILATION_RATE)),
            keys_block,
            values_block,
            bias_block,
            pl.BlockSpec((1, 1, head_size, far_count), lambda h: (0, h, 0, 0)),
            pl.BlockSpec((1, 1, head_size, far_count), lambda h: (1, h, 0, 0)),
            pl.BlockSpec((1, 1, far_count), lambda h: (h, 0, 0)),
            pl.BlockSpec(memory_space=pl.ANY),
        ],
        out_specs=group_block,
        out_shape=jax.ShapeDtypeStruct((HEAD_COUNT, rows, head_size), jnp.bfloat16),
        input_output_aliases={7: 0},
    )(projected_t, projected_t, projected_t, near_bias, far, far, far_bias, nearby)

    output = jnp.einsum(
        "hnd,hde->ne",
        attended,
        out_weight.reshape(HEAD_COUNT, head_size, width),
        preferred_element_type=jnp.float32,
    ) + features.astype(jnp.float32)
    output = jnp.where(position_ok[:, None], output, 0.0).astype(jnp.bfloat16)
    output = output.reshape(DILATION_RATE, group_rows, width).transpose(1, 0, 2)
    return output.reshape(1, rows, width)


def solution(mesh):
    return jax.shard_map(
        body,
        mesh=mesh,
        in_specs=(P(("tile", "seq"), None), P(("tile", "seq")), P("tile"), P(), P(), P(), P()),
        out_specs=P("tile", "seq", None),
        check_vma=False,
    )
```

```python
import functools

import jax
import jax.numpy as jnp
from jax import lax
from jax.experimental import pallas as pl
from jax.sharding import PartitionSpec as P

HEAD_COUNT = 16
DILATION_RATE = 8


big_negative = -1e30
norm_epsilon = 1e-05


def normalize(features, gain):
    wide = features.astype(jnp.float32)
    average = jnp.mean(wide, axis=-1, keepdims=True)
    centered = wide - average
    spread = jnp.mean(centered * centered, axis=-1, keepdims=True)
    return (centered * lax.rsqrt(spread + norm_epsilon) * gain).astype(jnp.bfloat16)


def extend(block, extra):
    return jnp.concatenate([block, extra], axis=0)


def ones_row(width):
    row = lax.broadcasted_iota(jnp.int32, (16, width), 0)
    return jnp.where(row == 0, 1.0, 0.0).astype(jnp.bfloat16)


def nearby_kernel(qt_ref, kt_ref, vt_ref, bias_ref, o_ref, *, groups, group_rows, factor):
    offset = pl.program_id(0) % DILATION_RATE
    keys = extend(kt_ref[...], bias_ref[...]).T
    values_t = vt_ref[...]
    ones = ones_row(group_rows)
    for group in range(groups):

        @pl.when(group != offset)
        def _():
            rows = pl.ds(group * group_rows, group_rows)
            queries_t = extend(qt_ref[:, rows], ones)
            scores_t = jnp.dot(keys, queries_t, preferred_element_type=jnp.float32)
            top = jnp.max(scores_t, axis=0, keepdims=True)
            weights_t = jnp.exp2((scores_t - top) * factor)
            total = jnp.sum(weights_t, axis=0, keepdims=True)
            summed_t = jnp.dot(
                values_t, weights_t.astype(jnp.bfloat16), preferred_element_type=jnp.float32
            )
            o_ref[:, rows] = (summed_t / total).astype(o_ref.dtype)


def dilated_kernel(
    qt_ref, kt_ref, vt_ref, bias_ref, fk_ref, fv_ref, fbias_ref, prev_ref, o_ref, *, factor
):
    del prev_ref
    queries_t = extend(qt_ref[...], ones_row(qt_ref.shape[1]))
    near_keys = extend(kt_ref[...], bias_ref[...]).T
    far_keys = extend(fk_ref[0, 0], fbias_ref[0]).T
    near = jnp.dot(near_keys, queries_t, preferred_element_type=jnp.float32)
    far = jnp.dot(far_keys, queries_t, preferred_element_type=jnp.float32)
    top = jnp.maximum(
        jnp.max(near, axis=0, keepdims=True), jnp.max(far, axis=0, keepdims=True)
    )
    near_w = jnp.exp2((near - top) * factor)
    far_w = jnp.exp2((far - top) * factor)
    total = jnp.sum(near_w, axis=0, keepdims=True) + jnp.sum(far_w, axis=0, keepdims=True)
    summed_t = jnp.dot(
        vt_ref[...], near_w.astype(jnp.bfloat16), preferred_element_type=jnp.float32
    )
    summed_t = summed_t + jnp.dot(
        fv_ref[0, 0], far_w.astype(jnp.bfloat16), preferred_element_type=jnp.float32
    )
    o_ref[...] = (summed_t / total).astype(o_ref.dtype)


def body(embeddings, slot, lengths, in_weight, norm_gain, qkv_weight, out_weight):
    seq_count = lax.axis_size("seq")
    device_count = lax.axis_size("tile") * seq_count
    rows = embeddings.shape[0]
    block_rows = rows // device_count
    width = in_weight.shape[1]
    head_size = width // HEAD_COUNT
    group_rows = rows // DILATION_RATE
    far_count = group_rows * seq_count
    scale = head_size ** (-0.5)
    my_index = lax.axis_index("tile") * seq_count + lax.axis_index("seq")

    projected = jnp.dot(embeddings, in_weight, preferred_element_type=jnp.float32).astype(
        jnp.bfloat16
    )
    arrived = lax.all_to_all(
        projected.reshape(device_count, block_rows, width),
        ("tile", "seq"),
        split_axis=0,
        concat_axis=0,
        tiled=True,
    ).reshape(rows, width)
    arrived_slot = lax.all_to_all(
        slot.reshape(device_count, block_rows), ("tile", "seq"), split_axis=0, concat_axis=0, tiled=True
    ).reshape(rows)
    local_slot = arrived_slot - my_index * rows
    stored_slot = (local_slot % DILATION_RATE) * group_rows + local_slot // DILATION_RATE
    placement = (
        stored_slot[None, :] == jnp.arange(rows, dtype=jnp.int32)[:, None]
    ).astype(jnp.bfloat16)
    features = jnp.dot(placement, arrived, preferred_element_type=jnp.float32).astype(
        jnp.bfloat16
    )

    slide_length = lengths[0]
    stored = jnp.arange(rows, dtype=jnp.int32)
    local_position = (stored % group_rows) * DILATION_RATE + stored // group_rows
    position_ok = lax.axis_index("seq") * rows + local_position < slide_length
    extra_row = lax.broadcasted_iota(jnp.int32, (16, 1), 0) == 0
    near_bias = jnp.where(
        extra_row & ~position_ok[None, :], big_negative, 0.0
    ).astype(jnp.bfloat16)

    normed = normalize(features, norm_gain)
    projected_t = lax.dot_general(
        qkv_weight, normed, (((0,), (1,)), ((), ())), preferred_element_type=jnp.float32
    ).astype(jnp.bfloat16)

    offsets = [head % DILATION_RATE for head in range(HEAD_COUNT)]
    own_far = jnp.stack(
        [
            jnp.stack(
                [
                    projected_t[
                        (part * HEAD_COUNT + h) * head_size : (part * HEAD_COUNT + h + 1) * head_size,
                        o * group_rows : (o + 1) * group_rows,
                    ]
                    for h, o in enumerate(offsets)
                ]
            )
            for part in (1, 2)
        ]
    )
    far = lax.all_gather(own_far, "seq", axis=3, tiled=True)
    far_position = (
        jnp.arange(far_count, dtype=jnp.int32)[None, :] * DILATION_RATE
        + jnp.asarray(offsets, jnp.int32)[:, None]
    )
    far_bias = jnp.where(
        extra_row[None] & (far_position >= slide_length)[:, None, :], big_negative, 0.0
    ).astype(jnp.bfloat16)

    query_block = pl.BlockSpec((head_size, rows), lambda h: (h, 0))
    keys_block = pl.BlockSpec((head_size, rows), lambda h: (HEAD_COUNT + h, 0))
    values_block = pl.BlockSpec((head_size, rows), lambda h: (2 * HEAD_COUNT + h, 0))
    bias_block = pl.BlockSpec((16, rows), lambda h: (0, 0))
    factor = scale * 1.4426950408889634
    nearby = pl.pallas_call(
        functools.partial(
            nearby_kernel, groups=DILATION_RATE, group_rows=group_rows, factor=factor
        ),
        grid=(HEAD_COUNT,),
        in_specs=[query_block, keys_block, values_block, bias_block],
        out_specs=query_block,
        out_shape=jax.ShapeDtypeStruct((width, rows), jnp.bfloat16),
    )(projected_t, projected_t, projected_t, near_bias)

    group_block = pl.BlockSpec((head_size, group_rows), lambda h: (h, h % DILATION_RATE))
    attended_t = pl.pallas_call(
        functools.partial(dilated_kernel, factor=factor),
        grid=(HEAD_COUNT,),
        in_specs=[
            group_block,
            keys_block,
            values_block,
            bias_block,
            pl.BlockSpec((1, 1, head_size, far_count), lambda h: (0, h, 0, 0)),
            pl.BlockSpec((1, 1, head_size, far_count), lambda h: (1, h, 0, 0)),
            pl.BlockSpec((1, 16, far_count), lambda h: (h, 0, 0)),
            pl.BlockSpec(memory_space=pl.ANY),
        ],
        out_specs=group_block,
        out_shape=jax.ShapeDtypeStruct((width, rows), jnp.bfloat16),
        input_output_aliases={7: 0},
    )(projected_t, projected_t, projected_t, near_bias, far, far, far_bias, nearby)

    output = lax.dot_general(
        attended_t, out_weight, (((0,), (0,)), ((), ())), preferred_element_type=jnp.float32
    ) + features.astype(jnp.float32)
    output = jnp.where(position_ok[:, None], output, 0.0).astype(jnp.bfloat16)
    output = output.reshape(DILATION_RATE, group_rows, width).transpose(1, 0, 2)
    return output.reshape(1, rows, width)


def solution(mesh):
    return jax.shard_map(
        body,
        mesh=mesh,
        in_specs=(P(("tile", "seq"), None), P(("tile", "seq")), P("tile"), P(), P(), P(), P()),
        out_specs=P("tile", "seq", None),
        check_vma=False,
    )
```

```python
import functools

import jax
import jax.numpy as jnp
from jax import lax
from jax.experimental import pallas as pl
from jax.experimental.pallas import tpu as pltpu
from jax.sharding import PartitionSpec as P

HEAD_COUNT = 16
QUERY_BLOCK = 256
PASS1 = 1024
PASS2 = 512
DILATION_RATE = 8


big_negative = -1e30
norm_epsilon = 1e-05


def normalize(features, gain):
    wide = features.astype(jnp.float32)
    average = jnp.mean(wide, axis=-1, keepdims=True)
    centered = wide - average
    spread = jnp.mean(centered * centered, axis=-1, keepdims=True)
    return (centered * lax.rsqrt(spread + norm_epsilon) * gain).astype(jnp.bfloat16)


def extend(block, extra):
    return jnp.concatenate([block, extra], axis=0)


def ones_row(width):
    row = lax.broadcasted_iota(jnp.int32, (16, width), 0)
    return jnp.where(row == 0, 1.0, 0.0).astype(jnp.bfloat16)


def nearby_kernel(
    qt_ref, kt_ref, vt_ref, bias_ref, o_ref, keys_ref, *, groups, group_rows, factor
):
    keys_ref[...] = extend(kt_ref[...], bias_ref[...]).T
    key_count = keys_ref.shape[0]
    block = QUERY_BLOCK
    ones = ones_row(block)
    for first_row in range(0, groups * group_rows, block):
        rows = pl.ds(first_row, block)
        queries_t = extend(qt_ref[:, rows], ones)
        if PASS1 >= key_count and PASS2 >= key_count:
            scores_t = jnp.dot(keys_ref[...], queries_t, preferred_element_type=jnp.float32)
            top = jnp.max(scores_t, axis=0, keepdims=True)
            weights_t = jnp.exp2((scores_t - top) * factor)
            total = jnp.sum(weights_t, axis=0, keepdims=True)
            summed_t = jnp.dot(
                vt_ref[...], weights_t.astype(jnp.bfloat16), preferred_element_type=jnp.float32
            )
        else:
            top = None
            for first in range(0, key_count, PASS1):
                scores_t = jnp.dot(
                    keys_ref[pl.ds(first, PASS1), :], queries_t, preferred_element_type=jnp.float32
                )
                part = jnp.max(scores_t, axis=0, keepdims=True)
                top = part if top is None else jnp.maximum(top, part)
            total = None
            summed_t = None
            for first in range(0, key_count, PASS2):
                scores_t = jnp.dot(
                    keys_ref[pl.ds(first, PASS2), :], queries_t, preferred_element_type=jnp.float32
                )
                weights_t = jnp.exp2((scores_t - top) * factor)
                part = jnp.sum(weights_t, axis=0, keepdims=True)
                step = jnp.dot(
                    vt_ref[:, pl.ds(first, PASS2)],
                    weights_t.astype(jnp.bfloat16),
                    preferred_element_type=jnp.float32,
                )
                total = part if total is None else total + part
                summed_t = step if summed_t is None else summed_t + step
        o_ref[:, rows] = (summed_t / total).astype(o_ref.dtype)


def dilated_kernel(
    qt_ref, kt_ref, vt_ref, bias_ref, fk_ref, fv_ref, fbias_ref, prev_ref, o_ref, *, factor
):
    del prev_ref
    queries_t = extend(qt_ref[...], ones_row(qt_ref.shape[1]))
    near_keys = extend(kt_ref[...], bias_ref[...]).T
    far_keys = extend(fk_ref[0, 0], fbias_ref[0]).T
    near = jnp.dot(near_keys, queries_t, preferred_element_type=jnp.float32)
    far = jnp.dot(far_keys, queries_t, preferred_element_type=jnp.float32)
    top = jnp.maximum(
        jnp.max(near, axis=0, keepdims=True), jnp.max(far, axis=0, keepdims=True)
    )
    near_w = jnp.exp2((near - top) * factor)
    far_w = jnp.exp2((far - top) * factor)
    total = jnp.sum(near_w, axis=0, keepdims=True) + jnp.sum(far_w, axis=0, keepdims=True)
    summed_t = jnp.dot(
        vt_ref[...], near_w.astype(jnp.bfloat16), preferred_element_type=jnp.float32
    )
    summed_t = summed_t + jnp.dot(
        fv_ref[0, 0], far_w.astype(jnp.bfloat16), preferred_element_type=jnp.float32
    )
    o_ref[...] = (summed_t / total).astype(o_ref.dtype)


def body(embeddings, slot, lengths, in_weight, norm_gain, qkv_weight, out_weight):
    seq_count = lax.axis_size("seq")
    device_count = lax.axis_size("tile") * seq_count
    rows = embeddings.shape[0]
    block_rows = rows // device_count
    width = in_weight.shape[1]
    head_size = width // HEAD_COUNT
    group_rows = rows // DILATION_RATE
    far_count = group_rows * seq_count
    scale = head_size ** (-0.5)
    my_index = lax.axis_index("tile") * seq_count + lax.axis_index("seq")

    projected = jnp.dot(embeddings, in_weight, preferred_element_type=jnp.float32).astype(
        jnp.bfloat16
    )
    arrived = lax.all_to_all(
        projected.reshape(device_count, block_rows, width),
        ("tile", "seq"),
        split_axis=0,
        concat_axis=0,
        tiled=True,
    ).reshape(rows, width)
    every_slot = lax.all_gather(slot, ("tile", "seq"), tiled=True)
    arrived_slot = lax.dynamic_slice_in_dim(
        every_slot.reshape(device_count, device_count, block_rows), my_index, 1, axis=1
    ).reshape(rows)
    local_slot = arrived_slot - my_index * rows
    stored_slot = (local_slot % DILATION_RATE) * group_rows + local_slot // DILATION_RATE
    placement = (
        stored_slot[None, :] == jnp.arange(rows, dtype=jnp.int32)[:, None]
    ).astype(jnp.bfloat16)
    features = jnp.dot(placement, arrived, preferred_element_type=jnp.float32).astype(
        jnp.bfloat16
    )

    slide_length = lengths[0]
    stored = jnp.arange(rows, dtype=jnp.int32)
    local_position = (stored % group_rows) * DILATION_RATE + stored // group_rows
    position_ok = lax.axis_index("seq") * rows + local_position < slide_length
    extra_row = lax.broadcasted_iota(jnp.int32, (16, 1), 0) == 0
    near_bias = jnp.where(
        extra_row & ~position_ok[None, :], big_negative, 0.0
    ).astype(jnp.bfloat16)

    normed = normalize(features, norm_gain)
    projected_t = lax.dot_general(
        qkv_weight, normed, (((0,), (1,)), ((), ())), preferred_element_type=jnp.float32
    ).astype(jnp.bfloat16)

    offsets = [head % DILATION_RATE for head in range(HEAD_COUNT)]
    own_far = jnp.stack(
        [
            jnp.stack(
                [
                    projected_t[
                        (part * HEAD_COUNT + h) * head_size : (part * HEAD_COUNT + h + 1) * head_size,
                        o * group_rows : (o + 1) * group_rows,
                    ]
                    for h, o in enumerate(offsets)
                ]
            )
            for part in (1, 2)
        ]
    )
    far = lax.all_gather(own_far, "seq", axis=3, tiled=True)
    far_position = (
        jnp.arange(far_count, dtype=jnp.int32)[None, :] * DILATION_RATE
        + jnp.asarray(offsets, jnp.int32)[:, None]
    )
    far_bias = jnp.where(
        extra_row[None] & (far_position >= slide_length)[:, None, :], big_negative, 0.0
    ).astype(jnp.bfloat16)

    query_block = pl.BlockSpec((head_size, rows), lambda h: (h, 0))
    keys_block = pl.BlockSpec((head_size, rows), lambda h: (HEAD_COUNT + h, 0))
    values_block = pl.BlockSpec((head_size, rows), lambda h: (2 * HEAD_COUNT + h, 0))
    bias_block = pl.BlockSpec((16, rows), lambda h: (0, 0))
    factor = scale * 1.4426950408889634
    nearby = pl.pallas_call(
        functools.partial(
            nearby_kernel, groups=DILATION_RATE, group_rows=group_rows, factor=factor
        ),
        grid=(HEAD_COUNT,),
        in_specs=[query_block, keys_block, values_block, bias_block],
        out_specs=query_block,
        out_shape=jax.ShapeDtypeStruct((width, rows), jnp.bfloat16),
        scratch_shapes=[pltpu.VMEM((rows, head_size + 16), jnp.bfloat16)],
    )(projected_t, projected_t, projected_t, near_bias)

    group_block = pl.BlockSpec((head_size, group_rows), lambda h: (h, h % DILATION_RATE))
    attended_t = pl.pallas_call(
        functools.partial(dilated_kernel, factor=factor),
        grid=(HEAD_COUNT,),
        in_specs=[
            group_block,
            keys_block,
            values_block,
            bias_block,
            pl.BlockSpec((1, 1, head_size, far_count), lambda h: (0, h, 0, 0)),
            pl.BlockSpec((1, 1, head_size, far_count), lambda h: (1, h, 0, 0)),
            pl.BlockSpec((1, 16, far_count), lambda h: (h, 0, 0)),
            pl.BlockSpec(memory_space=pl.ANY),
        ],
        out_specs=group_block,
        out_shape=jax.ShapeDtypeStruct((width, rows), jnp.bfloat16),
        input_output_aliases={7: 0},
    )(projected_t, projected_t, projected_t, near_bias, far, far, far_bias, nearby)

    output = lax.dot_general(
        attended_t, out_weight, (((0,), (0,)), ((), ())), preferred_element_type=jnp.float32
    ) + features.astype(jnp.float32)
    output = jnp.where(position_ok[:, None], output, 0.0).astype(jnp.bfloat16)
    output = output.reshape(DILATION_RATE, group_rows, width).transpose(1, 0, 2)
    return output.reshape(1, rows, width)


def solution(mesh):
    return jax.shard_map(
        body,
        mesh=mesh,
        in_specs=(P(("tile", "seq"), None), P(("tile", "seq")), P("tile"), P(), P(), P(), P()),
        out_specs=P("tile", "seq", None),
        check_vma=False,
    )
```

```python
import functools

import jax
import jax.numpy as jnp
from jax import lax
from jax.experimental import pallas as pl
from jax.experimental.pallas import tpu as pltpu
from jax.sharding import PartitionSpec as P

HEAD_COUNT = 16
QUERY_BLOCK = 256
PASS1 = 1024
PASS2 = 512
DILATION_RATE = 8


big_negative = -1e30
norm_epsilon = 1e-05


def normalize(features, gain):
    wide = features.astype(jnp.float32)
    average = jnp.mean(wide, axis=-1, keepdims=True)
    centered = wide - average
    spread = jnp.mean(centered * centered, axis=-1, keepdims=True)
    return (centered * lax.rsqrt(spread + norm_epsilon) * gain).astype(jnp.bfloat16)


def extend(block, extra):
    return jnp.concatenate([block, extra], axis=0)


def ones_row(width):
    row = lax.broadcasted_iota(jnp.int32, (16, width), 0)
    return jnp.where(row == 0, 1.0, 0.0).astype(jnp.bfloat16)


def nearby_kernel(
    qt_ref, kt_ref, vt_ref, bias_ref, o_ref, keys_ref, *, groups, group_rows, factor
):
    keys_ref[...] = extend(kt_ref[...], bias_ref[...]).T
    key_count = keys_ref.shape[0]
    block = QUERY_BLOCK
    ones = ones_row(block)
    for first_row in range(0, groups * group_rows, block):
        rows = pl.ds(first_row, block)
        queries_t = extend(qt_ref[:, rows], ones)
        if PASS1 >= key_count and PASS2 >= key_count:
            scores_t = jnp.dot(keys_ref[...], queries_t, preferred_element_type=jnp.float32)
            top = jnp.max(scores_t, axis=0, keepdims=True)
            weights_t = jnp.exp2((scores_t - top) * factor)
            total = jnp.sum(weights_t, axis=0, keepdims=True)
            summed_t = jnp.dot(
                vt_ref[...], weights_t.astype(jnp.bfloat16), preferred_element_type=jnp.float32
            )
        else:
            top = None
            for first in range(0, key_count, PASS1):
                scores_t = jnp.dot(
                    keys_ref[pl.ds(first, PASS1), :], queries_t, preferred_element_type=jnp.float32
                )
                part = jnp.max(scores_t, axis=0, keepdims=True)
                top = part if top is None else jnp.maximum(top, part)
            total = None
            summed_t = None
            for first in range(0, key_count, PASS2):
                scores_t = jnp.dot(
                    keys_ref[pl.ds(first, PASS2), :], queries_t, preferred_element_type=jnp.float32
                )
                weights_t = jnp.exp2((scores_t - top) * factor)
                part = jnp.sum(weights_t, axis=0, keepdims=True)
                step = jnp.dot(
                    vt_ref[:, pl.ds(first, PASS2)],
                    weights_t.astype(jnp.bfloat16),
                    preferred_element_type=jnp.float32,
                )
                total = part if total is None else total + part
                summed_t = step if summed_t is None else summed_t + step
        o_ref[:, rows] = (summed_t / total).astype(o_ref.dtype)


def dilated_kernel(
    qt_ref, kt_ref, vt_ref, bias_ref, fk_ref, fv_ref, fbias_ref, prev_ref, o_ref, *, factor
):
    del prev_ref
    queries_t = extend(qt_ref[...], ones_row(qt_ref.shape[1]))
    near_keys = extend(kt_ref[...], bias_ref[...]).T
    far_keys = extend(fk_ref[0, 0], fbias_ref[0]).T
    near = jnp.dot(near_keys, queries_t, preferred_element_type=jnp.float32)
    far = jnp.dot(far_keys, queries_t, preferred_element_type=jnp.float32)
    top = jnp.maximum(
        jnp.max(near, axis=0, keepdims=True), jnp.max(far, axis=0, keepdims=True)
    )
    near_w = jnp.exp2((near - top) * factor)
    far_w = jnp.exp2((far - top) * factor)
    total = jnp.sum(near_w, axis=0, keepdims=True) + jnp.sum(far_w, axis=0, keepdims=True)
    summed_t = jnp.dot(
        vt_ref[...], near_w.astype(jnp.bfloat16), preferred_element_type=jnp.float32
    )
    summed_t = summed_t + jnp.dot(
        fv_ref[0, 0], far_w.astype(jnp.bfloat16), preferred_element_type=jnp.float32
    )
    o_ref[...] = (summed_t / total).astype(o_ref.dtype)


def body(embeddings, slot, lengths, in_weight, norm_gain, qkv_weight, out_weight):
    seq_count = lax.axis_size("seq")
    device_count = lax.axis_size("tile") * seq_count
    rows = embeddings.shape[0]
    block_rows = rows // device_count
    width = in_weight.shape[1]
    head_size = width // HEAD_COUNT
    group_rows = rows // DILATION_RATE
    far_count = group_rows * seq_count
    scale = head_size ** (-0.5)
    my_index = lax.axis_index("tile") * seq_count + lax.axis_index("seq")

    projected = jnp.dot(embeddings, in_weight, preferred_element_type=jnp.float32).astype(
        jnp.bfloat16
    )
    arrived = lax.all_to_all(
        projected.reshape(device_count, block_rows, width),
        ("tile", "seq"),
        split_axis=0,
        concat_axis=0,
        tiled=True,
    ).reshape(rows, width)
    arrived_slot = lax.all_to_all(
        slot.reshape(device_count, block_rows), ("tile", "seq"), split_axis=0, concat_axis=0, tiled=True
    ).reshape(rows)
    local_slot = arrived_slot - my_index * rows
    stored_slot = (local_slot % DILATION_RATE) * group_rows + local_slot // DILATION_RATE
    placement = (
        stored_slot[None, :] == jnp.arange(rows, dtype=jnp.int32)[:, None]
    ).astype(jnp.bfloat16)
    features = jnp.dot(placement, arrived, preferred_element_type=jnp.float32).astype(
        jnp.bfloat16
    )

    slide_length = lengths[0]
    stored = jnp.arange(rows, dtype=jnp.int32)
    local_position = (stored % group_rows) * DILATION_RATE + stored // group_rows
    position_ok = lax.axis_index("seq") * rows + local_position < slide_length
    extra_row = lax.broadcasted_iota(jnp.int32, (16, 1), 0) == 0
    near_bias = jnp.where(
        extra_row & ~position_ok[None, :], big_negative, 0.0
    ).astype(jnp.bfloat16)

    normed = normalize(features, norm_gain)
    projected_t = lax.dot_general(
        qkv_weight, normed, (((0,), (1,)), ((), ())), preferred_element_type=jnp.float32
    ).astype(jnp.bfloat16)

    offsets = [head % DILATION_RATE for head in range(HEAD_COUNT)]
    own_far = jnp.stack(
        [
            jnp.stack(
                [
                    projected_t[
                        (part * HEAD_COUNT + h) * head_size : (part * HEAD_COUNT + h + 1) * head_size,
                        o * group_rows : (o + 1) * group_rows,
                    ]
                    for h, o in enumerate(offsets)
                ]
            )
            for part in (1, 2)
        ]
    )
    far = lax.all_gather(own_far, "seq", axis=3, tiled=True)
    far_position = (
        jnp.arange(far_count, dtype=jnp.int32)[None, :] * DILATION_RATE
        + jnp.asarray(offsets, jnp.int32)[:, None]
    )
    far_bias = jnp.where(
        extra_row[None] & (far_position >= slide_length)[:, None, :], big_negative, 0.0
    ).astype(jnp.bfloat16)

    query_block = pl.BlockSpec((head_size, rows), lambda h: (h, 0))
    keys_block = pl.BlockSpec((head_size, rows), lambda h: (HEAD_COUNT + h, 0))
    values_block = pl.BlockSpec((head_size, rows), lambda h: (2 * HEAD_COUNT + h, 0))
    bias_block = pl.BlockSpec((16, rows), lambda h: (0, 0))
    factor = scale * 1.4426950408889634
    nearby = pl.pallas_call(
        functools.partial(
            nearby_kernel, groups=DILATION_RATE, group_rows=group_rows, factor=factor
        ),
        grid=(HEAD_COUNT,),
        in_specs=[query_block, keys_block, values_block, bias_block],
        out_specs=query_block,
        out_shape=jax.ShapeDtypeStruct((width, rows), jnp.bfloat16),
        scratch_shapes=[pltpu.VMEM((rows, head_size + 16), jnp.bfloat16)],
    )(projected_t, projected_t, projected_t, near_bias)

    group_block = pl.BlockSpec((head_size, group_rows), lambda h: (h, h % DILATION_RATE))
    attended_t = pl.pallas_call(
        functools.partial(dilated_kernel, factor=factor),
        grid=(HEAD_COUNT,),
        in_specs=[
            group_block,
            keys_block,
            values_block,
            bias_block,
            pl.BlockSpec((1, 1, head_size, far_count), lambda h: (0, h, 0, 0)),
            pl.BlockSpec((1, 1, head_size, far_count), lambda h: (1, h, 0, 0)),
            pl.BlockSpec((1, 16, far_count), lambda h: (h, 0, 0)),
            pl.BlockSpec(memory_space=pl.ANY),
        ],
        out_specs=group_block,
        out_shape=jax.ShapeDtypeStruct((width, rows), jnp.bfloat16),
        input_output_aliases={7: 0},
    )(projected_t, projected_t, projected_t, near_bias, far, far, far_bias, nearby)

    output = lax.dot_general(
        attended_t, out_weight, (((0,), (0,)), ((), ())), preferred_element_type=jnp.float32
    ) + features.astype(jnp.float32)
    output = jnp.where(position_ok[:, None], output, 0.0).astype(jnp.bfloat16)
    output = output.reshape(DILATION_RATE, group_rows, width).transpose(1, 0, 2)
    return output.reshape(1, rows, width)


def solution(mesh):
    return jax.shard_map(
        body,
        mesh=mesh,
        in_specs=(P(("tile", "seq"), None), P(("tile", "seq")), P("tile"), P(), P(), P(), P()),
        out_specs=P("tile", "seq", None),
        check_vma=False,
    )
```

```python
import functools

import jax
import jax.numpy as jnp
from jax import lax
from jax.experimental import pallas as pl
from jax.experimental.pallas import tpu as pltpu
from jax.sharding import PartitionSpec as P

HEAD_COUNT = 16
QUERY_BLOCK = 256
PASS1 = 1024
PASS2 = 512
DILATION_RATE = 8


big_negative = -1e30
norm_epsilon = 1e-05


def normalize(features, gain):
    wide = features.astype(jnp.float32)
    average = jnp.mean(wide, axis=-1, keepdims=True)
    centered = wide - average
    spread = jnp.mean(centered * centered, axis=-1, keepdims=True)
    return (centered * lax.rsqrt(spread + norm_epsilon) * gain).astype(jnp.bfloat16)


def extend(block, extra):
    return jnp.concatenate([block, extra], axis=0)


def ones_row(width):
    row = lax.broadcasted_iota(jnp.int32, (16, width), 0)
    return jnp.where(row == 0, 1.0, 0.0).astype(jnp.bfloat16)


def nearby_kernel(
    qt_ref, kt_ref, vt_ref, bias_ref, o_ref, keys_ref, *, groups, group_rows, factor
):
    keys_ref[...] = extend(kt_ref[...], bias_ref[...]).T
    key_count = keys_ref.shape[0]
    block = QUERY_BLOCK
    ones = ones_row(block)
    for first_row in range(0, groups * group_rows, block):
        rows = pl.ds(first_row, block)
        queries_t = extend(qt_ref[:, rows], ones)
        if PASS1 >= key_count and PASS2 >= key_count:
            scores_t = jnp.dot(keys_ref[...], queries_t, preferred_element_type=jnp.float32)
            top = jnp.max(scores_t, axis=0, keepdims=True)
            weights_t = jnp.exp2((scores_t - top) * factor)
            total = jnp.sum(weights_t, axis=0, keepdims=True)
            summed_t = jnp.dot(
                vt_ref[...], weights_t.astype(jnp.bfloat16), preferred_element_type=jnp.float32
            )
        else:
            top = None
            for first in range(0, key_count, PASS1):
                scores_t = jnp.dot(
                    keys_ref[pl.ds(first, PASS1), :], queries_t, preferred_element_type=jnp.float32
                )
                part = jnp.max(scores_t, axis=0, keepdims=True)
                top = part if top is None else jnp.maximum(top, part)
            total = None
            summed_t = None
            for first in range(0, key_count, PASS2):
                scores_t = jnp.dot(
                    keys_ref[pl.ds(first, PASS2), :], queries_t, preferred_element_type=jnp.float32
                )
                weights_t = jnp.exp2((scores_t - top) * factor)
                part = jnp.sum(weights_t, axis=0, keepdims=True)
                step = jnp.dot(
                    vt_ref[:, pl.ds(first, PASS2)],
                    weights_t.astype(jnp.bfloat16),
                    preferred_element_type=jnp.float32,
                )
                total = part if total is None else total + part
                summed_t = step if summed_t is None else summed_t + step
        o_ref[:, rows] = (summed_t / total).astype(o_ref.dtype)


def dilated_kernel(
    qt_ref, kt_ref, vt_ref, bias_ref, fk_ref, fv_ref, fbias_ref, prev_ref, o_ref,
    near_ref, far_ref, *, factor
):
    del prev_ref
    queries_t = extend(qt_ref[...], ones_row(qt_ref.shape[1]))
    near_ref[...] = extend(kt_ref[...], bias_ref[...]).T
    far_ref[...] = extend(fk_ref[0, 0], fbias_ref[0]).T
    sources = ((near_ref, lambda c: vt_ref[:, c]), (far_ref, lambda c: fv_ref[0, 0, :, c]))
    top = None
    for keys_ref, _ in sources:
        for first in range(0, keys_ref.shape[0], PASS1):
            scores_t = jnp.dot(
                keys_ref[pl.ds(first, PASS1), :], queries_t, preferred_element_type=jnp.float32
            )
            part = jnp.max(scores_t, axis=0, keepdims=True)
            top = part if top is None else jnp.maximum(top, part)
    total = None
    summed_t = None
    for keys_ref, values in sources:
        for first in range(0, keys_ref.shape[0], PASS2):
            chunk = pl.ds(first, PASS2)
            scores_t = jnp.dot(keys_ref[chunk, :], queries_t, preferred_element_type=jnp.float32)
            weights_t = jnp.exp2((scores_t - top) * factor)
            part = jnp.sum(weights_t, axis=0, keepdims=True)
            step = jnp.dot(
                values(chunk), weights_t.astype(jnp.bfloat16), preferred_element_type=jnp.float32
            )
            total = part if total is None else total + part
            summed_t = step if summed_t is None else summed_t + step
    o_ref[...] = (summed_t / total).astype(o_ref.dtype)


def body(embeddings, slot, lengths, in_weight, norm_gain, qkv_weight, out_weight):
    seq_count = lax.axis_size("seq")
    device_count = lax.axis_size("tile") * seq_count
    rows = embeddings.shape[0]
    block_rows = rows // device_count
    width = in_weight.shape[1]
    head_size = width // HEAD_COUNT
    group_rows = rows // DILATION_RATE
    far_count = group_rows * seq_count
    scale = head_size ** (-0.5)
    my_index = lax.axis_index("tile") * seq_count + lax.axis_index("seq")

    projected = jnp.dot(embeddings, in_weight, preferred_element_type=jnp.float32).astype(
        jnp.bfloat16
    )
    arrived = lax.all_to_all(
        projected.reshape(device_count, block_rows, width),
        ("tile", "seq"),
        split_axis=0,
        concat_axis=0,
        tiled=True,
    ).reshape(rows, width)
    arrived_slot = lax.all_to_all(
        slot.reshape(device_count, block_rows), ("tile", "seq"), split_axis=0, concat_axis=0, tiled=True
    ).reshape(rows)
    local_slot = arrived_slot - my_index * rows
    stored_slot = (local_slot % DILATION_RATE) * group_rows + local_slot // DILATION_RATE
    placement = (
        stored_slot[None, :] == jnp.arange(rows, dtype=jnp.int32)[:, None]
    ).astype(jnp.bfloat16)
    features = jnp.dot(placement, arrived, preferred_element_type=jnp.float32).astype(
        jnp.bfloat16
    )

    slide_length = lengths[0]
    stored = jnp.arange(rows, dtype=jnp.int32)
    local_position = (stored % group_rows) * DILATION_RATE + stored // group_rows
    position_ok = lax.axis_index("seq") * rows + local_position < slide_length
    extra_row = lax.broadcasted_iota(jnp.int32, (16, 1), 0) == 0
    near_bias = jnp.where(
        extra_row & ~position_ok[None, :], big_negative, 0.0
    ).astype(jnp.bfloat16)

    normed = normalize(features, norm_gain)
    projected_t = lax.dot_general(
        qkv_weight, normed, (((0,), (1,)), ((), ())), preferred_element_type=jnp.float32
    ).astype(jnp.bfloat16)

    offsets = [head % DILATION_RATE for head in range(HEAD_COUNT)]
    own_far = jnp.stack(
        [
            jnp.stack(
                [
                    projected_t[
                        (part * HEAD_COUNT + h) * head_size : (part * HEAD_COUNT + h + 1) * head_size,
                        o * group_rows : (o + 1) * group_rows,
                    ]
                    for h, o in enumerate(offsets)
                ]
            )
            for part in (1, 2)
        ]
    )
    far = lax.all_gather(own_far, "seq", axis=3, tiled=True)
    far_position = (
        jnp.arange(far_count, dtype=jnp.int32)[None, :] * DILATION_RATE
        + jnp.asarray(offsets, jnp.int32)[:, None]
    )
    far_bias = jnp.where(
        extra_row[None] & (far_position >= slide_length)[:, None, :], big_negative, 0.0
    ).astype(jnp.bfloat16)

    query_block = pl.BlockSpec((head_size, rows), lambda h: (h, 0))
    keys_block = pl.BlockSpec((head_size, rows), lambda h: (HEAD_COUNT + h, 0))
    values_block = pl.BlockSpec((head_size, rows), lambda h: (2 * HEAD_COUNT + h, 0))
    bias_block = pl.BlockSpec((16, rows), lambda h: (0, 0))
    factor = scale * 1.4426950408889634
    nearby = pl.pallas_call(
        functools.partial(
            nearby_kernel, groups=DILATION_RATE, group_rows=group_rows, factor=factor
        ),
        grid=(HEAD_COUNT,),
        in_specs=[query_block, keys_block, values_block, bias_block],
        out_specs=query_block,
        out_shape=jax.ShapeDtypeStruct((width, rows), jnp.bfloat16),
        scratch_shapes=[pltpu.VMEM((rows, head_size + 16), jnp.bfloat16)],
    )(projected_t, projected_t, projected_t, near_bias)

    group_block = pl.BlockSpec((head_size, group_rows), lambda h: (h, h % DILATION_RATE))
    attended_t = pl.pallas_call(
        functools.partial(dilated_kernel, factor=factor),
        grid=(HEAD_COUNT,),
        in_specs=[
            group_block,
            keys_block,
            values_block,
            bias_block,
            pl.BlockSpec((1, 1, head_size, far_count), lambda h: (0, h, 0, 0)),
            pl.BlockSpec((1, 1, head_size, far_count), lambda h: (1, h, 0, 0)),
            pl.BlockSpec((1, 16, far_count), lambda h: (h, 0, 0)),
            pl.BlockSpec(memory_space=pl.ANY),
        ],
        out_specs=group_block,
        out_shape=jax.ShapeDtypeStruct((width, rows), jnp.bfloat16),
        scratch_shapes=[
            pltpu.VMEM((rows, head_size + 16), jnp.bfloat16),
            pltpu.VMEM((far_count, head_size + 16), jnp.bfloat16),
        ],
        input_output_aliases={7: 0},
    )(projected_t, projected_t, projected_t, near_bias, far, far, far_bias, nearby)

    output = lax.dot_general(
        attended_t, out_weight, (((0,), (0,)), ((), ())), preferred_element_type=jnp.float32
    ) + features.astype(jnp.float32)
    output = jnp.where(position_ok[:, None], output, 0.0).astype(jnp.bfloat16)
    output = output.reshape(DILATION_RATE, group_rows, width).transpose(1, 0, 2)
    return output.reshape(1, rows, width)


def solution(mesh):
    return jax.shard_map(
        body,
        mesh=mesh,
        in_specs=(P(("tile", "seq"), None), P(("tile", "seq")), P("tile"), P(), P(), P(), P()),
        out_specs=P("tile", "seq", None),
        check_vma=False,
    )
```

```python
import functools

import jax
import jax.numpy as jnp
from jax import lax
from jax.experimental import pallas as pl
from jax.experimental.pallas import tpu as pltpu
from jax.sharding import PartitionSpec as P

HEAD_COUNT = 16
QUERY_BLOCK = 1024
PASS1 = 1024
PASS2 = 512
DILATION_RATE = 8


big_negative = -1e30
norm_epsilon = 1e-05


def normalize(features, gain):
    wide = features.astype(jnp.float32)
    average = jnp.mean(wide, axis=-1, keepdims=True)
    centered = wide - average
    spread = jnp.mean(centered * centered, axis=-1, keepdims=True)
    return (centered * lax.rsqrt(spread + norm_epsilon) * gain).astype(jnp.bfloat16)


def extend(block, extra):
    return jnp.concatenate([block, extra], axis=0)


def ones_row(width):
    row = lax.broadcasted_iota(jnp.int32, (16, width), 0)
    return jnp.where(row == 0, 1.0, 0.0).astype(jnp.bfloat16)


def nearby_kernel(
    qt_ref, kt_ref, vt_ref, bias_ref, o_ref, keys_ref, *, groups, group_rows, factor
):
    keys_ref[...] = extend(kt_ref[...], bias_ref[...]).T
    key_count = keys_ref.shape[0]
    block = QUERY_BLOCK
    ones = ones_row(block)
    for first_row in range(0, groups * group_rows, block):
        rows = pl.ds(first_row, block)
        queries_t = extend(qt_ref[:, rows], ones)
        if PASS1 >= key_count and PASS2 >= key_count:
            scores_t = jnp.dot(keys_ref[...], queries_t, preferred_element_type=jnp.float32)
            top = jnp.max(scores_t, axis=0, keepdims=True)
            weights_t = jnp.exp2((scores_t - top) * factor)
            total = jnp.sum(weights_t, axis=0, keepdims=True)
            summed_t = jnp.dot(
                vt_ref[...], weights_t.astype(jnp.bfloat16), preferred_element_type=jnp.float32
            )
        else:
            top = None
            for first in range(0, key_count, PASS1):
                scores_t = jnp.dot(
                    keys_ref[pl.ds(first, PASS1), :], queries_t, preferred_element_type=jnp.float32
                )
                part = jnp.max(scores_t, axis=0, keepdims=True)
                top = part if top is None else jnp.maximum(top, part)
            total = None
            summed_t = None
            for first in range(0, key_count, PASS2):
                scores_t = jnp.dot(
                    keys_ref[pl.ds(first, PASS2), :], queries_t, preferred_element_type=jnp.float32
                )
                weights_t = jnp.exp2((scores_t - top) * factor)
                part = jnp.sum(weights_t, axis=0, keepdims=True)
                step = jnp.dot(
                    vt_ref[:, pl.ds(first, PASS2)],
                    weights_t.astype(jnp.bfloat16),
                    preferred_element_type=jnp.float32,
                )
                total = part if total is None else total + part
                summed_t = step if summed_t is None else summed_t + step
        o_ref[:, rows] = (summed_t / total).astype(o_ref.dtype)


def dilated_kernel(
    qt_ref, kt_ref, vt_ref, bias_ref, fk_ref, fv_ref, fbias_ref, prev_ref, o_ref, *, factor
):
    del prev_ref
    queries_t = extend(qt_ref[...], ones_row(qt_ref.shape[1]))
    near_keys = extend(kt_ref[...], bias_ref[...]).T
    far_keys = extend(fk_ref[0, 0], fbias_ref[0]).T
    near = jnp.dot(near_keys, queries_t, preferred_element_type=jnp.float32)
    far = jnp.dot(far_keys, queries_t, preferred_element_type=jnp.float32)
    top = jnp.maximum(
        jnp.max(near, axis=0, keepdims=True), jnp.max(far, axis=0, keepdims=True)
    )
    near_w = jnp.exp2((near - top) * factor)
    far_w = jnp.exp2((far - top) * factor)
    total = jnp.sum(near_w, axis=0, keepdims=True) + jnp.sum(far_w, axis=0, keepdims=True)
    summed_t = jnp.dot(
        vt_ref[...], near_w.astype(jnp.bfloat16), preferred_element_type=jnp.float32
    )
    summed_t = summed_t + jnp.dot(
        fv_ref[0, 0], far_w.astype(jnp.bfloat16), preferred_element_type=jnp.float32
    )
    o_ref[...] = (summed_t / total).astype(o_ref.dtype)


def body(embeddings, slot, lengths, in_weight, norm_gain, qkv_weight, out_weight):
    seq_count = lax.axis_size("seq")
    device_count = lax.axis_size("tile") * seq_count
    rows = embeddings.shape[0]
    block_rows = rows // device_count
    width = in_weight.shape[1]
    head_size = width // HEAD_COUNT
    group_rows = rows // DILATION_RATE
    far_count = group_rows * seq_count
    scale = head_size ** (-0.5)
    my_index = lax.axis_index("tile") * seq_count + lax.axis_index("seq")

    projected = jnp.dot(embeddings, in_weight, preferred_element_type=jnp.float32).astype(
        jnp.bfloat16
    )
    arrived = lax.all_to_all(
        projected.reshape(device_count, block_rows, width),
        ("tile", "seq"),
        split_axis=0,
        concat_axis=0,
        tiled=True,
    ).reshape(rows, width)
    arrived_slot = lax.all_to_all(
        slot.reshape(device_count, block_rows), ("tile", "seq"), split_axis=0, concat_axis=0, tiled=True
    ).reshape(rows)
    local_slot = arrived_slot - my_index * rows
    stored_slot = (local_slot % DILATION_RATE) * group_rows + local_slot // DILATION_RATE
    placement = (
        stored_slot[None, :] == jnp.arange(rows, dtype=jnp.int32)[:, None]
    ).astype(jnp.bfloat16)
    features = jnp.dot(placement, arrived, preferred_element_type=jnp.float32).astype(
        jnp.bfloat16
    )

    slide_length = lengths[0]
    stored = jnp.arange(rows, dtype=jnp.int32)
    local_position = (stored % group_rows) * DILATION_RATE + stored // group_rows
    position_ok = lax.axis_index("seq") * rows + local_position < slide_length
    extra_row = lax.broadcasted_iota(jnp.int32, (16, 1), 0) == 0
    near_bias = jnp.where(
        extra_row & ~position_ok[None, :], big_negative, 0.0
    ).astype(jnp.bfloat16)

    normed = normalize(features, norm_gain)
    projected_t = lax.dot_general(
        qkv_weight, normed, (((0,), (1,)), ((), ())), preferred_element_type=jnp.float32
    ).astype(jnp.bfloat16)

    offsets = [head % DILATION_RATE for head in range(HEAD_COUNT)]
    own_far = jnp.stack(
        [
            jnp.stack(
                [
                    projected_t[
                        (part * HEAD_COUNT + h) * head_size : (part * HEAD_COUNT + h + 1) * head_size,
                        o * group_rows : (o + 1) * group_rows,
                    ]
                    for h, o in enumerate(offsets)
                ]
            )
            for part in (1, 2)
        ]
    )
    far = lax.all_gather(own_far, "seq", axis=3, tiled=True)
    far_position = (
        jnp.arange(far_count, dtype=jnp.int32)[None, :] * DILATION_RATE
        + jnp.asarray(offsets, jnp.int32)[:, None]
    )
    far_bias = jnp.where(
        extra_row[None] & (far_position >= slide_length)[:, None, :], big_negative, 0.0
    ).astype(jnp.bfloat16)

    query_block = pl.BlockSpec((head_size, rows), lambda h: (h, 0))
    keys_block = pl.BlockSpec((head_size, rows), lambda h: (HEAD_COUNT + h, 0))
    values_block = pl.BlockSpec((head_size, rows), lambda h: (2 * HEAD_COUNT + h, 0))
    bias_block = pl.BlockSpec((16, rows), lambda h: (0, 0))
    factor = scale * 1.4426950408889634
    nearby = pl.pallas_call(
        functools.partial(
            nearby_kernel, groups=DILATION_RATE, group_rows=group_rows, factor=factor
        ),
        grid=(HEAD_COUNT,),
        in_specs=[query_block, keys_block, values_block, bias_block],
        out_specs=query_block,
        out_shape=jax.ShapeDtypeStruct((width, rows), jnp.bfloat16),
        scratch_shapes=[pltpu.VMEM((rows, head_size + 16), jnp.bfloat16)],
    )(projected_t, projected_t, projected_t, near_bias)

    group_block = pl.BlockSpec((head_size, group_rows), lambda h: (h, h % DILATION_RATE))
    attended_t = pl.pallas_call(
        functools.partial(dilated_kernel, factor=factor),
        grid=(HEAD_COUNT,),
        in_specs=[
            group_block,
            keys_block,
            values_block,
            bias_block,
            pl.BlockSpec((1, 1, head_size, far_count), lambda h: (0, h, 0, 0)),
            pl.BlockSpec((1, 1, head_size, far_count), lambda h: (1, h, 0, 0)),
            pl.BlockSpec((1, 16, far_count), lambda h: (h, 0, 0)),
            pl.BlockSpec(memory_space=pl.ANY),
        ],
        out_specs=group_block,
        out_shape=jax.ShapeDtypeStruct((width, rows), jnp.bfloat16),
        input_output_aliases={7: 0},
    )(projected_t, projected_t, projected_t, near_bias, far, far, far_bias, nearby)

    output = lax.dot_general(
        attended_t, out_weight, (((0,), (0,)), ((), ())), preferred_element_type=jnp.float32
    ) + features.astype(jnp.float32)
    output = jnp.where(position_ok[:, None], output, 0.0).astype(jnp.bfloat16)
    output = output.reshape(DILATION_RATE, group_rows, width).transpose(1, 0, 2)
    return output.reshape(1, rows, width)


def solution(mesh):
    return jax.shard_map(
        body,
        mesh=mesh,
        in_specs=(P(("tile", "seq"), None), P(("tile", "seq")), P("tile"), P(), P(), P(), P()),
        out_specs=P("tile", "seq", None),
        check_vma=False,
    )
```

```python
import functools

import jax
import jax.numpy as jnp
from jax import lax
from jax.experimental import pallas as pl
from jax.experimental.pallas import tpu as pltpu
from jax.sharding import PartitionSpec as P

HEAD_COUNT = 16
QUERY_BLOCK = 1024
PASS1 = 1024
PASS2 = 512
DILATION_RATE = 8


big_negative = -1e30
norm_epsilon = 1e-05


def normalize(features, gain):
    wide = features.astype(jnp.float32)
    average = jnp.mean(wide, axis=-1, keepdims=True)
    centered = wide - average
    spread = jnp.mean(centered * centered, axis=-1, keepdims=True)
    return (centered * lax.rsqrt(spread + norm_epsilon) * gain).astype(jnp.bfloat16)


def extend(block, extra):
    return jnp.concatenate([block, extra], axis=0)


def ones_row(width):
    row = lax.broadcasted_iota(jnp.int32, (16, width), 0)
    return jnp.where(row == 0, 1.0, 0.0).astype(jnp.bfloat16)


def nearby_kernel(
    qt_ref, kt_ref, vt_ref, bias_ref, o_ref, keys_ref, *, groups, group_rows, factor
):
    keys_ref[...] = extend(kt_ref[...], bias_ref[...]).T
    key_count = keys_ref.shape[0]
    block = QUERY_BLOCK
    ones = ones_row(block)
    for first_row in range(0, groups * group_rows, block):
        rows = pl.ds(first_row, block)
        queries_t = extend(qt_ref[:, rows], ones)
        if PASS1 >= key_count and PASS2 >= key_count:
            scores_t = jnp.dot(keys_ref[...], queries_t, preferred_element_type=jnp.float32)
            top = jnp.max(scores_t, axis=0, keepdims=True)
            weights_t = jnp.exp2((scores_t - top) * factor)
            total = jnp.sum(weights_t, axis=0, keepdims=True)
            summed_t = jnp.dot(
                vt_ref[...], weights_t.astype(jnp.bfloat16), preferred_element_type=jnp.float32
            )
        else:
            top = None
            for first in range(0, key_count, PASS1):
                scores_t = jnp.dot(
                    keys_ref[pl.ds(first, PASS1), :], queries_t, preferred_element_type=jnp.float32
                )
                part = jnp.max(scores_t, axis=0, keepdims=True)
                top = part if top is None else jnp.maximum(top, part)
            total = None
            summed_t = None
            for first in range(0, key_count, PASS2):
                scores_t = jnp.dot(
                    keys_ref[pl.ds(first, PASS2), :], queries_t, preferred_element_type=jnp.float32
                )
                weights_t = jnp.exp2((scores_t - top) * factor)
                part = jnp.sum(weights_t, axis=0, keepdims=True)
                step = jnp.dot(
                    vt_ref[:, pl.ds(first, PASS2)],
                    weights_t.astype(jnp.bfloat16),
                    preferred_element_type=jnp.float32,
                )
                total = part if total is None else total + part
                summed_t = step if summed_t is None else summed_t + step
        o_ref[:, rows] = (summed_t / total).astype(o_ref.dtype)


def dilated_kernel(
    qt_ref, kt_ref, vt_ref, bias_ref, fk_ref, fv_ref, fbias_ref, prev_ref, o_ref, *, factor
):
    del prev_ref
    for pair in range(2):
        queries_t = extend(qt_ref[pair], ones_row(qt_ref.shape[2]))
        near_keys = extend(kt_ref[pair], bias_ref[...]).T
        far_keys = extend(fk_ref[0, pair, 0], fbias_ref[0]).T
        near = jnp.dot(near_keys, queries_t, preferred_element_type=jnp.float32)
        far = jnp.dot(far_keys, queries_t, preferred_element_type=jnp.float32)
        top = jnp.maximum(
            jnp.max(near, axis=0, keepdims=True), jnp.max(far, axis=0, keepdims=True)
        )
        near_w = jnp.exp2((near - top) * factor)
        far_w = jnp.exp2((far - top) * factor)
        total = jnp.sum(near_w, axis=0, keepdims=True) + jnp.sum(far_w, axis=0, keepdims=True)
        summed_t = jnp.dot(
            vt_ref[pair], near_w.astype(jnp.bfloat16), preferred_element_type=jnp.float32
        )
        summed_t = summed_t + jnp.dot(
            fv_ref[0, pair, 0], far_w.astype(jnp.bfloat16), preferred_element_type=jnp.float32
        )
        o_ref[pair] = (summed_t / total).astype(o_ref.dtype)


def body(embeddings, slot, lengths, in_weight, norm_gain, qkv_weight, out_weight):
    seq_count = lax.axis_size("seq")
    device_count = lax.axis_size("tile") * seq_count
    rows = embeddings.shape[0]
    block_rows = rows // device_count
    width = in_weight.shape[1]
    head_size = width // HEAD_COUNT
    group_rows = rows // DILATION_RATE
    far_count = group_rows * seq_count
    scale = head_size ** (-0.5)
    my_index = lax.axis_index("tile") * seq_count + lax.axis_index("seq")

    projected = jnp.dot(embeddings, in_weight, preferred_element_type=jnp.float32).astype(
        jnp.bfloat16
    )
    arrived = lax.all_to_all(
        projected.reshape(device_count, block_rows, width),
        ("tile", "seq"),
        split_axis=0,
        concat_axis=0,
        tiled=True,
    ).reshape(rows, width)
    arrived_slot = lax.all_to_all(
        slot.reshape(device_count, block_rows), ("tile", "seq"), split_axis=0, concat_axis=0, tiled=True
    ).reshape(rows)
    local_slot = arrived_slot - my_index * rows
    stored_slot = (local_slot % DILATION_RATE) * group_rows + local_slot // DILATION_RATE
    placement = (
        stored_slot[None, :] == jnp.arange(rows, dtype=jnp.int32)[:, None]
    ).astype(jnp.bfloat16)
    features = jnp.dot(placement, arrived, preferred_element_type=jnp.float32).astype(
        jnp.bfloat16
    )

    slide_length = lengths[0]
    stored = jnp.arange(rows, dtype=jnp.int32)
    local_position = (stored % group_rows) * DILATION_RATE + stored // group_rows
    position_ok = lax.axis_index("seq") * rows + local_position < slide_length
    extra_row = lax.broadcasted_iota(jnp.int32, (16, 1), 0) == 0
    near_bias = jnp.where(
        extra_row & ~position_ok[None, :], big_negative, 0.0
    ).astype(jnp.bfloat16)

    normed = normalize(features, norm_gain)
    projected_t = lax.dot_general(
        qkv_weight, normed, (((0,), (1,)), ((), ())), preferred_element_type=jnp.float32
    ).astype(jnp.bfloat16)

    offsets = [head % DILATION_RATE for head in range(HEAD_COUNT)]
    own_far = jnp.stack(
        [
            jnp.stack(
                [
                    projected_t[
                        (part * HEAD_COUNT + h) * head_size : (part * HEAD_COUNT + h + 1) * head_size,
                        o * group_rows : (o + 1) * group_rows,
                    ]
                    for h, o in enumerate(offsets)
                ]
            )
            for part in (1, 2)
        ]
    )
    far = lax.all_gather(own_far, "seq", axis=3, tiled=True)
    far_position = (
        jnp.arange(far_count, dtype=jnp.int32)[None, :] * DILATION_RATE
        + jnp.asarray(offsets, jnp.int32)[:, None]
    )
    far_bias = jnp.where(
        extra_row[None] & (far_position >= slide_length)[:, None, :], big_negative, 0.0
    ).astype(jnp.bfloat16)

    query_block = pl.BlockSpec((head_size, rows), lambda h: (h, 0))
    keys_block = pl.BlockSpec((head_size, rows), lambda h: (HEAD_COUNT + h, 0))
    values_block = pl.BlockSpec((head_size, rows), lambda h: (2 * HEAD_COUNT + h, 0))
    bias_block = pl.BlockSpec((16, rows), lambda h: (0, 0))
    factor = scale * 1.4426950408889634
    nearby = pl.pallas_call(
        functools.partial(
            nearby_kernel, groups=DILATION_RATE, group_rows=group_rows, factor=factor
        ),
        grid=(HEAD_COUNT,),
        in_specs=[query_block, keys_block, values_block, bias_block],
        out_specs=query_block,
        out_shape=jax.ShapeDtypeStruct((width, rows), jnp.bfloat16),
        scratch_shapes=[pltpu.VMEM((rows, head_size + 16), jnp.bfloat16)],
    )(projected_t, projected_t, projected_t, near_bias)

    half = HEAD_COUNT // 2
    paired = projected_t.reshape(6, half * head_size, rows)
    far_paired = far.reshape(2, 2, half, head_size, far_count)
    group_block = pl.BlockSpec(
        (2, head_size, group_rows), lambda i: (0, i, i % DILATION_RATE)
    )
    far_block = (1, 2, 1, head_size, far_count)
    attended_t = pl.pallas_call(
        functools.partial(dilated_kernel, factor=factor),
        grid=(half,),
        in_specs=[
            pl.BlockSpec((2, head_size, group_rows), lambda i: (0, i, i % DILATION_RATE)),
            pl.BlockSpec((2, head_size, rows), lambda i: (1, i, 0)),
            pl.BlockSpec((2, head_size, rows), lambda i: (2, i, 0)),
            bias_block,
            pl.BlockSpec(far_block, lambda i: (0, 0, i, 0, 0)),
            pl.BlockSpec(far_block, lambda i: (1, 0, i, 0, 0)),
            pl.BlockSpec((1, 16, far_count), lambda i: (i, 0, 0)),
            pl.BlockSpec(memory_space=pl.ANY),
        ],
        out_specs=group_block,
        out_shape=jax.ShapeDtypeStruct((2, half * head_size, rows), jnp.bfloat16),
        input_output_aliases={7: 0},
    )(
        paired, paired, paired, near_bias, far_paired, far_paired, far_bias,
        nearby.reshape(2, half * head_size, rows),
    ).reshape(width, rows)

    output = lax.dot_general(
        attended_t, out_weight, (((0,), (0,)), ((), ())), preferred_element_type=jnp.float32
    ) + features.astype(jnp.float32)
    output = jnp.where(position_ok[:, None], output, 0.0).astype(jnp.bfloat16)
    output = output.reshape(DILATION_RATE, group_rows, width).transpose(1, 0, 2)
    return output.reshape(1, rows, width)


def solution(mesh):
    return jax.shard_map(
        body,
        mesh=mesh,
        in_specs=(P(("tile", "seq"), None), P(("tile", "seq")), P("tile"), P(), P(), P(), P()),
        out_specs=P("tile", "seq", None),
        check_vma=False,
    )
```

```python
import functools

import jax
import jax.numpy as jnp
from jax import lax
from jax.experimental import pallas as pl
from jax.experimental.pallas import tpu as pltpu
from jax.sharding import PartitionSpec as P

HEAD_COUNT = 16
QUERY_BLOCK = 1024
PASS1 = 1024
PASS2 = 512
DILATION_RATE = 8


big_negative = -1e30
norm_epsilon = 1e-05


def normalize(features, gain):
    wide = features.astype(jnp.float32)
    average = jnp.mean(wide, axis=-1, keepdims=True)
    centered = wide - average
    spread = jnp.mean(centered * centered, axis=-1, keepdims=True)
    return (centered * lax.rsqrt(spread + norm_epsilon) * gain).astype(jnp.bfloat16)


def extend(block, extra):
    return jnp.concatenate([block, extra], axis=0)


def ones_row(width):
    row = lax.broadcasted_iota(jnp.int32, (16, width), 0)
    return jnp.where(row == 0, 1.0, 0.0).astype(jnp.bfloat16)


def nearby_kernel(
    qt_ref, kt_ref, vt_ref, bias_ref, o_ref, keys_ref, *, groups, group_rows, factor
):
    keys_ref[...] = extend(kt_ref[...], bias_ref[...]).T
    key_count = keys_ref.shape[0]
    block = QUERY_BLOCK
    ones = ones_row(block)
    for first_row in range(0, groups * group_rows, block):
        rows = pl.ds(first_row, block)
        queries_t = extend(qt_ref[:, rows], ones)
        if PASS1 >= key_count and PASS2 >= key_count:
            scores_t = jnp.dot(keys_ref[...], queries_t, preferred_element_type=jnp.float32)
            top = jnp.max(scores_t, axis=0, keepdims=True)
            weights_t = jnp.exp2((scores_t - top) * factor)
            total = jnp.sum(weights_t, axis=0, keepdims=True)
            summed_t = jnp.dot(
                vt_ref[...], weights_t.astype(jnp.bfloat16), preferred_element_type=jnp.float32
            )
        else:
            top = None
            for first in range(0, key_count, PASS1):
                scores_t = jnp.dot(
                    keys_ref[pl.ds(first, PASS1), :], queries_t, preferred_element_type=jnp.float32
                )
                part = jnp.max(scores_t, axis=0, keepdims=True)
                top = part if top is None else jnp.maximum(top, part)
            total = None
            summed_t = None
            for first in range(0, key_count, PASS2):
                scores_t = jnp.dot(
                    keys_ref[pl.ds(first, PASS2), :], queries_t, preferred_element_type=jnp.float32
                )
                weights_t = jnp.exp2((scores_t - top) * factor)
                part = jnp.sum(weights_t, axis=0, keepdims=True)
                step = jnp.dot(
                    vt_ref[:, pl.ds(first, PASS2)],
                    weights_t.astype(jnp.bfloat16),
                    preferred_element_type=jnp.float32,
                )
                total = part if total is None else total + part
                summed_t = step if summed_t is None else summed_t + step
        o_ref[:, rows] = (summed_t / total).astype(o_ref.dtype)


def joined(ref, pair):
    return jnp.concatenate([ref[chunk, 0, pair, 0] for chunk in range(ref.shape[0])], axis=1)


def dilated_kernel(
    qt_ref, kt_ref, vt_ref, bias_ref, fk_ref, fv_ref, fbias_ref, prev_ref, o_ref, *, factor
):
    del prev_ref
    for pair in range(2):
        queries_t = extend(qt_ref[pair], ones_row(qt_ref.shape[2]))
        near_keys = extend(kt_ref[pair], bias_ref[...]).T
        far_keys = extend(joined(fk_ref, pair), fbias_ref[0]).T
        near = jnp.dot(near_keys, queries_t, preferred_element_type=jnp.float32)
        far = jnp.dot(far_keys, queries_t, preferred_element_type=jnp.float32)
        top = jnp.maximum(
            jnp.max(near, axis=0, keepdims=True), jnp.max(far, axis=0, keepdims=True)
        )
        near_w = jnp.exp2((near - top) * factor)
        far_w = jnp.exp2((far - top) * factor)
        total = jnp.sum(near_w, axis=0, keepdims=True) + jnp.sum(far_w, axis=0, keepdims=True)
        summed_t = jnp.dot(
            vt_ref[pair], near_w.astype(jnp.bfloat16), preferred_element_type=jnp.float32
        )
        summed_t = summed_t + jnp.dot(
            joined(fv_ref, pair), far_w.astype(jnp.bfloat16), preferred_element_type=jnp.float32
        )
        o_ref[pair] = (summed_t / total).astype(o_ref.dtype)


def body(embeddings, slot, lengths, in_weight, norm_gain, qkv_weight, out_weight):
    seq_count = lax.axis_size("seq")
    device_count = lax.axis_size("tile") * seq_count
    rows = embeddings.shape[0]
    block_rows = rows // device_count
    width = in_weight.shape[1]
    head_size = width // HEAD_COUNT
    group_rows = rows // DILATION_RATE
    far_count = group_rows * seq_count
    scale = head_size ** (-0.5)
    my_index = lax.axis_index("tile") * seq_count + lax.axis_index("seq")

    projected = jnp.dot(embeddings, in_weight, preferred_element_type=jnp.float32).astype(
        jnp.bfloat16
    )
    arrived = lax.all_to_all(
        projected.reshape(device_count, block_rows, width),
        ("tile", "seq"),
        split_axis=0,
        concat_axis=0,
        tiled=True,
    ).reshape(rows, width)
    arrived_slot = lax.all_to_all(
        slot.reshape(device_count, block_rows), ("tile", "seq"), split_axis=0, concat_axis=0, tiled=True
    ).reshape(rows)
    local_slot = arrived_slot - my_index * rows
    stored_slot = (local_slot % DILATION_RATE) * group_rows + local_slot // DILATION_RATE
    placement = (
        stored_slot[None, :] == jnp.arange(rows, dtype=jnp.int32)[:, None]
    ).astype(jnp.bfloat16)
    features = jnp.dot(placement, arrived, preferred_element_type=jnp.float32).astype(
        jnp.bfloat16
    )

    slide_length = lengths[0]
    stored = jnp.arange(rows, dtype=jnp.int32)
    local_position = (stored % group_rows) * DILATION_RATE + stored // group_rows
    position_ok = lax.axis_index("seq") * rows + local_position < slide_length
    extra_row = lax.broadcasted_iota(jnp.int32, (16, 1), 0) == 0
    near_bias = jnp.where(
        extra_row & ~position_ok[None, :], big_negative, 0.0
    ).astype(jnp.bfloat16)

    normed = normalize(features, norm_gain)
    projected_t = lax.dot_general(
        qkv_weight, normed, (((0,), (1,)), ((), ())), preferred_element_type=jnp.float32
    ).astype(jnp.bfloat16)

    offsets = [head % DILATION_RATE for head in range(HEAD_COUNT)]
    own_far = jnp.stack(
        [
            jnp.stack(
                [
                    projected_t[
                        (part * HEAD_COUNT + h) * head_size : (part * HEAD_COUNT + h + 1) * head_size,
                        o * group_rows : (o + 1) * group_rows,
                    ]
                    for h, o in enumerate(offsets)
                ]
            )
            for part in (1, 2)
        ]
    )
    far = lax.all_to_all(
        jnp.broadcast_to(own_far[None], (seq_count,) + own_far.shape),
        "seq",
        split_axis=0,
        concat_axis=0,
        tiled=True,
    )
    far_position = (
        jnp.arange(far_count, dtype=jnp.int32)[None, :] * DILATION_RATE
        + jnp.asarray(offsets, jnp.int32)[:, None]
    )
    far_bias = jnp.where(
        extra_row[None] & (far_position >= slide_length)[:, None, :], big_negative, 0.0
    ).astype(jnp.bfloat16)

    query_block = pl.BlockSpec((head_size, rows), lambda h: (h, 0))
    keys_block = pl.BlockSpec((head_size, rows), lambda h: (HEAD_COUNT + h, 0))
    values_block = pl.BlockSpec((head_size, rows), lambda h: (2 * HEAD_COUNT + h, 0))
    bias_block = pl.BlockSpec((16, rows), lambda h: (0, 0))
    factor = scale * 1.4426950408889634
    nearby = pl.pallas_call(
        functools.partial(
            nearby_kernel, groups=DILATION_RATE, group_rows=group_rows, factor=factor
        ),
        grid=(HEAD_COUNT,),
        in_specs=[query_block, keys_block, values_block, bias_block],
        out_specs=query_block,
        out_shape=jax.ShapeDtypeStruct((width, rows), jnp.bfloat16),
        scratch_shapes=[pltpu.VMEM((rows, head_size + 16), jnp.bfloat16)],
    )(projected_t, projected_t, projected_t, near_bias)

    half = HEAD_COUNT // 2
    paired = projected_t.reshape(6, half * head_size, rows)
    far_paired = far.reshape(seq_count, 2, 2, half, head_size, group_rows)
    group_block = pl.BlockSpec(
        (2, head_size, group_rows), lambda i: (0, i, i % DILATION_RATE)
    )
    far_block = (seq_count, 1, 2, 1, head_size, group_rows)
    attended_t = pl.pallas_call(
        functools.partial(dilated_kernel, factor=factor),
        grid=(half,),
        in_specs=[
            pl.BlockSpec((2, head_size, group_rows), lambda i: (0, i, i % DILATION_RATE)),
            pl.BlockSpec((2, head_size, rows), lambda i: (1, i, 0)),
            pl.BlockSpec((2, head_size, rows), lambda i: (2, i, 0)),
            bias_block,
            pl.BlockSpec(far_block, lambda i: (0, 0, 0, i, 0, 0)),
            pl.BlockSpec(far_block, lambda i: (0, 1, 0, i, 0, 0)),
            pl.BlockSpec((1, 16, far_count), lambda i: (i, 0, 0)),
            pl.BlockSpec(memory_space=pl.ANY),
        ],
        out_specs=group_block,
        out_shape=jax.ShapeDtypeStruct((2, half * head_size, rows), jnp.bfloat16),
        input_output_aliases={7: 0},
    )(
        paired, paired, paired, near_bias, far_paired, far_paired, far_bias,
        nearby.reshape(2, half * head_size, rows),
    ).reshape(width, rows)

    output = lax.dot_general(
        attended_t, out_weight, (((0,), (0,)), ((), ())), preferred_element_type=jnp.float32
    ) + features.astype(jnp.float32)
    output = jnp.where(position_ok[:, None], output, 0.0).astype(jnp.bfloat16)
    output = output.reshape(DILATION_RATE, group_rows, width).transpose(1, 0, 2)
    return output.reshape(1, rows, width)


def solution(mesh):
    return jax.shard_map(
        body,
        mesh=mesh,
        in_specs=(P(("tile", "seq"), None), P(("tile", "seq")), P("tile"), P(), P(), P(), P()),
        out_specs=P("tile", "seq", None),
        check_vma=False,
    )
```

```python
import functools

import jax
import jax.numpy as jnp
from jax import lax
from jax.experimental import pallas as pl
from jax.experimental.pallas import tpu as pltpu
from jax.sharding import PartitionSpec as P

HEAD_COUNT = 16
QUERY_BLOCK = 1024
PASS1 = 1024
PASS2 = 512
DILATION_RATE = 8


big_negative = -1e30
norm_epsilon = 1e-05


def normalize(features, gain):
    wide = features.astype(jnp.float32)
    average = jnp.mean(wide, axis=-1, keepdims=True)
    centered = wide - average
    spread = jnp.mean(centered * centered, axis=-1, keepdims=True)
    return (centered * lax.rsqrt(spread + norm_epsilon) * gain).astype(jnp.bfloat16)


def extend(block, extra):
    return jnp.concatenate([block, extra], axis=0)


def ones_row(width):
    row = lax.broadcasted_iota(jnp.int32, (16, width), 0)
    return jnp.where(row == 0, 1.0, 0.0).astype(jnp.bfloat16)


def nearby_kernel(
    qt_ref, kt_ref, vt_ref, bias_ref, o_ref, keys_ref, *, groups, group_rows, factor
):
    keys_ref[...] = extend(kt_ref[...], bias_ref[...]).T
    key_count = keys_ref.shape[0]
    block = QUERY_BLOCK
    ones = ones_row(block)
    for first_row in range(0, groups * group_rows, block):
        rows = pl.ds(first_row, block)
        queries_t = extend(qt_ref[:, rows], ones)
        if PASS1 >= key_count and PASS2 >= key_count:
            scores_t = jnp.dot(keys_ref[...], queries_t, preferred_element_type=jnp.float32)
            top = jnp.max(scores_t, axis=0, keepdims=True)
            weights_t = jnp.exp2((scores_t - top) * factor)
            total = jnp.sum(weights_t, axis=0, keepdims=True)
            summed_t = jnp.dot(
                vt_ref[...], weights_t.astype(jnp.bfloat16), preferred_element_type=jnp.float32
            )
        else:
            top = None
            for first in range(0, key_count, PASS1):
                scores_t = jnp.dot(
                    keys_ref[pl.ds(first, PASS1), :], queries_t, preferred_element_type=jnp.float32
                )
                part = jnp.max(scores_t, axis=0, keepdims=True)
                top = part if top is None else jnp.maximum(top, part)
            total = None
            summed_t = None
            for first in range(0, key_count, PASS2):
                scores_t = jnp.dot(
                    keys_ref[pl.ds(first, PASS2), :], queries_t, preferred_element_type=jnp.float32
                )
                weights_t = jnp.exp2((scores_t - top) * factor)
                part = jnp.sum(weights_t, axis=0, keepdims=True)
                step = jnp.dot(
                    vt_ref[:, pl.ds(first, PASS2)],
                    weights_t.astype(jnp.bfloat16),
                    preferred_element_type=jnp.float32,
                )
                total = part if total is None else total + part
                summed_t = step if summed_t is None else summed_t + step
        o_ref[:, rows] = (summed_t / total).astype(o_ref.dtype)


def joined(ref, pair):
    return jnp.concatenate([ref[chunk, 0, pair, 0] for chunk in range(ref.shape[0])], axis=1)


def dilated_kernel(
    qt_ref, kt_ref, vt_ref, bias_ref, fk_ref, fv_ref, fbias_ref, prev_ref, o_ref, *, factor
):
    del prev_ref
    for pair in range(2):
        queries_t = extend(qt_ref[pair], ones_row(qt_ref.shape[2]))
        near_keys = extend(kt_ref[pair], bias_ref[...]).T
        far_keys = extend(joined(fk_ref, pair), fbias_ref[0]).T
        near = jnp.dot(near_keys, queries_t, preferred_element_type=jnp.float32)
        far = jnp.dot(far_keys, queries_t, preferred_element_type=jnp.float32)
        top = jnp.maximum(
            jnp.max(near, axis=0, keepdims=True), jnp.max(far, axis=0, keepdims=True)
        )
        near_w = jnp.exp2((near - top) * factor)
        far_w = jnp.exp2((far - top) * factor)
        total = jnp.sum(near_w, axis=0, keepdims=True) + jnp.sum(far_w, axis=0, keepdims=True)
        summed_t = jnp.dot(
            vt_ref[pair], near_w.astype(jnp.bfloat16), preferred_element_type=jnp.float32
        )
        summed_t = summed_t + jnp.dot(
            joined(fv_ref, pair), far_w.astype(jnp.bfloat16), preferred_element_type=jnp.float32
        )
        o_ref[pair] = (summed_t / total).astype(o_ref.dtype)


def body(embeddings, slot, lengths, in_weight, norm_gain, qkv_weight, out_weight):
    seq_count = lax.axis_size("seq")
    device_count = lax.axis_size("tile") * seq_count
    rows = embeddings.shape[0]
    block_rows = rows // device_count
    width = in_weight.shape[1]
    head_size = width // HEAD_COUNT
    group_rows = rows // DILATION_RATE
    far_count = group_rows * seq_count
    scale = head_size ** (-0.5)
    my_index = lax.axis_index("tile") * seq_count + lax.axis_index("seq")

    projected = jnp.dot(embeddings, in_weight, preferred_element_type=jnp.float32).astype(
        jnp.bfloat16
    )
    arrived = lax.all_to_all(
        projected.reshape(device_count, block_rows, width),
        ("tile", "seq"),
        split_axis=0,
        concat_axis=0,
        tiled=True,
    ).reshape(rows, width)
    arrived_slot = lax.all_to_all(
        slot.reshape(device_count, block_rows), ("tile", "seq"), split_axis=0, concat_axis=0, tiled=True
    ).reshape(rows)
    local_slot = arrived_slot - my_index * rows
    stored_slot = (local_slot % DILATION_RATE) * group_rows + local_slot // DILATION_RATE
    placement = (
        stored_slot[None, :] == jnp.arange(rows, dtype=jnp.int32)[:, None]
    ).astype(jnp.bfloat16)
    features = jnp.dot(placement, arrived, preferred_element_type=jnp.float32).astype(
        jnp.bfloat16
    )

    slide_length = lengths[0]
    stored = jnp.arange(rows, dtype=jnp.int32)
    local_position = (stored % group_rows) * DILATION_RATE + stored // group_rows
    position_ok = lax.axis_index("seq") * rows + local_position < slide_length
    extra_row = lax.broadcasted_iota(jnp.int32, (16, 1), 0) == 0
    near_bias = jnp.where(
        extra_row & ~position_ok[None, :], big_negative, 0.0
    ).astype(jnp.bfloat16)

    normed = normalize(features, norm_gain)
    projected_t = lax.dot_general(
        qkv_weight, normed, (((0,), (1,)), ((), ())), preferred_element_type=jnp.float32
    ).astype(jnp.bfloat16)

    offsets = [head % DILATION_RATE for head in range(HEAD_COUNT)]
    half = HEAD_COUNT // 2
    grouped = normed.reshape(DILATION_RATE, group_rows, width)
    own_far = jnp.stack(
        [
            jnp.einsum(
                "ljc,chld->hldj",
                grouped,
                qkv_weight[:, part * width : (part + 1) * width].reshape(
                    width, HEAD_COUNT // DILATION_RATE, DILATION_RATE, head_size
                ),
                preferred_element_type=jnp.float32,
            )
            .astype(jnp.bfloat16)
            .reshape(HEAD_COUNT, head_size, group_rows)
            for part in (1, 2)
        ]
    )
    far = lax.all_to_all(
        jnp.broadcast_to(own_far[None], (seq_count,) + own_far.shape),
        "seq",
        split_axis=0,
        concat_axis=0,
        tiled=True,
    )
    far_position = (
        jnp.arange(far_count, dtype=jnp.int32)[None, :] * DILATION_RATE
        + jnp.asarray(offsets, jnp.int32)[:, None]
    )
    far_bias = jnp.where(
        extra_row[None] & (far_position >= slide_length)[:, None, :], big_negative, 0.0
    ).astype(jnp.bfloat16)

    query_block = pl.BlockSpec((head_size, rows), lambda h: (h, 0))
    keys_block = pl.BlockSpec((head_size, rows), lambda h: (HEAD_COUNT + h, 0))
    values_block = pl.BlockSpec((head_size, rows), lambda h: (2 * HEAD_COUNT + h, 0))
    bias_block = pl.BlockSpec((16, rows), lambda h: (0, 0))
    factor = scale * 1.4426950408889634
    nearby = pl.pallas_call(
        functools.partial(
            nearby_kernel, groups=DILATION_RATE, group_rows=group_rows, factor=factor
        ),
        grid=(HEAD_COUNT,),
        in_specs=[query_block, keys_block, values_block, bias_block],
        out_specs=query_block,
        out_shape=jax.ShapeDtypeStruct((width, rows), jnp.bfloat16),
        scratch_shapes=[pltpu.VMEM((rows, head_size + 16), jnp.bfloat16)],
    )(projected_t, projected_t, projected_t, near_bias)

    paired = projected_t.reshape(6, half * head_size, rows)
    far_paired = far.reshape(seq_count, 2, 2, half, head_size, group_rows)
    group_block = pl.BlockSpec(
        (2, head_size, group_rows), lambda i: (0, i, i % DILATION_RATE)
    )
    far_block = (seq_count, 1, 2, 1, head_size, group_rows)
    attended_t = pl.pallas_call(
        functools.partial(dilated_kernel, factor=factor),
        grid=(half,),
        in_specs=[
            pl.BlockSpec((2, head_size, group_rows), lambda i: (0, i, i % DILATION_RATE)),
            pl.BlockSpec((2, head_size, rows), lambda i: (1, i, 0)),
            pl.BlockSpec((2, head_size, rows), lambda i: (2, i, 0)),
            bias_block,
            pl.BlockSpec(far_block, lambda i: (0, 0, 0, i, 0, 0)),
            pl.BlockSpec(far_block, lambda i: (0, 1, 0, i, 0, 0)),
            pl.BlockSpec((1, 16, far_count), lambda i: (i, 0, 0)),
            pl.BlockSpec(memory_space=pl.ANY),
        ],
        out_specs=group_block,
        out_shape=jax.ShapeDtypeStruct((2, half * head_size, rows), jnp.bfloat16),
        input_output_aliases={7: 0},
    )(
        paired, paired, paired, near_bias, far_paired, far_paired, far_bias,
        nearby.reshape(2, half * head_size, rows),
    ).reshape(width, rows)

    output = lax.dot_general(
        attended_t, out_weight, (((0,), (0,)), ((), ())), preferred_element_type=jnp.float32
    ) + features.astype(jnp.float32)
    output = jnp.where(position_ok[:, None], output, 0.0).astype(jnp.bfloat16)
    output = output.reshape(DILATION_RATE, group_rows, width).transpose(1, 0, 2)
    return output.reshape(1, rows, width)


def solution(mesh):
    return jax.shard_map(
        body,
        mesh=mesh,
        in_specs=(P(("tile", "seq"), None), P(("tile", "seq")), P("tile"), P(), P(), P(), P()),
        out_specs=P("tile", "seq", None),
        check_vma=False,
    )
```

```python
import functools

import jax
import jax.numpy as jnp
from jax import lax
from jax.experimental import pallas as pl
from jax.experimental.pallas import tpu as pltpu
from jax.sharding import PartitionSpec as P

HEAD_COUNT = 16
QUERY_BLOCK = 1024
PASS1 = 1024
PASS2 = 512
DILATION_RATE = 8


big_negative = -1e30
norm_epsilon = 1e-05


def normalize(features, gain):
    wide = features.astype(jnp.float32)
    average = jnp.mean(wide, axis=-1, keepdims=True)
    centered = wide - average
    spread = jnp.mean(centered * centered, axis=-1, keepdims=True)
    return (centered * lax.rsqrt(spread + norm_epsilon) * gain).astype(jnp.bfloat16)


def extend(block, extra):
    return jnp.concatenate([block, extra], axis=0)


def ones_row(width):
    row = lax.broadcasted_iota(jnp.int32, (16, width), 0)
    return jnp.where(row == 0, 1.0, 0.0).astype(jnp.bfloat16)


def nearby_kernel(
    qt_ref, kt_ref, vt_ref, bias_ref, o_ref, keys_ref, *, groups, group_rows, factor
):
    key_count = keys_ref.shape[1]
    block = QUERY_BLOCK
    ones = ones_row(block)
    for pair in range(2):
        keys_ref[pair] = extend(kt_ref[pair], bias_ref[...]).T
    for pair in range(2):
        for first_row in range(0, groups * group_rows, block):
            rows = pl.ds(first_row, block)
            queries_t = extend(qt_ref[pair, :, rows], ones)
            top = None
            for first in range(0, key_count, PASS1):
                scores_t = jnp.dot(
                    keys_ref[pair, pl.ds(first, PASS1), :],
                    queries_t,
                    preferred_element_type=jnp.float32,
                )
                part = jnp.max(scores_t, axis=0, keepdims=True)
                top = part if top is None else jnp.maximum(top, part)
            total = None
            summed_t = None
            for first in range(0, key_count, PASS2):
                scores_t = jnp.dot(
                    keys_ref[pair, pl.ds(first, PASS2), :],
                    queries_t,
                    preferred_element_type=jnp.float32,
                )
                weights_t = jnp.exp2((scores_t - top) * factor)
                part = jnp.sum(weights_t, axis=0, keepdims=True)
                step = jnp.dot(
                    vt_ref[pair, :, pl.ds(first, PASS2)],
                    weights_t.astype(jnp.bfloat16),
                    preferred_element_type=jnp.float32,
                )
                total = part if total is None else total + part
                summed_t = step if summed_t is None else summed_t + step
            o_ref[pair, :, rows] = (summed_t / total).astype(o_ref.dtype)


def joined(ref, pair):
    return jnp.concatenate([ref[chunk, 0, pair, 0] for chunk in range(ref.shape[0])], axis=1)


def dilated_kernel(
    qt_ref, kt_ref, vt_ref, bias_ref, fk_ref, fv_ref, fbias_ref, prev_ref, o_ref, *, factor
):
    del prev_ref
    for pair in range(2):
        queries_t = extend(qt_ref[pair], ones_row(qt_ref.shape[2]))
        near_keys = extend(kt_ref[pair], bias_ref[...]).T
        far_keys = extend(joined(fk_ref, pair), fbias_ref[0]).T
        near = jnp.dot(near_keys, queries_t, preferred_element_type=jnp.float32)
        far = jnp.dot(far_keys, queries_t, preferred_element_type=jnp.float32)
        top = jnp.maximum(
            jnp.max(near, axis=0, keepdims=True), jnp.max(far, axis=0, keepdims=True)
        )
        near_w = jnp.exp2((near - top) * factor)
        far_w = jnp.exp2((far - top) * factor)
        total = jnp.sum(near_w, axis=0, keepdims=True) + jnp.sum(far_w, axis=0, keepdims=True)
        summed_t = jnp.dot(
            vt_ref[pair], near_w.astype(jnp.bfloat16), preferred_element_type=jnp.float32
        )
        summed_t = summed_t + jnp.dot(
            joined(fv_ref, pair), far_w.astype(jnp.bfloat16), preferred_element_type=jnp.float32
        )
        o_ref[pair] = (summed_t / total).astype(o_ref.dtype)


def body(embeddings, slot, lengths, in_weight, norm_gain, qkv_weight, out_weight):
    seq_count = lax.axis_size("seq")
    device_count = lax.axis_size("tile") * seq_count
    rows = embeddings.shape[0]
    block_rows = rows // device_count
    width = in_weight.shape[1]
    head_size = width // HEAD_COUNT
    group_rows = rows // DILATION_RATE
    far_count = group_rows * seq_count
    scale = head_size ** (-0.5)
    my_index = lax.axis_index("tile") * seq_count + lax.axis_index("seq")

    projected = jnp.dot(embeddings, in_weight, preferred_element_type=jnp.float32).astype(
        jnp.bfloat16
    )
    arrived = lax.all_to_all(
        projected.reshape(device_count, block_rows, width),
        ("tile", "seq"),
        split_axis=0,
        concat_axis=0,
        tiled=True,
    ).reshape(rows, width)
    arrived_slot = lax.all_to_all(
        slot.reshape(device_count, block_rows), ("tile", "seq"), split_axis=0, concat_axis=0, tiled=True
    ).reshape(rows)
    local_slot = arrived_slot - my_index * rows
    stored_slot = (local_slot % DILATION_RATE) * group_rows + local_slot // DILATION_RATE
    placement = (
        stored_slot[None, :] == jnp.arange(rows, dtype=jnp.int32)[:, None]
    ).astype(jnp.bfloat16)
    features = jnp.dot(placement, arrived, preferred_element_type=jnp.float32).astype(
        jnp.bfloat16
    )

    slide_length = lengths[0]
    stored = jnp.arange(rows, dtype=jnp.int32)
    local_position = (stored % group_rows) * DILATION_RATE + stored // group_rows
    position_ok = lax.axis_index("seq") * rows + local_position < slide_length
    extra_row = lax.broadcasted_iota(jnp.int32, (16, 1), 0) == 0
    near_bias = jnp.where(
        extra_row & ~position_ok[None, :], big_negative, 0.0
    ).astype(jnp.bfloat16)

    normed = normalize(features, norm_gain)
    projected_t = lax.dot_general(
        qkv_weight, normed, (((0,), (1,)), ((), ())), preferred_element_type=jnp.float32
    ).astype(jnp.bfloat16)

    offsets = [head % DILATION_RATE for head in range(HEAD_COUNT)]
    half = HEAD_COUNT // 2
    grouped = normed.reshape(DILATION_RATE, group_rows, width)
    own_far = jnp.stack(
        [
            jnp.einsum(
                "ljc,chld->hldj",
                grouped,
                qkv_weight[:, part * width : (part + 1) * width].reshape(
                    width, HEAD_COUNT // DILATION_RATE, DILATION_RATE, head_size
                ),
                preferred_element_type=jnp.float32,
            )
            .astype(jnp.bfloat16)
            .reshape(HEAD_COUNT, head_size, group_rows)
            for part in (1, 2)
        ]
    )
    far = lax.all_to_all(
        jnp.broadcast_to(own_far[None], (seq_count,) + own_far.shape),
        "seq",
        split_axis=0,
        concat_axis=0,
        tiled=True,
    )
    far_position = (
        jnp.arange(far_count, dtype=jnp.int32)[None, :] * DILATION_RATE
        + jnp.asarray(offsets, jnp.int32)[:, None]
    )
    far_bias = jnp.where(
        extra_row[None] & (far_position >= slide_length)[:, None, :], big_negative, 0.0
    ).astype(jnp.bfloat16)

    bias_block = pl.BlockSpec((16, rows), lambda i: (0, 0))
    factor = scale * 1.4426950408889634
    paired = projected_t.reshape(6, half * head_size, rows)
    head_pairs = [
        pl.BlockSpec((2, head_size, rows), lambda i, part=part: (part, i, 0)) for part in range(3)
    ]
    nearby = pl.pallas_call(
        functools.partial(
            nearby_kernel, groups=DILATION_RATE, group_rows=group_rows, factor=factor
        ),
        grid=(half,),
        in_specs=head_pairs + [bias_block],
        out_specs=head_pairs[0],
        out_shape=jax.ShapeDtypeStruct((2, half * head_size, rows), jnp.bfloat16),
        scratch_shapes=[pltpu.VMEM((2, rows, head_size + 16), jnp.bfloat16)],
    )(paired, paired, paired, near_bias)

    far_paired = far.reshape(seq_count, 2, 2, half, head_size, group_rows)
    group_block = pl.BlockSpec(
        (2, head_size, group_rows), lambda i: (0, i, i % DILATION_RATE)
    )
    far_block = (seq_count, 1, 2, 1, head_size, group_rows)
    attended_t = pl.pallas_call(
        functools.partial(dilated_kernel, factor=factor),
        grid=(half,),
        in_specs=[
            pl.BlockSpec((2, head_size, group_rows), lambda i: (0, i, i % DILATION_RATE)),
            pl.BlockSpec((2, head_size, rows), lambda i: (1, i, 0)),
            pl.BlockSpec((2, head_size, rows), lambda i: (2, i, 0)),
            bias_block,
            pl.BlockSpec(far_block, lambda i: (0, 0, 0, i, 0, 0)),
            pl.BlockSpec(far_block, lambda i: (0, 1, 0, i, 0, 0)),
            pl.BlockSpec((1, 16, far_count), lambda i: (i, 0, 0)),
            pl.BlockSpec(memory_space=pl.ANY),
        ],
        out_specs=group_block,
        out_shape=jax.ShapeDtypeStruct((2, half * head_size, rows), jnp.bfloat16),
        input_output_aliases={7: 0},
    )(
        paired, paired, paired, near_bias, far_paired, far_paired, far_bias,
        nearby,
    ).reshape(width, rows)

    output = lax.dot_general(
        attended_t, out_weight, (((0,), (0,)), ((), ())), preferred_element_type=jnp.float32
    ) + features.astype(jnp.float32)
    output = jnp.where(position_ok[:, None], output, 0.0).astype(jnp.bfloat16)
    output = output.reshape(DILATION_RATE, group_rows, width).transpose(1, 0, 2)
    return output.reshape(1, rows, width)


def solution(mesh):
    return jax.shard_map(
        body,
        mesh=mesh,
        in_specs=(P(("tile", "seq"), None), P(("tile", "seq")), P("tile"), P(), P(), P(), P()),
        out_specs=P("tile", "seq", None),
        check_vma=False,
    )
```

```python
import functools

import jax
import jax.numpy as jnp
from jax import lax
from jax.experimental import pallas as pl
from jax.experimental.pallas import tpu as pltpu
from jax.sharding import PartitionSpec as P

HEAD_COUNT = 16
QUERY_BLOCK = 1024
PASS1 = 1024
PASS2 = 512
DILATION_RATE = 8


big_negative = -1e30
norm_epsilon = 1e-05


def normalize(features, gain):
    wide = features.astype(jnp.float32)
    average = jnp.mean(wide, axis=-1, keepdims=True)
    centered = wide - average
    spread = jnp.mean(centered * centered, axis=-1, keepdims=True)
    return (centered * lax.rsqrt(spread + norm_epsilon) * gain).astype(jnp.bfloat16)


def extend(block, extra):
    return jnp.concatenate([block, extra], axis=0)


def ones_row(width):
    row = lax.broadcasted_iota(jnp.int32, (16, width), 0)
    return jnp.where(row == 0, 1.0, 0.0).astype(jnp.bfloat16)


def nearby_kernel(*refs, groups, group_rows, factor):
    *query_refs, kt_ref, vt_ref, bias_ref, o_ref, keys_ref = refs
    keys_ref[...] = extend(kt_ref[...], bias_ref[...]).T
    key_count = keys_ref.shape[0]
    width = (groups - 1) * group_rows
    queries_t = extend(
        jnp.concatenate([ref[...] for ref in query_refs], axis=1), ones_row(width)
    )
    top = None
    for first in range(0, key_count, PASS1):
        scores_t = jnp.dot(
            keys_ref[pl.ds(first, PASS1), :], queries_t, preferred_element_type=jnp.float32
        )
        part = jnp.max(scores_t, axis=0, keepdims=True)
        top = part if top is None else jnp.maximum(top, part)
    total = None
    summed_t = None
    for first in range(0, key_count, PASS2):
        scores_t = jnp.dot(
            keys_ref[pl.ds(first, PASS2), :], queries_t, preferred_element_type=jnp.float32
        )
        weights_t = jnp.exp2((scores_t - top) * factor)
        part = jnp.sum(weights_t, axis=0, keepdims=True)
        step = jnp.dot(
            vt_ref[:, pl.ds(first, PASS2)],
            weights_t.astype(jnp.bfloat16),
            preferred_element_type=jnp.float32,
        )
        total = part if total is None else total + part
        summed_t = step if summed_t is None else summed_t + step
    o_ref[:, pl.ds(0, width)] = (summed_t / total).astype(o_ref.dtype)


def joined(ref, pair):
    return jnp.concatenate([ref[chunk, 0, pair, 0] for chunk in range(ref.shape[0])], axis=1)


def dilated_kernel(
    qt_ref, kt_ref, vt_ref, bias_ref, fk_ref, fv_ref, fbias_ref, prev_ref, o_ref, *, factor
):
    del prev_ref
    for pair in range(2):
        queries_t = extend(qt_ref[pair], ones_row(qt_ref.shape[2]))
        near_keys = extend(kt_ref[pair], bias_ref[...]).T
        far_keys = extend(joined(fk_ref, pair), fbias_ref[0]).T
        near = jnp.dot(near_keys, queries_t, preferred_element_type=jnp.float32)
        far = jnp.dot(far_keys, queries_t, preferred_element_type=jnp.float32)
        top = jnp.maximum(
            jnp.max(near, axis=0, keepdims=True), jnp.max(far, axis=0, keepdims=True)
        )
        near_w = jnp.exp2((near - top) * factor)
        far_w = jnp.exp2((far - top) * factor)
        total = jnp.sum(near_w, axis=0, keepdims=True) + jnp.sum(far_w, axis=0, keepdims=True)
        summed_t = jnp.dot(
            vt_ref[pair], near_w.astype(jnp.bfloat16), preferred_element_type=jnp.float32
        )
        summed_t = summed_t + jnp.dot(
            joined(fv_ref, pair), far_w.astype(jnp.bfloat16), preferred_element_type=jnp.float32
        )
        o_ref[pair] = (summed_t / total).astype(o_ref.dtype)


def body(embeddings, slot, lengths, in_weight, norm_gain, qkv_weight, out_weight):
    seq_count = lax.axis_size("seq")
    device_count = lax.axis_size("tile") * seq_count
    rows = embeddings.shape[0]
    block_rows = rows // device_count
    width = in_weight.shape[1]
    head_size = width // HEAD_COUNT
    group_rows = rows // DILATION_RATE
    far_count = group_rows * seq_count
    scale = head_size ** (-0.5)
    my_index = lax.axis_index("tile") * seq_count + lax.axis_index("seq")

    projected = jnp.dot(embeddings, in_weight, preferred_element_type=jnp.float32).astype(
        jnp.bfloat16
    )
    arrived = lax.all_to_all(
        projected.reshape(device_count, block_rows, width),
        ("tile", "seq"),
        split_axis=0,
        concat_axis=0,
        tiled=True,
    ).reshape(rows, width)
    arrived_slot = lax.all_to_all(
        slot.reshape(device_count, block_rows), ("tile", "seq"), split_axis=0, concat_axis=0, tiled=True
    ).reshape(rows)
    local_slot = arrived_slot - my_index * rows
    stored_slot = (local_slot % DILATION_RATE) * group_rows + local_slot // DILATION_RATE
    placement = (
        stored_slot[None, :] == jnp.arange(rows, dtype=jnp.int32)[:, None]
    ).astype(jnp.bfloat16)
    features = jnp.dot(placement, arrived, preferred_element_type=jnp.float32).astype(
        jnp.bfloat16
    )

    slide_length = lengths[0]
    stored = jnp.arange(rows, dtype=jnp.int32)
    local_position = (stored % group_rows) * DILATION_RATE + stored // group_rows
    position_ok = lax.axis_index("seq") * rows + local_position < slide_length
    extra_row = lax.broadcasted_iota(jnp.int32, (16, 1), 0) == 0
    near_bias = jnp.where(
        extra_row & ~position_ok[None, :], big_negative, 0.0
    ).astype(jnp.bfloat16)

    normed = normalize(features, norm_gain)
    projected_t = lax.dot_general(
        qkv_weight, normed, (((0,), (1,)), ((), ())), preferred_element_type=jnp.float32
    ).astype(jnp.bfloat16)

    offsets = [head % DILATION_RATE for head in range(HEAD_COUNT)]
    half = HEAD_COUNT // 2
    grouped = normed.reshape(DILATION_RATE, group_rows, width)
    own_far = jnp.stack(
        [
            jnp.einsum(
                "ljc,chld->hldj",
                grouped,
                qkv_weight[:, part * width : (part + 1) * width].reshape(
                    width, HEAD_COUNT // DILATION_RATE, DILATION_RATE, head_size
                ),
                preferred_element_type=jnp.float32,
            )
            .astype(jnp.bfloat16)
            .reshape(HEAD_COUNT, head_size, group_rows)
            for part in (1, 2)
        ]
    )
    far = lax.all_to_all(
        jnp.broadcast_to(own_far[None], (seq_count,) + own_far.shape),
        "seq",
        split_axis=0,
        concat_axis=0,
        tiled=True,
    )
    far_position = (
        jnp.arange(far_count, dtype=jnp.int32)[None, :] * DILATION_RATE
        + jnp.asarray(offsets, jnp.int32)[:, None]
    )
    far_bias = jnp.where(
        extra_row[None] & (far_position >= slide_length)[:, None, :], big_negative, 0.0
    ).astype(jnp.bfloat16)

    query_block = pl.BlockSpec((head_size, rows), lambda h: (h, 0))
    keys_block = pl.BlockSpec((head_size, rows), lambda h: (HEAD_COUNT + h, 0))
    values_block = pl.BlockSpec((head_size, rows), lambda h: (2 * HEAD_COUNT + h, 0))
    bias_block = pl.BlockSpec((16, rows), lambda h: (0, 0))
    factor = scale * 1.4426950408889634
    nearby = pl.pallas_call(
        functools.partial(
            nearby_kernel, groups=DILATION_RATE, group_rows=group_rows, factor=factor
        ),
        grid=(HEAD_COUNT,),
        in_specs=[
            pl.BlockSpec(
                (head_size, group_rows),
                lambda h, t=t: (h, (h % DILATION_RATE + 1 + t) % DILATION_RATE),
            )
            for t in range(DILATION_RATE - 1)
        ]
        + [keys_block, values_block, bias_block],
        out_specs=query_block,
        out_shape=jax.ShapeDtypeStruct((width, rows), jnp.bfloat16),
        scratch_shapes=[pltpu.VMEM((rows, head_size + 16), jnp.bfloat16)],
    )(*([projected_t] * (DILATION_RATE - 1)), projected_t, projected_t, near_bias)

    paired = projected_t.reshape(6, half * head_size, rows)
    far_paired = far.reshape(seq_count, 2, 2, half, head_size, group_rows)
    group_block = pl.BlockSpec((2, head_size, group_rows), lambda i: (0, i, DILATION_RATE - 1))
    far_block = (seq_count, 1, 2, 1, head_size, group_rows)
    attended_t = pl.pallas_call(
        functools.partial(dilated_kernel, factor=factor),
        grid=(half,),
        in_specs=[
            pl.BlockSpec((2, head_size, group_rows), lambda i: (0, i, i % DILATION_RATE)),
            pl.BlockSpec((2, head_size, rows), lambda i: (1, i, 0)),
            pl.BlockSpec((2, head_size, rows), lambda i: (2, i, 0)),
            bias_block,
            pl.BlockSpec(far_block, lambda i: (0, 0, 0, i, 0, 0)),
            pl.BlockSpec(far_block, lambda i: (0, 1, 0, i, 0, 0)),
            pl.BlockSpec((1, 16, far_count), lambda i: (i, 0, 0)),
            pl.BlockSpec(memory_space=pl.ANY),
        ],
        out_specs=group_block,
        out_shape=jax.ShapeDtypeStruct((2, half * head_size, rows), jnp.bfloat16),
        input_output_aliases={7: 0},
    )(
        paired, paired, paired, near_bias, far_paired, far_paired, far_bias,
        nearby.reshape(2, half * head_size, rows),
    ).reshape(width, rows)
    attended_t = jnp.concatenate(
        [
            jnp.roll(
                attended_t[h * head_size : (h + 1) * head_size], (o + 1) * group_rows, axis=1
            )
            for h, o in enumerate(offsets)
        ]
    )

    output = lax.dot_general(
        attended_t, out_weight, (((0,), (0,)), ((), ())), preferred_element_type=jnp.float32
    ) + features.astype(jnp.float32)
    output = jnp.where(position_ok[:, None], output, 0.0).astype(jnp.bfloat16)
    output = output.reshape(DILATION_RATE, group_rows, width).transpose(1, 0, 2)
    return output.reshape(1, rows, width)


def solution(mesh):
    return jax.shard_map(
        body,
        mesh=mesh,
        in_specs=(P(("tile", "seq"), None), P(("tile", "seq")), P("tile"), P(), P(), P(), P()),
        out_specs=P("tile", "seq", None),
        check_vma=False,
    )
```

```python
import functools

import jax
import jax.numpy as jnp
from jax import lax
from jax.experimental import pallas as pl
from jax.experimental.pallas import tpu as pltpu
from jax.sharding import PartitionSpec as P

HEAD_COUNT = 16
QUERY_BLOCK = 1024
PASS1 = 1024
PASS2 = 512
DILATION_RATE = 8


big_negative = -1e30
norm_epsilon = 1e-05


def normalize(features, gain):
    wide = features.astype(jnp.float32)
    average = jnp.mean(wide, axis=-1, keepdims=True)
    centered = wide - average
    spread = jnp.mean(centered * centered, axis=-1, keepdims=True)
    return (centered * lax.rsqrt(spread + norm_epsilon) * gain).astype(jnp.bfloat16)


def extend(block, extra):
    return jnp.concatenate([block, extra], axis=0)


def ones_row(width):
    row = lax.broadcasted_iota(jnp.int32, (16, width), 0)
    return jnp.where(row == 0, 1.0, 0.0).astype(jnp.bfloat16)


def nearby_kernel(
    qt_ref, kt_ref, vt_ref, bias_ref, o_ref, keys_ref, *, groups, group_rows, factor
):
    keys_ref[...] = extend(kt_ref[...], bias_ref[...]).T
    key_count = keys_ref.shape[0]
    block = QUERY_BLOCK
    ones = ones_row(block)
    for first_row in range(0, groups * group_rows, block):
        rows = pl.ds(first_row, block)
        queries_t = extend(qt_ref[:, rows], ones)
        if PASS1 >= key_count and PASS2 >= key_count:
            scores_t = jnp.dot(keys_ref[...], queries_t, preferred_element_type=jnp.float32)
            top = jnp.max(scores_t, axis=0, keepdims=True)
            weights_t = jnp.exp2((scores_t - top) * factor)
            total = jnp.sum(weights_t, axis=0, keepdims=True)
            summed_t = jnp.dot(
                vt_ref[...], weights_t.astype(jnp.bfloat16), preferred_element_type=jnp.float32
            )
        else:
            top = None
            for first in range(0, key_count, PASS1):
                scores_t = jnp.dot(
                    keys_ref[pl.ds(first, PASS1), :], queries_t, preferred_element_type=jnp.float32
                )
                part = jnp.max(scores_t, axis=0, keepdims=True)
                top = part if top is None else jnp.maximum(top, part)
            total = None
            summed_t = None
            for first in range(0, key_count, PASS2):
                scores_t = jnp.dot(
                    keys_ref[pl.ds(first, PASS2), :], queries_t, preferred_element_type=jnp.float32
                )
                weights_t = jnp.exp2((scores_t - top) * factor)
                part = jnp.sum(weights_t, axis=0, keepdims=True)
                step = jnp.dot(
                    vt_ref[:, pl.ds(first, PASS2)],
                    weights_t.astype(jnp.bfloat16),
                    preferred_element_type=jnp.float32,
                )
                total = part if total is None else total + part
                summed_t = step if summed_t is None else summed_t + step
        o_ref[:, rows] = (summed_t / total).astype(o_ref.dtype)


def joined(ref, pair):
    return jnp.concatenate([ref[chunk, 0, pair, 0] for chunk in range(ref.shape[0])], axis=1)


def dilated_kernel(
    qt_ref, kt_ref, vt_ref, bias_ref, fk_ref, fv_ref, fbias_ref, prev_ref, o_ref, *, factor
):
    del prev_ref
    for pair in range(2):
        queries_t = extend(qt_ref[pair], ones_row(qt_ref.shape[2]))
        near_keys = extend(kt_ref[pair], bias_ref[...]).T
        far_keys = extend(joined(fk_ref, pair), fbias_ref[0]).T
        near = jnp.dot(near_keys, queries_t, preferred_element_type=jnp.float32)
        far = jnp.dot(far_keys, queries_t, preferred_element_type=jnp.float32)
        top = jnp.maximum(
            jnp.max(near, axis=0, keepdims=True), jnp.max(far, axis=0, keepdims=True)
        )
        near_w = jnp.exp2((near - top) * factor)
        far_w = jnp.exp2((far - top) * factor)
        total = jnp.sum(near_w, axis=0, keepdims=True) + jnp.sum(far_w, axis=0, keepdims=True)
        summed_t = jnp.dot(
            vt_ref[pair], near_w.astype(jnp.bfloat16), preferred_element_type=jnp.float32
        )
        summed_t = summed_t + jnp.dot(
            joined(fv_ref, pair), far_w.astype(jnp.bfloat16), preferred_element_type=jnp.float32
        )
        o_ref[pair] = (summed_t / total).astype(o_ref.dtype)


def body(embeddings, slot, lengths, in_weight, norm_gain, qkv_weight, out_weight):
    seq_count = lax.axis_size("seq")
    device_count = lax.axis_size("tile") * seq_count
    rows = embeddings.shape[0]
    block_rows = rows // device_count
    width = in_weight.shape[1]
    head_size = width // HEAD_COUNT
    group_rows = rows // DILATION_RATE
    far_count = group_rows * seq_count
    scale = head_size ** (-0.5)
    my_index = lax.axis_index("tile") * seq_count + lax.axis_index("seq")

    projected = jnp.dot(embeddings, in_weight, preferred_element_type=jnp.float32).astype(
        jnp.bfloat16
    )
    destination = jnp.arange(rows, dtype=jnp.int32) // block_rows
    own_slot = slot - destination * rows
    digits = jnp.stack([own_slot // 32, own_slot % 32], axis=1).astype(jnp.bfloat16)
    sent = jnp.concatenate([projected, jnp.pad(digits, ((0, 0), (0, 126)))], axis=1)
    received = lax.all_to_all(
        sent.reshape(device_count, block_rows, width + 128),
        ("tile", "seq"),
        split_axis=0,
        concat_axis=0,
        tiled=True,
    ).reshape(rows, width + 128)
    arrived = received[:, :width]
    local_slot = (
        received[:, width].astype(jnp.int32) * 32 + received[:, width + 1].astype(jnp.int32)
    )
    stored_slot = (local_slot % DILATION_RATE) * group_rows + local_slot // DILATION_RATE
    placement = (
        stored_slot[None, :] == jnp.arange(rows, dtype=jnp.int32)[:, None]
    ).astype(jnp.bfloat16)
    features = jnp.dot(placement, arrived, preferred_element_type=jnp.float32).astype(
        jnp.bfloat16
    )

    slide_length = lengths[0]
    stored = jnp.arange(rows, dtype=jnp.int32)
    local_position = (stored % group_rows) * DILATION_RATE + stored // group_rows
    position_ok = lax.axis_index("seq") * rows + local_position < slide_length
    extra_row = lax.broadcasted_iota(jnp.int32, (16, 1), 0) == 0
    near_bias = jnp.where(
        extra_row & ~position_ok[None, :], big_negative, 0.0
    ).astype(jnp.bfloat16)

    normed = normalize(features, norm_gain)
    projected_t = lax.dot_general(
        qkv_weight, normed, (((0,), (1,)), ((), ())), preferred_element_type=jnp.float32
    ).astype(jnp.bfloat16)

    offsets = [head % DILATION_RATE for head in range(HEAD_COUNT)]
    half = HEAD_COUNT // 2
    grouped = normed.reshape(DILATION_RATE, group_rows, width)
    own_far = jnp.stack(
        [
            jnp.einsum(
                "ljc,chld->hldj",
                grouped,
                qkv_weight[:, part * width : (part + 1) * width].reshape(
                    width, HEAD_COUNT // DILATION_RATE, DILATION_RATE, head_size
                ),
                preferred_element_type=jnp.float32,
            )
            .astype(jnp.bfloat16)
            .reshape(HEAD_COUNT, head_size, group_rows)
            for part in (1, 2)
        ]
    )
    far = lax.all_to_all(
        jnp.broadcast_to(own_far[None], (seq_count,) + own_far.shape),
        "seq",
        split_axis=0,
        concat_axis=0,
        tiled=True,
    )
    far_position = (
        jnp.arange(far_count, dtype=jnp.int32)[None, :] * DILATION_RATE
        + jnp.asarray(offsets, jnp.int32)[:, None]
    )
    far_bias = jnp.where(
        extra_row[None] & (far_position >= slide_length)[:, None, :], big_negative, 0.0
    ).astype(jnp.bfloat16)

    query_block = pl.BlockSpec((head_size, rows), lambda h: (h, 0))
    keys_block = pl.BlockSpec((head_size, rows), lambda h: (HEAD_COUNT + h, 0))
    values_block = pl.BlockSpec((head_size, rows), lambda h: (2 * HEAD_COUNT + h, 0))
    bias_block = pl.BlockSpec((16, rows), lambda h: (0, 0))
    factor = scale * 1.4426950408889634
    nearby = pl.pallas_call(
        functools.partial(
            nearby_kernel, groups=DILATION_RATE, group_rows=group_rows, factor=factor
        ),
        grid=(HEAD_COUNT,),
        in_specs=[query_block, keys_block, values_block, bias_block],
        out_specs=query_block,
        out_shape=jax.ShapeDtypeStruct((width, rows), jnp.bfloat16),
        scratch_shapes=[pltpu.VMEM((rows, head_size + 16), jnp.bfloat16)],
    )(projected_t, projected_t, projected_t, near_bias)

    paired = projected_t.reshape(6, half * head_size, rows)
    far_paired = far.reshape(seq_count, 2, 2, half, head_size, group_rows)
    group_block = pl.BlockSpec(
        (2, head_size, group_rows), lambda i: (0, i, i % DILATION_RATE)
    )
    far_block = (seq_count, 1, 2, 1, head_size, group_rows)
    attended_t = pl.pallas_call(
        functools.partial(dilated_kernel, factor=factor),
        grid=(half,),
        in_specs=[
            pl.BlockSpec((2, head_size, group_rows), lambda i: (0, i, i % DILATION_RATE)),
            pl.BlockSpec((2, head_size, rows), lambda i: (1, i, 0)),
            pl.BlockSpec((2, head_size, rows), lambda i: (2, i, 0)),
            bias_block,
            pl.BlockSpec(far_block, lambda i: (0, 0, 0, i, 0, 0)),
            pl.BlockSpec(far_block, lambda i: (0, 1, 0, i, 0, 0)),
            pl.BlockSpec((1, 16, far_count), lambda i: (i, 0, 0)),
            pl.BlockSpec(memory_space=pl.ANY),
        ],
        out_specs=group_block,
        out_shape=jax.ShapeDtypeStruct((2, half * head_size, rows), jnp.bfloat16),
        input_output_aliases={7: 0},
    )(
        paired, paired, paired, near_bias, far_paired, far_paired, far_bias,
        nearby.reshape(2, half * head_size, rows),
    ).reshape(width, rows)

    output = lax.dot_general(
        attended_t, out_weight, (((0,), (0,)), ((), ())), preferred_element_type=jnp.float32
    ) + features.astype(jnp.float32)
    output = jnp.where(position_ok[:, None], output, 0.0).astype(jnp.bfloat16)
    output = output.reshape(DILATION_RATE, group_rows, width).transpose(1, 0, 2)
    return output.reshape(1, rows, width)


def solution(mesh):
    return jax.shard_map(
        body,
        mesh=mesh,
        in_specs=(P(("tile", "seq"), None), P(("tile", "seq")), P("tile"), P(), P(), P(), P()),
        out_specs=P("tile", "seq", None),
        check_vma=False,
    )
```

```python
import functools

import jax
import jax.numpy as jnp
from jax import lax
from jax.experimental import pallas as pl
from jax.experimental.pallas import tpu as pltpu
from jax.sharding import PartitionSpec as P

HEAD_COUNT = 16
QUERY_BLOCK = 1024
PASS1 = 1024
PASS2 = 512
DILATION_RATE = 8


big_negative = -1e30
norm_epsilon = 1e-05


def normalize(features, gain):
    wide = features.astype(jnp.float32)
    average = jnp.mean(wide, axis=-1, keepdims=True)
    centered = wide - average
    spread = jnp.mean(centered * centered, axis=-1, keepdims=True)
    return (centered * lax.rsqrt(spread + norm_epsilon) * gain).astype(jnp.bfloat16)


def extend(block, extra):
    return jnp.concatenate([block, extra], axis=0)


def ones_row(width):
    row = lax.broadcasted_iota(jnp.int32, (16, width), 0)
    return jnp.where(row == 0, 1.0, 0.0).astype(jnp.bfloat16)


def nearby_kernel(
    qa_ref, qb_ref, ka_ref, kb_ref, va_ref, vb_ref, bias_ref, o_ref, keys_ref,
    *, groups, group_rows, factor
):
    key_count = keys_ref.shape[1]
    block = QUERY_BLOCK
    ones = ones_row(block)
    heads = ((qa_ref, ka_ref, va_ref), (qb_ref, kb_ref, vb_ref))
    for pair, (_, kt_ref, _) in enumerate(heads):
        keys_ref[pair] = extend(kt_ref[...], bias_ref[...]).T
    for pair, (qt_ref, _, vt_ref) in enumerate(heads):
        for first_row in range(0, groups * group_rows, block):
            rows = pl.ds(first_row, block)
            queries_t = extend(qt_ref[:, rows], ones)
            top = None
            for first in range(0, key_count, PASS1):
                scores_t = jnp.dot(
                    keys_ref[pair, pl.ds(first, PASS1), :],
                    queries_t,
                    preferred_element_type=jnp.float32,
                )
                part = jnp.max(scores_t, axis=0, keepdims=True)
                top = part if top is None else jnp.maximum(top, part)
            total = None
            summed_t = None
            for first in range(0, key_count, PASS2):
                scores_t = jnp.dot(
                    keys_ref[pair, pl.ds(first, PASS2), :],
                    queries_t,
                    preferred_element_type=jnp.float32,
                )
                weights_t = jnp.exp2((scores_t - top) * factor)
                part = jnp.sum(weights_t, axis=0, keepdims=True)
                step = jnp.dot(
                    vt_ref[:, pl.ds(first, PASS2)],
                    weights_t.astype(jnp.bfloat16),
                    preferred_element_type=jnp.float32,
                )
                total = part if total is None else total + part
                summed_t = step if summed_t is None else summed_t + step
            o_ref[pair, :, rows] = (summed_t / total).astype(o_ref.dtype)


def joined(ref, pair):
    return jnp.concatenate([ref[chunk, 0, pair, 0] for chunk in range(ref.shape[0])], axis=1)


def dilated_kernel(
    qt_ref, kt_ref, vt_ref, bias_ref, fk_ref, fv_ref, fbias_ref, prev_ref, o_ref, *, factor
):
    del prev_ref
    for pair in range(2):
        queries_t = extend(qt_ref[pair], ones_row(qt_ref.shape[2]))
        near_keys = extend(kt_ref[pair], bias_ref[...]).T
        far_keys = extend(joined(fk_ref, pair), fbias_ref[0]).T
        near = jnp.dot(near_keys, queries_t, preferred_element_type=jnp.float32)
        far = jnp.dot(far_keys, queries_t, preferred_element_type=jnp.float32)
        top = jnp.maximum(
            jnp.max(near, axis=0, keepdims=True), jnp.max(far, axis=0, keepdims=True)
        )
        near_w = jnp.exp2((near - top) * factor)
        far_w = jnp.exp2((far - top) * factor)
        total = jnp.sum(near_w, axis=0, keepdims=True) + jnp.sum(far_w, axis=0, keepdims=True)
        summed_t = jnp.dot(
            vt_ref[pair], near_w.astype(jnp.bfloat16), preferred_element_type=jnp.float32
        )
        summed_t = summed_t + jnp.dot(
            joined(fv_ref, pair), far_w.astype(jnp.bfloat16), preferred_element_type=jnp.float32
        )
        o_ref[pair] = (summed_t / total).astype(o_ref.dtype)


def body(embeddings, slot, lengths, in_weight, norm_gain, qkv_weight, out_weight):
    seq_count = lax.axis_size("seq")
    device_count = lax.axis_size("tile") * seq_count
    rows = embeddings.shape[0]
    block_rows = rows // device_count
    width = in_weight.shape[1]
    head_size = width // HEAD_COUNT
    group_rows = rows // DILATION_RATE
    far_count = group_rows * seq_count
    scale = head_size ** (-0.5)
    my_index = lax.axis_index("tile") * seq_count + lax.axis_index("seq")

    projected = jnp.dot(embeddings, in_weight, preferred_element_type=jnp.float32).astype(
        jnp.bfloat16
    )
    arrived = lax.all_to_all(
        projected.reshape(device_count, block_rows, width),
        ("tile", "seq"),
        split_axis=0,
        concat_axis=0,
        tiled=True,
    ).reshape(rows, width)
    arrived_slot = lax.all_to_all(
        slot.reshape(device_count, block_rows), ("tile", "seq"), split_axis=0, concat_axis=0, tiled=True
    ).reshape(rows)
    local_slot = arrived_slot - my_index * rows
    stored_slot = (local_slot % DILATION_RATE) * group_rows + local_slot // DILATION_RATE
    placement = (
        stored_slot[None, :] == jnp.arange(rows, dtype=jnp.int32)[:, None]
    ).astype(jnp.bfloat16)
    features = jnp.dot(placement, arrived, preferred_element_type=jnp.float32).astype(
        jnp.bfloat16
    )

    slide_length = lengths[0]
    stored = jnp.arange(rows, dtype=jnp.int32)
    local_position = (stored % group_rows) * DILATION_RATE + stored // group_rows
    position_ok = lax.axis_index("seq") * rows + local_position < slide_length
    extra_row = lax.broadcasted_iota(jnp.int32, (16, 1), 0) == 0
    near_bias = jnp.where(
        extra_row & ~position_ok[None, :], big_negative, 0.0
    ).astype(jnp.bfloat16)

    normed = normalize(features, norm_gain)
    projected_t = lax.dot_general(
        qkv_weight, normed, (((0,), (1,)), ((), ())), preferred_element_type=jnp.float32
    ).astype(jnp.bfloat16)

    offsets = [head % DILATION_RATE for head in range(HEAD_COUNT)]
    half = HEAD_COUNT // 2
    grouped = normed.reshape(DILATION_RATE, group_rows, width)
    own_far = jnp.stack(
        [
            jnp.einsum(
                "ljc,chld->hldj",
                grouped,
                qkv_weight[:, part * width : (part + 1) * width].reshape(
                    width, HEAD_COUNT // DILATION_RATE, DILATION_RATE, head_size
                ),
                preferred_element_type=jnp.float32,
            )
            .astype(jnp.bfloat16)
            .reshape(HEAD_COUNT, head_size, group_rows)
            for part in (1, 2)
        ]
    )
    far = lax.all_to_all(
        jnp.broadcast_to(own_far[None], (seq_count,) + own_far.shape),
        "seq",
        split_axis=0,
        concat_axis=0,
        tiled=True,
    )
    far_position = (
        jnp.arange(far_count, dtype=jnp.int32)[None, :] * DILATION_RATE
        + jnp.asarray(offsets, jnp.int32)[:, None]
    )
    far_bias = jnp.where(
        extra_row[None] & (far_position >= slide_length)[:, None, :], big_negative, 0.0
    ).astype(jnp.bfloat16)

    query_block = pl.BlockSpec((head_size, rows), lambda h: (h, 0))
    keys_block = pl.BlockSpec((head_size, rows), lambda h: (HEAD_COUNT + h, 0))
    values_block = pl.BlockSpec((head_size, rows), lambda h: (2 * HEAD_COUNT + h, 0))
    bias_block = pl.BlockSpec((16, rows), lambda h: (0, 0))
    factor = scale * 1.4426950408889634
    half = HEAD_COUNT // 2
    nearby = pl.pallas_call(
        functools.partial(
            nearby_kernel, groups=DILATION_RATE, group_rows=group_rows, factor=factor
        ),
        grid=(half,),
        in_specs=[
            pl.BlockSpec((head_size, rows), lambda i, first=first: (first + i, 0))
            for first in range(0, 3 * HEAD_COUNT, half)
        ]
        + [pl.BlockSpec((16, rows), lambda i: (0, 0))],
        out_specs=pl.BlockSpec((2, head_size, rows), lambda i: (0, i, 0)),
        out_shape=jax.ShapeDtypeStruct((2, half * head_size, rows), jnp.bfloat16),
        scratch_shapes=[pltpu.VMEM((2, rows, head_size + 16), jnp.bfloat16)],
    )(*([projected_t] * 6), near_bias)

    paired = projected_t.reshape(6, half * head_size, rows)
    far_paired = far.reshape(seq_count, 2, 2, half, head_size, group_rows)
    group_block = pl.BlockSpec(
        (2, head_size, group_rows), lambda i: (0, i, i % DILATION_RATE)
    )
    far_block = (seq_count, 1, 2, 1, head_size, group_rows)
    attended_t = pl.pallas_call(
        functools.partial(dilated_kernel, factor=factor),
        grid=(half,),
        in_specs=[
            pl.BlockSpec((2, head_size, group_rows), lambda i: (0, i, i % DILATION_RATE)),
            pl.BlockSpec((2, head_size, rows), lambda i: (1, i, 0)),
            pl.BlockSpec((2, head_size, rows), lambda i: (2, i, 0)),
            bias_block,
            pl.BlockSpec(far_block, lambda i: (0, 0, 0, i, 0, 0)),
            pl.BlockSpec(far_block, lambda i: (0, 1, 0, i, 0, 0)),
            pl.BlockSpec((1, 16, far_count), lambda i: (i, 0, 0)),
            pl.BlockSpec(memory_space=pl.ANY),
        ],
        out_specs=group_block,
        out_shape=jax.ShapeDtypeStruct((2, half * head_size, rows), jnp.bfloat16),
        input_output_aliases={7: 0},
    )(
        paired, paired, paired, near_bias, far_paired, far_paired, far_bias,
        nearby,
    ).reshape(width, rows)

    output = lax.dot_general(
        attended_t, out_weight, (((0,), (0,)), ((), ())), preferred_element_type=jnp.float32
    ) + features.astype(jnp.float32)
    output = jnp.where(position_ok[:, None], output, 0.0).astype(jnp.bfloat16)
    output = output.reshape(DILATION_RATE, group_rows, width).transpose(1, 0, 2)
    return output.reshape(1, rows, width)


def solution(mesh):
    return jax.shard_map(
        body,
        mesh=mesh,
        in_specs=(P(("tile", "seq"), None), P(("tile", "seq")), P("tile"), P(), P(), P(), P()),
        out_specs=P("tile", "seq", None),
        check_vma=False,
    )
```

```python
import functools

import jax
import jax.numpy as jnp
from jax import lax
from jax.experimental import pallas as pl
from jax.experimental.pallas import tpu as pltpu
from jax.sharding import PartitionSpec as P

HEAD_COUNT = 16
QUERY_BLOCK = 1024
PASS1 = 512
PASS2 = 512
DILATION_RATE = 8


big_negative = -1e30
norm_epsilon = 1e-05


def normalize(features, gain):
    wide = features.astype(jnp.float32)
    average = jnp.mean(wide, axis=-1, keepdims=True)
    centered = wide - average
    spread = jnp.mean(centered * centered, axis=-1, keepdims=True)
    return (centered * lax.rsqrt(spread + norm_epsilon) * gain).astype(jnp.bfloat16)


def extend(block, extra):
    return jnp.concatenate([block, extra], axis=0)


def ones_row(width):
    row = lax.broadcasted_iota(jnp.int32, (16, width), 0)
    return jnp.where(row == 0, 1.0, 0.0).astype(jnp.bfloat16)


def nearby_kernel(
    qa_ref, qb_ref, ka_ref, kb_ref, va_ref, vb_ref, bias_ref, o_ref, keys_ref,
    *, groups, group_rows, factor
):
    key_count = keys_ref.shape[1]
    block = QUERY_BLOCK
    ones = ones_row(block)
    heads = ((qa_ref, ka_ref, va_ref), (qb_ref, kb_ref, vb_ref))
    for pair, (_, kt_ref, _) in enumerate(heads):
        keys_ref[pair] = extend(kt_ref[...], bias_ref[...]).T
    for pair, (qt_ref, _, vt_ref) in enumerate(heads):
        for first_row in range(0, groups * group_rows, block):
            rows = pl.ds(first_row, block)
            queries_t = extend(qt_ref[:, rows], ones)
            top = None
            for first in range(0, key_count, PASS1):
                scores_t = jnp.dot(
                    keys_ref[pair, pl.ds(first, PASS1), :],
                    queries_t,
                    preferred_element_type=jnp.float32,
                )
                part = jnp.max(scores_t, axis=0, keepdims=True)
                top = part if top is None else jnp.maximum(top, part)
            total = None
            summed_t = None
            for first in range(0, key_count, PASS2):
                scores_t = jnp.dot(
                    keys_ref[pair, pl.ds(first, PASS2), :],
                    queries_t,
                    preferred_element_type=jnp.float32,
                )
                weights_t = jnp.exp2((scores_t - top) * factor)
                part = jnp.sum(weights_t, axis=0, keepdims=True)
                step = jnp.dot(
                    vt_ref[:, pl.ds(first, PASS2)],
                    weights_t.astype(jnp.bfloat16),
                    preferred_element_type=jnp.float32,
                )
                total = part if total is None else total + part
                summed_t = step if summed_t is None else summed_t + step
            o_ref[pair, :, rows] = (summed_t / total).astype(o_ref.dtype)


def joined(ref, pair):
    return jnp.concatenate([ref[chunk, 0, pair, 0] for chunk in range(ref.shape[0])], axis=1)


def dilated_kernel(
    qt_ref, kt_ref, vt_ref, bias_ref, fk_ref, fv_ref, fbias_ref, prev_ref, o_ref, *, factor
):
    del prev_ref
    for pair in range(2):
        queries_t = extend(qt_ref[pair], ones_row(qt_ref.shape[2]))
        near_keys = extend(kt_ref[pair], bias_ref[...]).T
        far_keys = extend(joined(fk_ref, pair), fbias_ref[0]).T
        near = jnp.dot(near_keys, queries_t, preferred_element_type=jnp.float32)
        far = jnp.dot(far_keys, queries_t, preferred_element_type=jnp.float32)
        top = jnp.maximum(
            jnp.max(near, axis=0, keepdims=True), jnp.max(far, axis=0, keepdims=True)
        )
        near_w = jnp.exp2((near - top) * factor)
        far_w = jnp.exp2((far - top) * factor)
        total = jnp.sum(near_w, axis=0, keepdims=True) + jnp.sum(far_w, axis=0, keepdims=True)
        summed_t = jnp.dot(
            vt_ref[pair], near_w.astype(jnp.bfloat16), preferred_element_type=jnp.float32
        )
        summed_t = summed_t + jnp.dot(
            joined(fv_ref, pair), far_w.astype(jnp.bfloat16), preferred_element_type=jnp.float32
        )
        o_ref[pair] = (summed_t / total).astype(o_ref.dtype)


def body(embeddings, slot, lengths, in_weight, norm_gain, qkv_weight, out_weight):
    seq_count = lax.axis_size("seq")
    device_count = lax.axis_size("tile") * seq_count
    rows = embeddings.shape[0]
    block_rows = rows // device_count
    width = in_weight.shape[1]
    head_size = width // HEAD_COUNT
    group_rows = rows // DILATION_RATE
    far_count = group_rows * seq_count
    scale = head_size ** (-0.5)
    my_index = lax.axis_index("tile") * seq_count + lax.axis_index("seq")

    projected = jnp.dot(embeddings, in_weight, preferred_element_type=jnp.float32).astype(
        jnp.bfloat16
    )
    arrived = lax.all_to_all(
        projected.reshape(device_count, block_rows, width),
        ("tile", "seq"),
        split_axis=0,
        concat_axis=0,
        tiled=True,
    ).reshape(rows, width)
    arrived_slot = lax.all_to_all(
        slot.reshape(device_count, block_rows), ("tile", "seq"), split_axis=0, concat_axis=0, tiled=True
    ).reshape(rows)
    local_slot = arrived_slot - my_index * rows
    stored_slot = (local_slot % DILATION_RATE) * group_rows + local_slot // DILATION_RATE
    placement = (
        stored_slot[None, :] == jnp.arange(rows, dtype=jnp.int32)[:, None]
    ).astype(jnp.bfloat16)
    features = jnp.dot(placement, arrived, preferred_element_type=jnp.float32).astype(
        jnp.bfloat16
    )

    slide_length = lengths[0]
    stored = jnp.arange(rows, dtype=jnp.int32)
    local_position = (stored % group_rows) * DILATION_RATE + stored // group_rows
    position_ok = lax.axis_index("seq") * rows + local_position < slide_length
    extra_row = lax.broadcasted_iota(jnp.int32, (16, 1), 0) == 0
    near_bias = jnp.where(
        extra_row & ~position_ok[None, :], big_negative, 0.0
    ).astype(jnp.bfloat16)

    normed = normalize(features, norm_gain)
    projected_t = lax.dot_general(
        qkv_weight, normed, (((0,), (1,)), ((), ())), preferred_element_type=jnp.float32
    ).astype(jnp.bfloat16)

    offsets = [head % DILATION_RATE for head in range(HEAD_COUNT)]
    half = HEAD_COUNT // 2
    grouped = normed.reshape(DILATION_RATE, group_rows, width)
    own_far = jnp.stack(
        [
            jnp.einsum(
                "ljc,chld->hldj",
                grouped,
                qkv_weight[:, part * width : (part + 1) * width].reshape(
                    width, HEAD_COUNT // DILATION_RATE, DILATION_RATE, head_size
                ),
                preferred_element_type=jnp.float32,
            )
            .astype(jnp.bfloat16)
            .reshape(HEAD_COUNT, head_size, group_rows)
            for part in (1, 2)
        ]
    )
    far = lax.all_to_all(
        jnp.broadcast_to(own_far[None], (seq_count,) + own_far.shape),
        "seq",
        split_axis=0,
        concat_axis=0,
        tiled=True,
    )
    far_position = (
        jnp.arange(far_count, dtype=jnp.int32)[None, :] * DILATION_RATE
        + jnp.asarray(offsets, jnp.int32)[:, None]
    )
    far_bias = jnp.where(
        extra_row[None] & (far_position >= slide_length)[:, None, :], big_negative, 0.0
    ).astype(jnp.bfloat16)

    query_block = pl.BlockSpec((head_size, rows), lambda h: (h, 0))
    keys_block = pl.BlockSpec((head_size, rows), lambda h: (HEAD_COUNT + h, 0))
    values_block = pl.BlockSpec((head_size, rows), lambda h: (2 * HEAD_COUNT + h, 0))
    bias_block = pl.BlockSpec((16, rows), lambda h: (0, 0))
    factor = scale * 1.4426950408889634
    half = HEAD_COUNT // 2
    nearby = pl.pallas_call(
        functools.partial(
            nearby_kernel, groups=DILATION_RATE, group_rows=group_rows, factor=factor
        ),
        grid=(half,),
        in_specs=[
            pl.BlockSpec((head_size, rows), lambda i, first=first: (first + i, 0))
            for first in range(0, 3 * HEAD_COUNT, half)
        ]
        + [pl.BlockSpec((16, rows), lambda i: (0, 0))],
        out_specs=pl.BlockSpec((2, head_size, rows), lambda i: (0, i, 0)),
        out_shape=jax.ShapeDtypeStruct((2, half * head_size, rows), jnp.bfloat16),
        scratch_shapes=[pltpu.VMEM((2, rows, head_size + 16), jnp.bfloat16)],
    )(*([projected_t] * 6), near_bias)

    paired = projected_t.reshape(6, half * head_size, rows)
    far_paired = far.reshape(seq_count, 2, 2, half, head_size, group_rows)
    group_block = pl.BlockSpec(
        (2, head_size, group_rows), lambda i: (0, i, i % DILATION_RATE)
    )
    far_block = (seq_count, 1, 2, 1, head_size, group_rows)
    attended_t = pl.pallas_call(
        functools.partial(dilated_kernel, factor=factor),
        grid=(half,),
        in_specs=[
            pl.BlockSpec((2, head_size, group_rows), lambda i: (0, i, i % DILATION_RATE)),
            pl.BlockSpec((2, head_size, rows), lambda i: (1, i, 0)),
            pl.BlockSpec((2, head_size, rows), lambda i: (2, i, 0)),
            bias_block,
            pl.BlockSpec(far_block, lambda i: (0, 0, 0, i, 0, 0)),
            pl.BlockSpec(far_block, lambda i: (0, 1, 0, i, 0, 0)),
            pl.BlockSpec((1, 16, far_count), lambda i: (i, 0, 0)),
            pl.BlockSpec(memory_space=pl.ANY),
        ],
        out_specs=group_block,
        out_shape=jax.ShapeDtypeStruct((2, half * head_size, rows), jnp.bfloat16),
        input_output_aliases={7: 0},
    )(
        paired, paired, paired, near_bias, far_paired, far_paired, far_bias,
        nearby,
    ).reshape(width, rows)

    output = lax.dot_general(
        attended_t, out_weight, (((0,), (0,)), ((), ())), preferred_element_type=jnp.float32
    ) + features.astype(jnp.float32)
    output = jnp.where(position_ok[:, None], output, 0.0).astype(jnp.bfloat16)
    output = output.reshape(DILATION_RATE, group_rows, width).transpose(1, 0, 2)
    return output.reshape(1, rows, width)


def solution(mesh):
    return jax.shard_map(
        body,
        mesh=mesh,
        in_specs=(P(("tile", "seq"), None), P(("tile", "seq")), P("tile"), P(), P(), P(), P()),
        out_specs=P("tile", "seq", None),
        check_vma=False,
    )
```

```python
import functools

import jax
import jax.numpy as jnp
from jax import lax
from jax.experimental import pallas as pl
from jax.experimental.pallas import tpu as pltpu
from jax.sharding import PartitionSpec as P

HEAD_COUNT = 16
QUERY_BLOCK = 1024
PASS1 = 512
PASS2 = 512
DILATION_RATE = 8


big_negative = -1e30
norm_epsilon = 1e-05


def normalize(features, gain):
    wide = features.astype(jnp.float32)
    average = jnp.mean(wide, axis=-1, keepdims=True)
    centered = wide - average
    spread = jnp.mean(centered * centered, axis=-1, keepdims=True)
    return (centered * lax.rsqrt(spread + norm_epsilon) * gain).astype(jnp.bfloat16)


def extend(block, extra):
    return jnp.concatenate([block, extra], axis=0)


def ones_row(width):
    row = lax.broadcasted_iota(jnp.int32, (16, width), 0)
    return jnp.where(row == 0, 1.0, 0.0).astype(jnp.bfloat16)


def mask_rows(limit, width, position_of):
    row = lax.broadcasted_iota(jnp.int32, (16, width), 0)
    lane = lax.broadcasted_iota(jnp.int32, (16, width), 1)
    invalid = (row == 0) & (position_of(lane) >= limit)
    return jnp.where(invalid, big_negative, 0.0).astype(jnp.bfloat16)


def near_mask(limits_ref, rows):
    group_rows = rows // DILATION_RATE
    return mask_rows(
        limits_ref[0],
        rows,
        lambda lane: limits_ref[1] + (lane % group_rows) * DILATION_RATE + lane // group_rows,
    )


def nearby_kernel(
    qa_ref, qb_ref, ka_ref, kb_ref, va_ref, vb_ref, limits_ref, o_ref, keys_ref,
    *, groups, group_rows, factor
):
    key_count = keys_ref.shape[1]
    block = QUERY_BLOCK
    ones = ones_row(block)
    heads = ((qa_ref, ka_ref, va_ref), (qb_ref, kb_ref, vb_ref))
    bias = near_mask(limits_ref, keys_ref.shape[1])
    for pair, (_, kt_ref, _) in enumerate(heads):
        keys_ref[pair] = extend(kt_ref[...], bias).T
    for pair, (qt_ref, _, vt_ref) in enumerate(heads):
        for first_row in range(0, groups * group_rows, block):
            rows = pl.ds(first_row, block)
            queries_t = extend(qt_ref[:, rows], ones)
            top = None
            for first in range(0, key_count, PASS1):
                scores_t = jnp.dot(
                    keys_ref[pair, pl.ds(first, PASS1), :],
                    queries_t,
                    preferred_element_type=jnp.float32,
                )
                part = jnp.max(scores_t, axis=0, keepdims=True)
                top = part if top is None else jnp.maximum(top, part)
            total = None
            summed_t = None
            for first in range(0, key_count, PASS2):
                scores_t = jnp.dot(
                    keys_ref[pair, pl.ds(first, PASS2), :],
                    queries_t,
                    preferred_element_type=jnp.float32,
                )
                weights_t = jnp.exp2((scores_t - top) * factor)
                part = jnp.sum(weights_t, axis=0, keepdims=True)
                step = jnp.dot(
                    vt_ref[:, pl.ds(first, PASS2)],
                    weights_t.astype(jnp.bfloat16),
                    preferred_element_type=jnp.float32,
                )
                total = part if total is None else total + part
                summed_t = step if summed_t is None else summed_t + step
            o_ref[pair, :, rows] = (summed_t / total).astype(o_ref.dtype)


def joined(ref, pair):
    return jnp.concatenate([ref[chunk, 0, pair, 0] for chunk in range(ref.shape[0])], axis=1)


def dilated_kernel(
    qt_ref, kt_ref, vt_ref, limits_ref, fk_ref, fv_ref, prev_ref, o_ref, *, factor
):
    del prev_ref
    offset = pl.program_id(0) % DILATION_RATE
    near_bias = near_mask(limits_ref, kt_ref.shape[2])
    far_bias = mask_rows(
        limits_ref[0],
        fk_ref.shape[0] * fk_ref.shape[5],
        lambda lane: lane * DILATION_RATE + offset,
    )
    for pair in range(2):
        queries_t = extend(qt_ref[pair], ones_row(qt_ref.shape[2]))
        near_keys = extend(kt_ref[pair], near_bias).T
        far_keys = extend(joined(fk_ref, pair), far_bias).T
        near = jnp.dot(near_keys, queries_t, preferred_element_type=jnp.float32)
        far = jnp.dot(far_keys, queries_t, preferred_element_type=jnp.float32)
        top = jnp.maximum(
            jnp.max(near, axis=0, keepdims=True), jnp.max(far, axis=0, keepdims=True)
        )
        near_w = jnp.exp2((near - top) * factor)
        far_w = jnp.exp2((far - top) * factor)
        total = jnp.sum(near_w, axis=0, keepdims=True) + jnp.sum(far_w, axis=0, keepdims=True)
        summed_t = jnp.dot(
            vt_ref[pair], near_w.astype(jnp.bfloat16), preferred_element_type=jnp.float32
        )
        summed_t = summed_t + jnp.dot(
            joined(fv_ref, pair), far_w.astype(jnp.bfloat16), preferred_element_type=jnp.float32
        )
        o_ref[pair] = (summed_t / total).astype(o_ref.dtype)


def body(embeddings, slot, lengths, in_weight, norm_gain, qkv_weight, out_weight):
    seq_count = lax.axis_size("seq")
    device_count = lax.axis_size("tile") * seq_count
    rows = embeddings.shape[0]
    block_rows = rows // device_count
    width = in_weight.shape[1]
    head_size = width // HEAD_COUNT
    group_rows = rows // DILATION_RATE
    far_count = group_rows * seq_count
    scale = head_size ** (-0.5)
    my_index = lax.axis_index("tile") * seq_count + lax.axis_index("seq")

    projected = jnp.dot(embeddings, in_weight, preferred_element_type=jnp.float32).astype(
        jnp.bfloat16
    )
    arrived = lax.all_to_all(
        projected.reshape(device_count, block_rows, width),
        ("tile", "seq"),
        split_axis=0,
        concat_axis=0,
        tiled=True,
    ).reshape(rows, width)
    arrived_slot = lax.all_to_all(
        slot.reshape(device_count, block_rows), ("tile", "seq"), split_axis=0, concat_axis=0, tiled=True
    ).reshape(rows)
    local_slot = arrived_slot - my_index * rows
    stored_slot = (local_slot % DILATION_RATE) * group_rows + local_slot // DILATION_RATE
    placement = (
        stored_slot[None, :] == jnp.arange(rows, dtype=jnp.int32)[:, None]
    ).astype(jnp.bfloat16)
    features = jnp.dot(placement, arrived, preferred_element_type=jnp.float32).astype(
        jnp.bfloat16
    )

    slide_length = lengths[0]
    stored = jnp.arange(rows, dtype=jnp.int32)
    local_position = (stored % group_rows) * DILATION_RATE + stored // group_rows
    position_ok = lax.axis_index("seq") * rows + local_position < slide_length
    limits = jnp.stack([slide_length, lax.axis_index("seq") * rows]).astype(jnp.int32)

    normed = normalize(features, norm_gain)
    projected_t = lax.dot_general(
        qkv_weight, normed, (((0,), (1,)), ((), ())), preferred_element_type=jnp.float32
    ).astype(jnp.bfloat16)

    offsets = [head % DILATION_RATE for head in range(HEAD_COUNT)]
    half = HEAD_COUNT // 2
    grouped = normed.reshape(DILATION_RATE, group_rows, width)
    own_far = jnp.stack(
        [
            jnp.einsum(
                "ljc,chld->hldj",
                grouped,
                qkv_weight[:, part * width : (part + 1) * width].reshape(
                    width, HEAD_COUNT // DILATION_RATE, DILATION_RATE, head_size
                ),
                preferred_element_type=jnp.float32,
            )
            .astype(jnp.bfloat16)
            .reshape(HEAD_COUNT, head_size, group_rows)
            for part in (1, 2)
        ]
    )
    far = lax.all_to_all(
        jnp.broadcast_to(own_far[None], (seq_count,) + own_far.shape),
        "seq",
        split_axis=0,
        concat_axis=0,
        tiled=True,
    )
    bias_block = pl.BlockSpec(memory_space=pltpu.SMEM)
    factor = scale * 1.4426950408889634
    half = HEAD_COUNT // 2
    nearby = pl.pallas_call(
        functools.partial(
            nearby_kernel, groups=DILATION_RATE, group_rows=group_rows, factor=factor
        ),
        grid=(half,),
        in_specs=[
            pl.BlockSpec((head_size, rows), lambda i, first=first: (first + i, 0))
            for first in range(0, 3 * HEAD_COUNT, half)
        ]
        + [bias_block],
        out_specs=pl.BlockSpec((2, head_size, rows), lambda i: (0, i, 0)),
        out_shape=jax.ShapeDtypeStruct((2, half * head_size, rows), jnp.bfloat16),
        scratch_shapes=[pltpu.VMEM((2, rows, head_size + 16), jnp.bfloat16)],
    )(*([projected_t] * 6), limits)

    paired = projected_t.reshape(6, half * head_size, rows)
    far_paired = far.reshape(seq_count, 2, 2, half, head_size, group_rows)
    group_block = pl.BlockSpec(
        (2, head_size, group_rows), lambda i: (0, i, i % DILATION_RATE)
    )
    far_block = (seq_count, 1, 2, 1, head_size, group_rows)
    attended_t = pl.pallas_call(
        functools.partial(dilated_kernel, factor=factor),
        grid=(half,),
        in_specs=[
            pl.BlockSpec((2, head_size, group_rows), lambda i: (0, i, i % DILATION_RATE)),
            pl.BlockSpec((2, head_size, rows), lambda i: (1, i, 0)),
            pl.BlockSpec((2, head_size, rows), lambda i: (2, i, 0)),
            bias_block,
            pl.BlockSpec(far_block, lambda i: (0, 0, 0, i, 0, 0)),
            pl.BlockSpec(far_block, lambda i: (0, 1, 0, i, 0, 0)),
            pl.BlockSpec(memory_space=pl.ANY),
        ],
        out_specs=group_block,
        out_shape=jax.ShapeDtypeStruct((2, half * head_size, rows), jnp.bfloat16),
        input_output_aliases={6: 0},
    )(
        paired, paired, paired, limits, far_paired, far_paired,
        nearby,
    ).reshape(width, rows)

    output = lax.dot_general(
        attended_t, out_weight, (((0,), (0,)), ((), ())), preferred_element_type=jnp.float32
    ) + features.astype(jnp.float32)
    output = jnp.where(position_ok[:, None], output, 0.0).astype(jnp.bfloat16)
    output = output.reshape(DILATION_RATE, group_rows, width).transpose(1, 0, 2)
    return output.reshape(1, rows, width)


def solution(mesh):
    return jax.shard_map(
        body,
        mesh=mesh,
        in_specs=(P(("tile", "seq"), None), P(("tile", "seq")), P("tile"), P(), P(), P(), P()),
        out_specs=P("tile", "seq", None),
        check_vma=False,
    )
```

```python
import functools

import jax
import jax.numpy as jnp
from jax import lax
from jax.experimental import pallas as pl
from jax.experimental.pallas import tpu as pltpu
from jax.sharding import PartitionSpec as P

HEAD_COUNT = 16
QUERY_BLOCK = 1024
PASS1 = 512
PASS2 = 512
DILATION_RATE = 8


big_negative = -1e30
norm_epsilon = 1e-05


def normalize(features, gain):
    wide = features.astype(jnp.float32)
    average = jnp.mean(wide, axis=-1, keepdims=True)
    centered = wide - average
    spread = jnp.mean(centered * centered, axis=-1, keepdims=True)
    return (centered * lax.rsqrt(spread + norm_epsilon) * gain).astype(jnp.bfloat16)


def extend(block, extra):
    return jnp.concatenate([block, extra], axis=0)


def ones_row(width):
    row = lax.broadcasted_iota(jnp.int32, (16, width), 0)
    return jnp.where(row == 0, 1.0, 0.0).astype(jnp.bfloat16)


def nearby_kernel(
    qa_ref, qb_ref, ka_ref, kb_ref, va_ref, vb_ref, bias_ref, o_ref, keys_ref,
    *, groups, group_rows, factor
):
    key_count = keys_ref.shape[1]
    block = QUERY_BLOCK
    ones = ones_row(block)
    heads = ((qa_ref, ka_ref, va_ref), (qb_ref, kb_ref, vb_ref))
    for pair, (_, kt_ref, _) in enumerate(heads):
        keys_ref[pair] = extend(kt_ref[...], bias_ref[...]).T
    for pair, (qt_ref, _, vt_ref) in enumerate(heads):
        for first_row in range(0, groups * group_rows, block):
            rows = pl.ds(first_row, block)
            queries_t = extend(qt_ref[:, rows], ones)
            top = None
            for first in range(0, key_count, PASS1):
                scores_t = jnp.dot(
                    keys_ref[pair, pl.ds(first, PASS1), :],
                    queries_t,
                    preferred_element_type=jnp.float32,
                )
                part = jnp.max(scores_t, axis=0, keepdims=True)
                top = part if top is None else jnp.maximum(top, part)
            total = None
            summed_t = None
            for first in range(0, key_count, PASS2):
                scores_t = jnp.dot(
                    keys_ref[pair, pl.ds(first, PASS2), :],
                    queries_t,
                    preferred_element_type=jnp.float32,
                )
                weights_t = jnp.exp2((scores_t - top) * factor)
                part = jnp.sum(weights_t, axis=0, keepdims=True)
                step = jnp.dot(
                    vt_ref[:, pl.ds(first, PASS2)],
                    weights_t.astype(jnp.bfloat16),
                    preferred_element_type=jnp.float32,
                )
                total = part if total is None else total + part
                summed_t = step if summed_t is None else summed_t + step
            o_ref[pair, :, rows] = (summed_t / total).astype(o_ref.dtype)


def joined(refs, pair):
    return jnp.concatenate([ref[0, pair, 0] for ref in refs], axis=1)


def dilated_kernel(
    qt_ref, kt_ref, vt_ref, bias_ref, *refs, factor, chunks
):
    fk_ref, fv_ref = refs[:chunks], refs[chunks : 2 * chunks]
    fbias_ref, _, o_ref = refs[2 * chunks :]
    for pair in range(2):
        queries_t = extend(qt_ref[pair], ones_row(qt_ref.shape[2]))
        near_keys = extend(kt_ref[pair], bias_ref[...]).T
        far_keys = extend(joined(fk_ref, pair), fbias_ref[0]).T
        near = jnp.dot(near_keys, queries_t, preferred_element_type=jnp.float32)
        far = jnp.dot(far_keys, queries_t, preferred_element_type=jnp.float32)
        top = jnp.maximum(
            jnp.max(near, axis=0, keepdims=True), jnp.max(far, axis=0, keepdims=True)
        )
        near_w = jnp.exp2((near - top) * factor)
        far_w = jnp.exp2((far - top) * factor)
        total = jnp.sum(near_w, axis=0, keepdims=True) + jnp.sum(far_w, axis=0, keepdims=True)
        summed_t = jnp.dot(
            vt_ref[pair], near_w.astype(jnp.bfloat16), preferred_element_type=jnp.float32
        )
        summed_t = summed_t + jnp.dot(
            joined(fv_ref, pair), far_w.astype(jnp.bfloat16), preferred_element_type=jnp.float32
        )
        o_ref[pair] = (summed_t / total).astype(o_ref.dtype)


def body(embeddings, slot, lengths, in_weight, norm_gain, qkv_weight, out_weight):
    seq_count = lax.axis_size("seq")
    device_count = lax.axis_size("tile") * seq_count
    rows = embeddings.shape[0]
    block_rows = rows // device_count
    width = in_weight.shape[1]
    head_size = width // HEAD_COUNT
    group_rows = rows // DILATION_RATE
    far_count = group_rows * seq_count
    scale = head_size ** (-0.5)
    my_index = lax.axis_index("tile") * seq_count + lax.axis_index("seq")

    projected = jnp.dot(embeddings, in_weight, preferred_element_type=jnp.float32).astype(
        jnp.bfloat16
    )
    arrived = lax.all_to_all(
        projected.reshape(device_count, block_rows, width),
        ("tile", "seq"),
        split_axis=0,
        concat_axis=0,
        tiled=True,
    ).reshape(rows, width)
    arrived_slot = lax.all_to_all(
        slot.reshape(device_count, block_rows), ("tile", "seq"), split_axis=0, concat_axis=0, tiled=True
    ).reshape(rows)
    local_slot = arrived_slot - my_index * rows
    stored_slot = (local_slot % DILATION_RATE) * group_rows + local_slot // DILATION_RATE
    placement = (
        stored_slot[None, :] == jnp.arange(rows, dtype=jnp.int32)[:, None]
    ).astype(jnp.bfloat16)
    features = jnp.dot(placement, arrived, preferred_element_type=jnp.float32).astype(
        jnp.bfloat16
    )

    slide_length = lengths[0]
    stored = jnp.arange(rows, dtype=jnp.int32)
    local_position = (stored % group_rows) * DILATION_RATE + stored // group_rows
    position_ok = lax.axis_index("seq") * rows + local_position < slide_length
    extra_row = lax.broadcasted_iota(jnp.int32, (16, 1), 0) == 0
    near_bias = jnp.where(
        extra_row & ~position_ok[None, :], big_negative, 0.0
    ).astype(jnp.bfloat16)

    normed = normalize(features, norm_gain)
    projected_t = lax.dot_general(
        qkv_weight, normed, (((0,), (1,)), ((), ())), preferred_element_type=jnp.float32
    ).astype(jnp.bfloat16)

    offsets = [head % DILATION_RATE for head in range(HEAD_COUNT)]
    half = HEAD_COUNT // 2
    grouped = normed.reshape(DILATION_RATE, group_rows, width)
    own_far = jnp.stack(
        [
            jnp.einsum(
                "ljc,chld->hldj",
                grouped,
                qkv_weight[:, part * width : (part + 1) * width].reshape(
                    width, HEAD_COUNT // DILATION_RATE, DILATION_RATE, head_size
                ),
                preferred_element_type=jnp.float32,
            )
            .astype(jnp.bfloat16)
            .reshape(HEAD_COUNT, head_size, group_rows)
            for part in (1, 2)
        ]
    )
    far_chunks = [own_far] + [
        lax.ppermute(own_far, "seq", [(j, (j + k) % seq_count) for j in range(seq_count)])
        for k in range(1, seq_count)
    ]
    source = (lax.axis_index("seq") - jnp.arange(seq_count, dtype=jnp.int32)) % seq_count
    far_position = (
        (source[:, None] * group_rows + jnp.arange(group_rows, dtype=jnp.int32)[None, :]).reshape(1, far_count)
        * DILATION_RATE
        + jnp.asarray(offsets, jnp.int32)[:, None]
    )
    far_bias = jnp.where(
        extra_row[None] & (far_position >= slide_length)[:, None, :], big_negative, 0.0
    ).astype(jnp.bfloat16)

    query_block = pl.BlockSpec((head_size, rows), lambda h: (h, 0))
    keys_block = pl.BlockSpec((head_size, rows), lambda h: (HEAD_COUNT + h, 0))
    values_block = pl.BlockSpec((head_size, rows), lambda h: (2 * HEAD_COUNT + h, 0))
    bias_block = pl.BlockSpec((16, rows), lambda h: (0, 0))
    factor = scale * 1.4426950408889634
    half = HEAD_COUNT // 2
    nearby = pl.pallas_call(
        functools.partial(
            nearby_kernel, groups=DILATION_RATE, group_rows=group_rows, factor=factor
        ),
        grid=(half,),
        in_specs=[
            pl.BlockSpec((head_size, rows), lambda i, first=first: (first + i, 0))
            for first in range(0, 3 * HEAD_COUNT, half)
        ]
        + [pl.BlockSpec((16, rows), lambda i: (0, 0))],
        out_specs=pl.BlockSpec((2, head_size, rows), lambda i: (0, i, 0)),
        out_shape=jax.ShapeDtypeStruct((2, half * head_size, rows), jnp.bfloat16),
        scratch_shapes=[pltpu.VMEM((2, rows, head_size + 16), jnp.bfloat16)],
    )(*([projected_t] * 6), near_bias)

    paired = projected_t.reshape(6, half * head_size, rows)
    far_paired = [chunk.reshape(2, 2, half, head_size, group_rows) for chunk in far_chunks]
    group_block = pl.BlockSpec(
        (2, head_size, group_rows), lambda i: (0, i, i % DILATION_RATE)
    )
    far_block = (1, 2, 1, head_size, group_rows)
    attended_t = pl.pallas_call(
        functools.partial(dilated_kernel, factor=factor, chunks=seq_count),
        grid=(half,),
        in_specs=[
            pl.BlockSpec((2, head_size, group_rows), lambda i: (0, i, i % DILATION_RATE)),
            pl.BlockSpec((2, head_size, rows), lambda i: (1, i, 0)),
            pl.BlockSpec((2, head_size, rows), lambda i: (2, i, 0)),
            bias_block,
        ]
        + [pl.BlockSpec(far_block, lambda i: (0, 0, i, 0, 0))] * seq_count
        + [pl.BlockSpec(far_block, lambda i: (1, 0, i, 0, 0))] * seq_count
        + [
            pl.BlockSpec((1, 16, far_count), lambda i: (i, 0, 0)),
            pl.BlockSpec(memory_space=pl.ANY),
        ],
        out_specs=group_block,
        out_shape=jax.ShapeDtypeStruct((2, half * head_size, rows), jnp.bfloat16),
        input_output_aliases={5 + 2 * seq_count: 0},
    )(
        paired, paired, paired, near_bias, *far_paired, *far_paired, far_bias,
        nearby,
    ).reshape(width, rows)

    output = lax.dot_general(
        attended_t, out_weight, (((0,), (0,)), ((), ())), preferred_element_type=jnp.float32
    ) + features.astype(jnp.float32)
    output = jnp.where(position_ok[:, None], output, 0.0).astype(jnp.bfloat16)
    output = output.reshape(DILATION_RATE, group_rows, width).transpose(1, 0, 2)
    return output.reshape(1, rows, width)


def solution(mesh):
    return jax.shard_map(
        body,
        mesh=mesh,
        in_specs=(P(("tile", "seq"), None), P(("tile", "seq")), P("tile"), P(), P(), P(), P()),
        out_specs=P("tile", "seq", None),
        check_vma=False,
    )
```

```python
import functools

import jax
import jax.numpy as jnp
from jax import lax
from jax.experimental import pallas as pl
from jax.experimental.pallas import tpu as pltpu
from jax.sharding import PartitionSpec as P

HEAD_COUNT = 16
QUERY_BLOCK = 1024
PASS1 = 1024
PASS2 = 512
DILATION_RATE = 8


big_negative = -1e30
norm_epsilon = 1e-05


def normalize(features, gain):
    wide = features.astype(jnp.float32)
    average = jnp.mean(wide, axis=-1, keepdims=True)
    centered = wide - average
    spread = jnp.mean(centered * centered, axis=-1, keepdims=True)
    return (centered * lax.rsqrt(spread + norm_epsilon) * gain).astype(jnp.bfloat16)


def extend(block, extra):
    return jnp.concatenate([block, extra], axis=0)


def ones_row(width):
    row = lax.broadcasted_iota(jnp.int32, (16, width), 0)
    return jnp.where(row == 0, 1.0, 0.0).astype(jnp.bfloat16)


def mask_rows(limit, width, position_of):
    row = lax.broadcasted_iota(jnp.int32, (16, width), 0)
    lane = lax.broadcasted_iota(jnp.int32, (16, width), 1)
    invalid = (row == 0) & (position_of(lane) >= limit)
    return jnp.where(invalid, big_negative, 0.0).astype(jnp.bfloat16)


def near_mask(limits_ref, rows):
    group_rows = rows // DILATION_RATE
    return mask_rows(
        limits_ref[0],
        rows,
        lambda lane: limits_ref[1] + (lane % group_rows) * DILATION_RATE + lane // group_rows,
    )


def nearby_kernel(
    qa_ref, qb_ref, ka_ref, kb_ref, va_ref, vb_ref, limits_ref, o_ref, keys_ref,
    *, groups, group_rows, factor
):
    key_count = keys_ref.shape[1]
    block = QUERY_BLOCK
    ones = ones_row(block)
    heads = ((qa_ref, ka_ref, va_ref), (qb_ref, kb_ref, vb_ref))
    bias = near_mask(limits_ref, keys_ref.shape[1])
    for pair, (_, kt_ref, _) in enumerate(heads):
        keys_ref[pair] = extend(kt_ref[...], bias).T
    for pair, (qt_ref, _, vt_ref) in enumerate(heads):
        for first_row in range(0, groups * group_rows, block):
            rows = pl.ds(first_row, block)
            queries_t = extend(qt_ref[:, rows], ones)
            top = None
            for first in range(0, key_count, PASS1):
                scores_t = jnp.dot(
                    keys_ref[pair, pl.ds(first, PASS1), :],
                    queries_t,
                    preferred_element_type=jnp.float32,
                )
                part = jnp.max(scores_t, axis=0, keepdims=True)
                top = part if top is None else jnp.maximum(top, part)
            total = None
            summed_t = None
            for first in range(0, key_count, PASS2):
                scores_t = jnp.dot(
                    keys_ref[pair, pl.ds(first, PASS2), :],
                    queries_t,
                    preferred_element_type=jnp.float32,
                )
                weights_t = jnp.exp2((scores_t - top) * factor)
                part = jnp.sum(weights_t, axis=0, keepdims=True)
                step = jnp.dot(
                    vt_ref[:, pl.ds(first, PASS2)],
                    weights_t.astype(jnp.bfloat16),
                    preferred_element_type=jnp.float32,
                )
                total = part if total is None else total + part
                summed_t = step if summed_t is None else summed_t + step
            o_ref[pair, :, rows] = (summed_t / total).astype(o_ref.dtype)


def joined(ref, pair):
    return jnp.concatenate([ref[chunk, 0, pair, 0] for chunk in range(ref.shape[0])], axis=1)


def dilated_kernel(
    qt_ref, kt_ref, vt_ref, limits_ref, fk_ref, fv_ref, prev_ref, o_ref, *, factor
):
    del prev_ref
    offset = pl.program_id(0) % DILATION_RATE
    near_bias = near_mask(limits_ref, kt_ref.shape[2])
    far_bias = mask_rows(
        limits_ref[0],
        fk_ref.shape[0] * fk_ref.shape[5],
        lambda lane: lane * DILATION_RATE + offset,
    )
    for pair in range(2):
        queries_t = extend(qt_ref[pair], ones_row(qt_ref.shape[2]))
        near_keys = extend(kt_ref[pair], near_bias).T
        far_keys = extend(joined(fk_ref, pair), far_bias).T
        near = jnp.dot(near_keys, queries_t, preferred_element_type=jnp.float32)
        far = jnp.dot(far_keys, queries_t, preferred_element_type=jnp.float32)
        top = jnp.maximum(
            jnp.max(near, axis=0, keepdims=True), jnp.max(far, axis=0, keepdims=True)
        )
        near_w = jnp.exp2((near - top) * factor)
        far_w = jnp.exp2((far - top) * factor)
        total = jnp.sum(near_w, axis=0, keepdims=True) + jnp.sum(far_w, axis=0, keepdims=True)
        summed_t = jnp.dot(
            vt_ref[pair], near_w.astype(jnp.bfloat16), preferred_element_type=jnp.float32
        )
        summed_t = summed_t + jnp.dot(
            joined(fv_ref, pair), far_w.astype(jnp.bfloat16), preferred_element_type=jnp.float32
        )
        o_ref[pair] = (summed_t / total).astype(o_ref.dtype)


def body(embeddings, slot, lengths, in_weight, norm_gain, qkv_weight, out_weight):
    seq_count = lax.axis_size("seq")
    device_count = lax.axis_size("tile") * seq_count
    rows = embeddings.shape[0]
    block_rows = rows // device_count
    width = in_weight.shape[1]
    head_size = width // HEAD_COUNT
    group_rows = rows // DILATION_RATE
    far_count = group_rows * seq_count
    scale = head_size ** (-0.5)
    my_index = lax.axis_index("tile") * seq_count + lax.axis_index("seq")

    projected = jnp.dot(embeddings, in_weight, preferred_element_type=jnp.float32).astype(
        jnp.bfloat16
    )
    arrived = lax.all_to_all(
        projected.reshape(device_count, block_rows, width),
        ("tile", "seq"),
        split_axis=0,
        concat_axis=0,
        tiled=True,
    ).reshape(rows, width)
    arrived_slot = lax.all_to_all(
        slot.reshape(device_count, block_rows), ("tile", "seq"), split_axis=0, concat_axis=0, tiled=True
    ).reshape(rows)
    local_slot = arrived_slot - my_index * rows
    stored_slot = (local_slot % DILATION_RATE) * group_rows + local_slot // DILATION_RATE
    placement = (
        stored_slot[None, :] == jnp.arange(rows, dtype=jnp.int32)[:, None]
    ).astype(jnp.bfloat16)
    features = jnp.dot(placement, arrived, preferred_element_type=jnp.float32).astype(
        jnp.bfloat16
    )

    slide_length = lengths[0]
    stored = jnp.arange(rows, dtype=jnp.int32)
    local_position = (stored % group_rows) * DILATION_RATE + stored // group_rows
    position_ok = lax.axis_index("seq") * rows + local_position < slide_length
    limits = jnp.stack([slide_length, lax.axis_index("seq") * rows]).astype(jnp.int32)

    normed = normalize(features, norm_gain)
    projected_t = lax.dot_general(
        qkv_weight, normed, (((0,), (1,)), ((), ())), preferred_element_type=jnp.float32
    ).astype(jnp.bfloat16)

    offsets = [head % DILATION_RATE for head in range(HEAD_COUNT)]
    half = HEAD_COUNT // 2
    grouped = normed.reshape(DILATION_RATE, group_rows, width)
    own_far = jnp.stack(
        [
            jnp.einsum(
                "ljc,chld->hldj",
                grouped,
                qkv_weight[:, part * width : (part + 1) * width].reshape(
                    width, HEAD_COUNT // DILATION_RATE, DILATION_RATE, head_size
                ),
                preferred_element_type=jnp.float32,
            )
            .astype(jnp.bfloat16)
            .reshape(HEAD_COUNT, head_size, group_rows)
            for part in (1, 2)
        ]
    )
    far = lax.all_to_all(
        jnp.broadcast_to(own_far[None], (seq_count,) + own_far.shape),
        "seq",
        split_axis=0,
        concat_axis=0,
        tiled=True,
    )
    bias_block = pl.BlockSpec(memory_space=pltpu.SMEM)
    factor = scale * 1.4426950408889634
    half = HEAD_COUNT // 2
    nearby = pl.pallas_call(
        functools.partial(
            nearby_kernel, groups=DILATION_RATE, group_rows=group_rows, factor=factor
        ),
        grid=(half,),
        in_specs=[
            pl.BlockSpec((head_size, rows), lambda i, first=first: (first + i, 0))
            for first in range(0, 3 * HEAD_COUNT, half)
        ]
        + [bias_block],
        out_specs=pl.BlockSpec((2, head_size, rows), lambda i: (0, i, 0)),
        out_shape=jax.ShapeDtypeStruct((2, half * head_size, rows), jnp.bfloat16),
        scratch_shapes=[pltpu.VMEM((2, rows, head_size + 16), jnp.bfloat16)],
    )(*([projected_t] * 6), limits)

    paired = projected_t.reshape(6, half * head_size, rows)
    far_paired = far.reshape(seq_count, 2, 2, half, head_size, group_rows)
    group_block = pl.BlockSpec(
        (2, head_size, group_rows), lambda i: (0, i, i % DILATION_RATE)
    )
    far_block = (seq_count, 1, 2, 1, head_size, group_rows)
    attended_t = pl.pallas_call(
        functools.partial(dilated_kernel, factor=factor),
        grid=(half,),
        in_specs=[
            pl.BlockSpec((2, head_size, group_rows), lambda i: (0, i, i % DILATION_RATE)),
            pl.BlockSpec((2, head_size, rows), lambda i: (1, i, 0)),
            pl.BlockSpec((2, head_size, rows), lambda i: (2, i, 0)),
            bias_block,
            pl.BlockSpec(far_block, lambda i: (0, 0, 0, i, 0, 0)),
            pl.BlockSpec(far_block, lambda i: (0, 1, 0, i, 0, 0)),
            pl.BlockSpec(memory_space=pl.ANY),
        ],
        out_specs=group_block,
        out_shape=jax.ShapeDtypeStruct((2, half * head_size, rows), jnp.bfloat16),
        input_output_aliases={6: 0},
    )(
        paired, paired, paired, limits, far_paired, far_paired,
        nearby,
    ).reshape(width, rows)

    output = lax.dot_general(
        attended_t, out_weight, (((0,), (0,)), ((), ())), preferred_element_type=jnp.float32
    ) + features.astype(jnp.float32)
    output = jnp.where(position_ok[:, None], output, 0.0).astype(jnp.bfloat16)
    output = output.reshape(DILATION_RATE, group_rows, width).transpose(1, 0, 2)
    return output.reshape(1, rows, width)


def solution(mesh):
    return jax.shard_map(
        body,
        mesh=mesh,
        in_specs=(P(("tile", "seq"), None), P(("tile", "seq")), P("tile"), P(), P(), P(), P()),
        out_specs=P("tile", "seq", None),
        check_vma=False,
    )
```

```python
import functools

import jax
import jax.numpy as jnp
from jax import lax
from jax.experimental import pallas as pl
from jax.experimental.pallas import tpu as pltpu
from jax.sharding import PartitionSpec as P

HEAD_COUNT = 16
QUERY_BLOCK = 1024
PASS1 = 512
PASS2 = 512
DILATION_RATE = 8


big_negative = -1e30
norm_epsilon = 1e-05


def normalize(features, gain):
    wide = features.astype(jnp.float32)
    average = jnp.mean(wide, axis=-1, keepdims=True)
    centered = wide - average
    spread = jnp.mean(centered * centered, axis=-1, keepdims=True)
    return (centered * lax.rsqrt(spread + norm_epsilon) * gain).astype(jnp.bfloat16)


def extend(block, extra):
    return jnp.concatenate([block, extra], axis=0)


def ones_row(width):
    row = lax.broadcasted_iota(jnp.int32, (16, width), 0)
    return jnp.where(row == 0, 1.0, 0.0).astype(jnp.bfloat16)


def nearby_kernel(
    qa_ref, qb_ref, ka_ref, kb_ref, va_ref, vb_ref, bias_ref, o_ref, keys_ref,
    *, groups, group_rows, factor
):
    key_count = keys_ref.shape[1]
    block = QUERY_BLOCK
    ones = ones_row(block)
    heads = ((qa_ref, ka_ref, va_ref), (qb_ref, kb_ref, vb_ref))
    for pair, (_, kt_ref, _) in enumerate(heads):
        keys_ref[pair] = extend(kt_ref[...], bias_ref[...]).T
    for pair, (qt_ref, _, vt_ref) in enumerate(heads):
        for first_row in range(0, groups * group_rows, block):
            rows = pl.ds(first_row, block)
            queries_t = extend(qt_ref[:, rows], ones)
            top = None
            for first in range(0, key_count, PASS1):
                scores_t = jnp.dot(
                    keys_ref[pair, pl.ds(first, PASS1), :],
                    queries_t,
                    preferred_element_type=jnp.float32,
                )
                part = jnp.max(scores_t, axis=0, keepdims=True)
                top = part if top is None else jnp.maximum(top, part)
            total = None
            summed_t = None
            for first in range(0, key_count, PASS2):
                scores_t = jnp.dot(
                    keys_ref[pair, pl.ds(first, PASS2), :],
                    queries_t,
                    preferred_element_type=jnp.float32,
                )
                weights_t = jnp.exp2((scores_t - top) * factor)
                part = jnp.sum(weights_t, axis=0, keepdims=True)
                step = jnp.dot(
                    vt_ref[:, pl.ds(first, PASS2)],
                    weights_t.astype(jnp.bfloat16),
                    preferred_element_type=jnp.float32,
                )
                total = part if total is None else total + part
                summed_t = step if summed_t is None else summed_t + step
            o_ref[pair, :, rows] = (summed_t / total).astype(o_ref.dtype)


def joined(ref, pair):
    return jnp.concatenate([ref[chunk, 0, pair, 0] for chunk in range(ref.shape[0])], axis=1)


def dilated_kernel(
    qt_ref, kt_ref, vt_ref, bias_ref, fk_ref, fv_ref, fbias_ref, prev_ref, o_ref, *, factor
):
    del prev_ref
    for pair in range(2):
        queries_t = extend(qt_ref[pair], ones_row(qt_ref.shape[2]))
        near_keys = extend(kt_ref[pair], bias_ref[...]).T
        far_keys = extend(joined(fk_ref, pair), fbias_ref[0]).T
        near = jnp.dot(near_keys, queries_t, preferred_element_type=jnp.float32)
        far = jnp.dot(far_keys, queries_t, preferred_element_type=jnp.float32)
        top = jnp.maximum(
            jnp.max(near, axis=0, keepdims=True), jnp.max(far, axis=0, keepdims=True)
        )
        near_w = jnp.exp2((near - top) * factor)
        far_w = jnp.exp2((far - top) * factor)
        total = jnp.sum(near_w, axis=0, keepdims=True) + jnp.sum(far_w, axis=0, keepdims=True)
        summed_t = jnp.dot(
            vt_ref[pair], near_w.astype(jnp.bfloat16), preferred_element_type=jnp.float32
        )
        summed_t = summed_t + jnp.dot(
            joined(fv_ref, pair), far_w.astype(jnp.bfloat16), preferred_element_type=jnp.float32
        )
        o_ref[pair] = (summed_t / total).astype(o_ref.dtype)


def body(embeddings, slot, lengths, in_weight, norm_gain, qkv_weight, out_weight):
    seq_count = lax.axis_size("seq")
    device_count = lax.axis_size("tile") * seq_count
    rows = embeddings.shape[0]
    block_rows = rows // device_count
    width = in_weight.shape[1]
    head_size = width // HEAD_COUNT
    group_rows = rows // DILATION_RATE
    far_count = group_rows * seq_count
    scale = head_size ** (-0.5)
    my_index = lax.axis_index("tile") * seq_count + lax.axis_index("seq")

    projected = jnp.dot(embeddings, in_weight, preferred_element_type=jnp.float32).astype(
        jnp.bfloat16
    )
    arrived = lax.all_to_all(
        projected.reshape(device_count, block_rows, width),
        ("tile", "seq"),
        split_axis=0,
        concat_axis=0,
        tiled=True,
    ).reshape(rows, width)
    arrived_slot = lax.all_to_all(
        slot.reshape(device_count, block_rows), ("tile", "seq"), split_axis=0, concat_axis=0, tiled=True
    ).reshape(rows)
    local_slot = arrived_slot - my_index * rows
    stored_slot = (local_slot % DILATION_RATE) * group_rows + local_slot // DILATION_RATE
    placement = (
        stored_slot[None, :] == jnp.arange(rows, dtype=jnp.int32)[:, None]
    ).astype(jnp.bfloat16)
    features = jnp.dot(placement, arrived, preferred_element_type=jnp.float32).astype(
        jnp.bfloat16
    )

    slide_length = lengths[0]
    stored = jnp.arange(rows, dtype=jnp.int32)
    local_position = (stored % group_rows) * DILATION_RATE + stored // group_rows
    position_ok = lax.axis_index("seq") * rows + local_position < slide_length
    extra_row = lax.broadcasted_iota(jnp.int32, (16, 1), 0) == 0
    near_bias = jnp.where(
        extra_row & ~position_ok[None, :], big_negative, 0.0
    ).astype(jnp.bfloat16)

    normed = normalize(features, norm_gain)
    projected_t = lax.dot_general(
        qkv_weight, normed, (((0,), (1,)), ((), ())), preferred_element_type=jnp.float32
    ).astype(jnp.bfloat16)

    offsets = [head % DILATION_RATE for head in range(HEAD_COUNT)]
    half = HEAD_COUNT // 2
    grouped = normed.reshape(DILATION_RATE, group_rows, width)
    own_far = jnp.stack(
        [
            jnp.einsum(
                "ljc,chld->hldj",
                grouped,
                qkv_weight[:, part * width : (part + 1) * width].reshape(
                    width, HEAD_COUNT // DILATION_RATE, DILATION_RATE, head_size
                ),
                preferred_element_type=jnp.float32,
            )
            .astype(jnp.bfloat16)
            .reshape(HEAD_COUNT, head_size, group_rows)
            for part in (1, 2)
        ]
    )
    far = lax.all_to_all(
        jnp.broadcast_to(own_far[None], (seq_count,) + own_far.shape),
        "seq",
        split_axis=0,
        concat_axis=0,
        tiled=True,
    )
    far_position = (
        jnp.arange(far_count, dtype=jnp.int32)[None, :] * DILATION_RATE
        + jnp.asarray(offsets[:half], jnp.int32)[:, None]
    )
    far_bias = jnp.where(
        extra_row[None] & (far_position >= slide_length)[:, None, :], big_negative, 0.0
    ).astype(jnp.bfloat16)

    query_block = pl.BlockSpec((head_size, rows), lambda h: (h, 0))
    keys_block = pl.BlockSpec((head_size, rows), lambda h: (HEAD_COUNT + h, 0))
    values_block = pl.BlockSpec((head_size, rows), lambda h: (2 * HEAD_COUNT + h, 0))
    bias_block = pl.BlockSpec((16, rows), lambda h: (0, 0))
    factor = scale * 1.4426950408889634
    half = HEAD_COUNT // 2
    nearby = pl.pallas_call(
        functools.partial(
            nearby_kernel, groups=DILATION_RATE, group_rows=group_rows, factor=factor
        ),
        grid=(half,),
        in_specs=[
            pl.BlockSpec((head_size, rows), lambda i, first=first: (first + i, 0))
            for first in range(0, 3 * HEAD_COUNT, half)
        ]
        + [pl.BlockSpec((16, rows), lambda i: (0, 0))],
        out_specs=pl.BlockSpec((2, head_size, rows), lambda i: (0, i, 0)),
        out_shape=jax.ShapeDtypeStruct((2, half * head_size, rows), jnp.bfloat16),
        scratch_shapes=[pltpu.VMEM((2, rows, head_size + 16), jnp.bfloat16)],
    )(*([projected_t] * 6), near_bias)

    paired = projected_t.reshape(6, half * head_size, rows)
    far_paired = far.reshape(seq_count, 2, 2, half, head_size, group_rows)
    group_block = pl.BlockSpec(
        (2, head_size, group_rows), lambda i: (0, i, i % DILATION_RATE)
    )
    far_block = (seq_count, 1, 2, 1, head_size, group_rows)
    attended_t = pl.pallas_call(
        functools.partial(dilated_kernel, factor=factor),
        grid=(half,),
        in_specs=[
            pl.BlockSpec((2, head_size, group_rows), lambda i: (0, i, i % DILATION_RATE)),
            pl.BlockSpec((2, head_size, rows), lambda i: (1, i, 0)),
            pl.BlockSpec((2, head_size, rows), lambda i: (2, i, 0)),
            bias_block,
            pl.BlockSpec(far_block, lambda i: (0, 0, 0, i, 0, 0)),
            pl.BlockSpec(far_block, lambda i: (0, 1, 0, i, 0, 0)),
            pl.BlockSpec((1, 16, far_count), lambda i: (i, 0, 0)),
            pl.BlockSpec(memory_space=pl.ANY),
        ],
        out_specs=group_block,
        out_shape=jax.ShapeDtypeStruct((2, half * head_size, rows), jnp.bfloat16),
        input_output_aliases={7: 0},
    )(
        paired, paired, paired, near_bias, far_paired, far_paired, far_bias,
        nearby,
    ).reshape(width, rows)

    output = lax.dot_general(
        attended_t, out_weight, (((0,), (0,)), ((), ())), preferred_element_type=jnp.float32
    ) + features.astype(jnp.float32)
    output = jnp.where(position_ok[:, None], output, 0.0).astype(jnp.bfloat16)
    output = output.reshape(DILATION_RATE, group_rows, width).transpose(1, 0, 2)
    return output.reshape(1, rows, width)


def solution(mesh):
    return jax.shard_map(
        body,
        mesh=mesh,
        in_specs=(P(("tile", "seq"), None), P(("tile", "seq")), P("tile"), P(), P(), P(), P()),
        out_specs=P("tile", "seq", None),
        check_vma=False,
    )
```
